32 devices in a mesh: seq: 16 (over z, x, core), head: 2 (over y).
Axes of the slice: x: 2, y: 2, z: 4, core: 2. Of those that a mesh axis runs over, the one named last changes fastest.
Arguments:
- step_tokens: bfloat16 [2, 12, 8, 2560], P(None, None, None, 'head'), may hold values from -6 to 6
- parents: int32 [2, 12, 8], replicated, may hold values from 0 to 7
- tail_cache: bfloat16 [12, 8, 64, 2048], P(None, 'head', 'seq'), may hold values from -192 to 192
- tail_len: int32 [12], replicated, may hold values from 0 to 62, as said below
- cache: bfloat16 [8, 2048, 2048], P(None, ('seq', 'head')), may hold values from -192 to 192
- cache_len: int32 [8], replicated, may hold values from 256 to 2048, as said below
- prompt_states: bfloat16 [4, 128, 2560], P(None, 'seq', 'head'), may hold values from -6 to 6
- prompt_len: int32 [4], replicated, may hold values from 32 to 128, as said below
- in_gain: float32 [2560], P('head'), may hold values from 0.5 to 1.5
- w_query: bfloat16 [2560, 2048], P('head', 'seq'), may hold values from -0.125 to 0.125
- w_keyval: bfloat16 [2560, 2048], P('head', 'seq'), may hold values from -0.125 to 0.125
- q_gain: float32 [256], replicated, may hold values from 0.6 to 32
- k_gain: float32 [256], replicated, may hold values from 0.6 to 32
- w_out: bfloat16 [2048, 2560], P('seq', 'head'), may hold values from -0.125 to 0.125
- post_gain: float32 [2560], P('head'), may hold values from 0.5 to 1.5
- ffn_gain: float32 [2560], P('head'), may hold values from 0.5 to 1.5
- w_gate: bfloat16 [2560, 10240], P('head', 'seq'), may hold values from -0.125 to 0.125
- w_up: bfloat16 [2560, 10240], P('head', 'seq'), may hold values from -0.125 to 0.125
- w_down: bfloat16 [10240, 2560], P('seq', 'head'), may hold values from -0.0625 to 0.0625
- final_gain: float32 [2560], P('head'), may hold values from 0.5 to 1.5
Outputs:
- decoded: bfloat16 [2, 12, 8, 2560], P(None, None, None, 'head')
The draws below stay inside these ranges and needn't reach their ends.
Inputs may be any that keep to these rules, and one draw needn't show every extreme that they name: `tail_len`: the first 4 groups have 0; the largest entry is exactly 62. `cache_len`: the largest entry is exactly 2048. `prompt_len`: the largest entry is exactly 128.
All inputs are finite; a program needn't handle non-finite values.
Results may differ from the reference program's by a relative error of at most 0.0055.
The reference program's roundings to bfloat16 on the way count: a program that leaves them out, or rounds other values in their place, can miss the bound.
Values may be sent and summed in bfloat16 or wider, within the bound.
No kernel may reach another device: no remote copies, remote signals or barrier semaphores. Data moves between devices by JAX's collectives and lax.ppermute only.
A program may use at most 128 MiB of HBM per device.

```python
import jax
import jax.numpy as jnp
from jax import lax

D = 2560
QH = 8
KVH = 4
HD = 256
FF = 10240
QD = 2048
KV2 = 2048
PRE_GROUPS = 4
DEC_GROUPS = 8
GROUPS = 12
BEAMS = 8
STEPS = 2
CACHE_MAX = 2048
PROMPT_MAX = 128
TAIL = 64


def draw_tail_len(key, part):
    live = jax.random.randint(jax.random.fold_in(key, 1), (DEC_GROUPS,), 0, TAIL - STEPS + 1)
    pick = jax.random.randint(jax.random.fold_in(key, 2), (), 0, DEC_GROUPS)
    live = jnp.where(jnp.arange(DEC_GROUPS) == pick, TAIL - STEPS, live)
    return jnp.concatenate([jnp.zeros((PRE_GROUPS,), jnp.int32), live.astype(jnp.int32)])


def draw_cache_len(key, part):
    lengths = jax.random.randint(jax.random.fold_in(key, 3), (DEC_GROUPS,), CACHE_MAX // 8, CACHE_MAX + 1)
    pick = jax.random.randint(jax.random.fold_in(key, 4), (), 0, DEC_GROUPS)
    return jnp.where(jnp.arange(DEC_GROUPS) == pick, CACHE_MAX, lengths).astype(jnp.int32)


def draw_prompt_len(key, part):
    lengths = jax.random.randint(jax.random.fold_in(key, 5), (PRE_GROUPS,), PROMPT_MAX // 4, PROMPT_MAX + 1)
    pick = jax.random.randint(jax.random.fold_in(key, 6), (), 0, PRE_GROUPS)
    return jnp.where(jnp.arange(PRE_GROUPS) == pick, PROMPT_MAX, lengths).astype(jnp.int32)


def gain_pair(key):
    columns = jax.random.permutation(jax.random.fold_in(key, 21), HD)
    places = jnp.arange(HD)
    first = places == columns[0]
    second = places == columns[1]
    f32 = jnp.float32
    q_base = jax.random.uniform(jax.random.fold_in(key, 22), (HD,), f32, 0.6, 1.4)
    k_base = jax.random.uniform(jax.random.fold_in(key, 23), (HD,), f32, 0.6, 1.4)
    q_lead = jax.random.uniform(jax.random.fold_in(key, 26), (), f32, 10.0, 20.0)
    k_lead = jax.random.uniform(jax.random.fold_in(key, 27), (), f32, 10.0, 20.0)
    q_next = jax.random.uniform(jax.random.fold_in(key, 24), (), f32, 10.0, 20.0)
    k_next = jax.random.uniform(jax.random.fold_in(key, 25), (), f32, 10.0, 20.0)
    q_gain = jnp.where(first, q_lead, jnp.where(second, q_next, q_base))
    k_gain = jnp.where(first, k_lead, jnp.where(second, k_next, k_base))
    return (q_gain, k_gain)


def draw_q_gain(key, part):
    return gain_pair(key)[0]


def draw_k_gain(key, part):
    return gain_pair(key)[1]


def stored_pairs(key, salt, shape):
    k_gain = gain_pair(key)[1]
    scale = jnp.concatenate([jnp.tile(k_gain, KVH), jnp.ones((KVH * HD,), jnp.float32)])
    noise = jax.random.truncated_normal(jax.random.fold_in(key, salt), -6.0, 6.0, shape, jnp.float32)
    return (noise * scale).astype(jnp.bfloat16)


def draw_cache(key, part):
    return stored_pairs(key, 31, (DEC_GROUPS, CACHE_MAX, KV2))


def draw_tail_cache(key, part):
    return stored_pairs(key, 32, (GROUPS, BEAMS, TAIL, KV2))


def with_ends(values, rng, least, largest):
    longest = values.shape.index(max(values.shape))
    spots = []
    for shift in (0, 1):
        where = [jax.random.randint(jax.random.fold_in(rng, axis), (), 0, length) for axis, length in enumerate(values.shape)]
        where[longest] = (where[longest] + shift) % values.shape[longest]
        spots.append(tuple(where))
    return values.at[spots[0]].set(least).at[spots[1]].set(largest)


def block_scale(stream_key, extent, cuts, low, largest):
    level = 1.0
    for dim, blocks in cuts:
        heights = jax.random.uniform(jax.random.fold_in(jax.random.fold_in(stream_key, 6), dim), (blocks,), jnp.float32, low / len(cuts), largest / len(cuts))
        level = level * jnp.repeat(jnp.exp(heights), extent[dim] // blocks).reshape((-1,) + (1,) * (len(extent) - 1 - dim))
    return level


def gaussian(rng, dims, width, bound, cuts=(), dtype=jnp.bfloat16):
    values = width * jax.random.normal(rng, dims, jnp.float32)
    if cuts:
        values = values * block_scale(rng, dims, cuts, -0.22, 0.18)
    return jnp.clip(values, -bound, bound).astype(dtype)


def setup_inputs(seed: int = 0) -> dict:
    key_list = jax.random.split(jax.random.key(seed), 21)
    step_tokens = gaussian(key_list[0], (STEPS, GROUPS, BEAMS, D), 1.0, 6.0, ((3, 2),))
    parents = with_ends(jax.random.randint(key_list[1], (STEPS, GROUPS, BEAMS), 0, BEAMS), jax.random.fold_in(key_list[1], 1), 0, BEAMS - 1).astype(jnp.int32)
    tail_cache = draw_tail_cache(jax.random.fold_in(key_list[20], 71), 0)
    tail_len = draw_tail_len(jax.random.fold_in(key_list[20], 71), 0)
    cache = draw_cache(jax.random.fold_in(key_list[20], 71), 0)
    cache_len = draw_cache_len(jax.random.fold_in(key_list[20], 71), 0)
    prompt_states = gaussian(key_list[6], (PRE_GROUPS, PROMPT_MAX, D), 1.0, 6.0, ((1, 16), (2, 2)))
    prompt_len = draw_prompt_len(jax.random.fold_in(key_list[20], 71), 0)
    in_gain = jnp.clip(1.0 + 0.1 * jax.random.normal(key_list[8], (D,), jnp.float32), 0.5, 1.5)
    w_query = gaussian(key_list[9], (D, QD), D ** -0.5, 0.125, ((0, 2), (1, 16)))
    w_keyval = gaussian(key_list[10], (D, KV2), D ** -0.5, 0.125, ((0, 2), (1, 16)))
    q_gain = draw_q_gain(jax.random.fold_in(key_list[20], 71), 0)
    k_gain = draw_k_gain(jax.random.fold_in(key_list[20], 71), 0)
    w_out = gaussian(key_list[13], (QD, D), QD ** -0.5, 0.125, ((0, 16), (1, 2)))
    post_gain = jnp.clip(1.0 + 0.1 * jax.random.normal(key_list[14], (D,), jnp.float32), 0.5, 1.5)
    ffn_gain = jnp.clip(1.0 + 0.1 * jax.random.normal(key_list[15], (D,), jnp.float32), 0.5, 1.5)
    w_gate = gaussian(key_list[16], (D, FF), D ** -0.5, 0.125, ((0, 2), (1, 16)))
    w_up = gaussian(key_list[17], (D, FF), D ** -0.5, 0.125, ((0, 2), (1, 16)))
    w_down = gaussian(key_list[18], (FF, D), FF ** -0.5, 0.0625, ((0, 16), (1, 2)))
    final_gain = jnp.clip(1.0 + 0.1 * jax.random.normal(key_list[19], (D,), jnp.float32), 0.5, 1.5)
    return dict(step_tokens=step_tokens, parents=parents, tail_cache=tail_cache, tail_len=tail_len, cache=cache, cache_len=cache_len, prompt_states=prompt_states, prompt_len=prompt_len, in_gain=in_gain, w_query=w_query, w_keyval=w_keyval, q_gain=q_gain, k_gain=k_gain, w_out=w_out, post_gain=post_gain, ffn_gain=ffn_gain, w_gate=w_gate, w_up=w_up, w_down=w_down, final_gain=final_gain)


EPS = 1e-06
NEG = -1e+30
QSCALE = 0.0625

def norm_heads(values, gain, scale):
    shaped = values.reshape(values.shape[:-1] + (-1, gain.shape[0]))
    shaped = shaped * lax.rsqrt(lax.optimization_barrier(jnp.mean(shaped * shaped, -1, keepdims=True)) + EPS) * gain * scale
    return shaped.reshape(values.shape)

def finish_keys(pairs, k_gain):
    half = pairs.shape[-1] // 2
    keys = norm_heads(pairs[..., :half], k_gain, 1.0)
    return jnp.concatenate([keys, pairs[..., half:]], -1).astype(jnp.bfloat16)

def split_pairs(pairs):
    half = pairs.shape[-1] // 2
    keys = pairs[..., :half].reshape(pairs.shape[:-1] + (KVH, HD))
    values = pairs[..., half:].reshape(pairs.shape[:-1] + (KVH, HD))
    return (keys, values)

def attend(items):
    query, keys, values, valid, tail_keys, tail_values, tail_valid = items
    f32 = jnp.float32
    first = jnp.einsum('bkrd,nkd->bkrn', query.astype(f32), keys.astype(f32))
    second = jnp.einsum('bkrd,btkd->bkrt', query.astype(f32), tail_keys.astype(f32))
    first = jnp.where(valid, first, NEG)
    second = jnp.where(tail_valid, second, NEG)
    top = jnp.maximum(lax.optimization_barrier(jnp.max(first, -1)), lax.optimization_barrier(jnp.max(second, -1)))[..., None]
    first = jnp.where(valid, jnp.exp(first - top), 0.0)
    second = jnp.where(tail_valid, jnp.exp(second - top), 0.0)
    total = lax.optimization_barrier(jnp.sum(first, -1)) + lax.optimization_barrier(jnp.sum(second, -1))
    rounded = lax.optimization_barrier((first.astype(jnp.bfloat16), second.astype(jnp.bfloat16)))
    mixed = jnp.einsum('bkrn,nkd->bkrd', rounded[0].astype(f32), values.astype(f32))
    mixed = mixed + jnp.einsum('bkrt,btkd->bkrd', rounded[1].astype(f32), tail_values.astype(f32))
    return (mixed / total[..., None]).astype(jnp.bfloat16).reshape(query.shape[0], -1)

def reference(step_tokens, parents, tail_cache, tail_len, cache, cache_len, prompt_states, prompt_len, in_gain, w_query, w_keyval, q_gain, k_gain, w_out, post_gain, ffn_gain, w_gate, w_up, w_down, final_gain):
    f32 = jnp.float32
    bf16 = jnp.bfloat16
    prompt_f = prompt_states.astype(f32).reshape(-1, D)
    prompt_scaled = (prompt_f * in_gain).astype(bf16)
    prompt_raw = jnp.dot(prompt_scaled, w_keyval, preferred_element_type=f32)
    prompt_factor = lax.rsqrt(lax.optimization_barrier(jnp.sum(prompt_f * prompt_f, -1)) / D + EPS)[:, None]
    prompt_kv = finish_keys(prompt_raw * prompt_factor, k_gain).reshape(PRE_GROUPS, PROMPT_MAX, KV2)
    prompt_keys, prompt_values = split_pairs(prompt_kv)
    prompt_valid = jnp.arange(PROMPT_MAX)[None, :] < prompt_len[:, None]
    cache_keys, cache_values = split_pairs(cache)
    cache_valid = jnp.arange(CACHE_MAX)[None, :] < cache_len[:, None]
    tok_f = step_tokens.astype(f32).reshape(-1, D)
    scaled = (tok_f * in_gain).astype(bf16)
    factor = lax.rsqrt(lax.optimization_barrier(jnp.sum(tok_f * tok_f, -1)) / D + EPS)[:, None]
    q_raw = (jnp.dot(scaled, w_query, preferred_element_type=f32) * factor).astype(bf16)
    kv_raw = (jnp.dot(scaled, w_keyval, preferred_element_type=f32) * factor).astype(bf16)
    q_raw, kv_raw = lax.optimization_barrier((q_raw, kv_raw))
    queries = norm_heads(q_raw.astype(f32), q_gain, QSCALE).astype(bf16)
    queries = queries.reshape(STEPS, GROUPS, BEAMS, KVH, QH // KVH, HD)
    new_kv = finish_keys(kv_raw.astype(f32), k_gain).reshape(STEPS, GROUPS, BEAMS, KV2)
    tails = tail_cache
    position = jnp.arange(TAIL)
    decoded = []
    for step in range(STEPS):
        tails = jnp.take_along_axis(tails, parents[step][:, :, None, None], axis=1)
        spot = position[None, :] == (tail_len + step)[:, None]
        tails = jnp.where(spot[:, None, :, None], new_kv[step][:, :, None, :], tails)
        tail_valid = position[None, :] <= (tail_len + step)[:, None]
        tail_keys, tail_values = split_pairs(tails)
        query = queries[step]
        first = lax.map(attend, (query[:PRE_GROUPS], prompt_keys, prompt_values, prompt_valid, tail_keys[:PRE_GROUPS], tail_values[:PRE_GROUPS], tail_valid[:PRE_GROUPS]))
        second = lax.map(attend, (query[PRE_GROUPS:], cache_keys, cache_values, cache_valid, tail_keys[PRE_GROUPS:], tail_values[PRE_GROUPS:], tail_valid[PRE_GROUPS:]))
        attn = jnp.concatenate([first, second], 0).reshape(GROUPS * BEAMS, QD)
        out_proj = jnp.dot(attn, w_out, preferred_element_type=f32)
        x_f = step_tokens[step].astype(f32).reshape(-1, D)
        norm_o = lax.rsqrt(lax.optimization_barrier(jnp.sum(out_proj * out_proj, -1)) / D + EPS)[:, None]
        state = (x_f + out_proj * norm_o * post_gain).astype(bf16)
        state = lax.optimization_barrier(state)
        state_f = state.astype(f32)
        scaled_two = (state_f * ffn_gain).astype(bf16)
        norm_s = lax.rsqrt(lax.optimization_barrier(jnp.sum(state_f * state_f, -1)) / D + EPS)[:, None]
        gate = jnp.dot(scaled_two, w_gate, preferred_element_type=f32) * norm_s
        upper = jnp.dot(scaled_two, w_up, preferred_element_type=f32) * norm_s
        inner = (jax.nn.gelu(gate, approximate=True) * upper).astype(bf16)
        ffn_out = jnp.dot(inner, w_down, preferred_element_type=f32)
        norm_f = lax.rsqrt(lax.optimization_barrier(jnp.sum(ffn_out * ffn_out, -1)) / D + EPS)[:, None]
        result = (state_f + ffn_out * norm_f * final_gain).astype(bf16)
        decoded.append(result.reshape(GROUPS, BEAMS, D))
    return jnp.stack(decoded)
```

```python
import jax
import jax.numpy as jnp
from jax import lax
from jax.sharding import PartitionSpec as P

D = 2560
QH = 8
KVH = 4
HD = 256
QD = 2048


EPS = 1e-06
NEG = -1e30
QSCALE = 0.0625


def norm_heads(values, gain, scale):
    shaped = values.reshape(values.shape[:-1] + (-1, gain.shape[0]))
    shaped = shaped * lax.rsqrt(jnp.mean(shaped * shaped, -1, keepdims=True) + EPS) * gain * scale
    return shaped.reshape(values.shape)


def finish_keys(pairs, k_gain):
    half = pairs.shape[-1] // 2
    keys = norm_heads(pairs[..., :half], k_gain, 1.0)
    return jnp.concatenate([keys, pairs[..., half:]], -1).astype(jnp.bfloat16)


def split_pairs(pairs):
    half = pairs.shape[-1] // 2
    keys = pairs[..., :half].reshape(pairs.shape[:-1] + (KVH, HD))
    values = pairs[..., half:].reshape(pairs.shape[:-1] + (KVH, HD))
    return (keys, values)


def project_tokens(tokens, in_gain, w_query, w_keyval, q_gain, k_gain):
    flat = tokens.reshape(-1, tokens.shape[-1]).astype(jnp.float32)
    scaled = (flat * in_gain).astype(jnp.bfloat16)
    q_part = jnp.dot(scaled, w_query, preferred_element_type=jnp.float32)
    kv_part = jnp.dot(scaled, w_keyval, preferred_element_type=jnp.float32)
    squares = jnp.sum(flat * flat, -1)
    q_part, kv_part, squares = lax.psum((q_part, kv_part, squares), "head")
    factor = lax.rsqrt(squares / D + EPS)[:, None]
    q_raw = (q_part * factor).astype(jnp.bfloat16)
    kv_raw = (kv_part * factor).astype(jnp.bfloat16)
    block = q_raw.shape[1]
    both = lax.all_gather(jnp.concatenate([q_raw, kv_raw], 1), "seq", axis=1)
    q_raw = both[:, :, :block].reshape(both.shape[0], -1)
    kv_raw = both[:, :, block:].reshape(both.shape[0], -1)
    queries = norm_heads(q_raw.astype(jnp.float32), q_gain, QSCALE).astype(jnp.bfloat16)
    fresh = finish_keys(kv_raw.astype(jnp.float32), k_gain)
    return (queries, fresh)


def shards(
    step_tokens,
    parents,
    tail_cache,
    tail_len,
    cache,
    cache_len,
    prompt_states,
    prompt_len,
    in_gain,
    w_query,
    w_keyval,
    q_gain,
    k_gain,
    w_out,
    post_gain,
    ffn_gain,
    w_gate,
    w_up,
    w_down,
    final_gain,
):
    f32 = jnp.float32
    bf16 = jnp.bfloat16
    n_head = lax.axis_size("head")
    n_seq = lax.axis_size("seq")
    seq_at = lax.axis_index("seq")
    head_at = lax.axis_index("head")
    flat_at = seq_at * n_head + head_at
    steps, groups, beams, width = step_tokens.shape
    pre = prompt_states.shape[0]
    repeat = QH // KVH
    rows = jnp.transpose(prompt_states, (1, 0, 2)).astype(f32)
    prompt_scaled = (rows * in_gain).astype(bf16).reshape(-1, width)
    prompt_squares = jnp.sum(rows * rows, -1).reshape(-1)
    prompt_terms = jnp.dot(
        prompt_scaled,
        lax.all_gather(w_keyval, "seq", axis=1, tiled=True),
        preferred_element_type=f32,
    )
    prompt_sum, prompt_sq = (
        lax.psum_scatter(prompt_terms, "head", scatter_dimension=0, tiled=True),
        lax.psum_scatter(prompt_squares, "head", scatter_dimension=0, tiled=True),
    )
    prompt_pairs = finish_keys(prompt_sum * lax.rsqrt(prompt_sq / D + EPS)[:, None], k_gain)
    prompt_seg = prompt_pairs.shape[0] // pre
    prompt_pairs = jnp.transpose(prompt_pairs.reshape(prompt_seg, pre, -1), (1, 0, 2))
    prompt_keys, prompt_values = split_pairs(prompt_pairs)
    prompt_ok = (flat_at * prompt_seg + jnp.arange(prompt_seg))[None, :] < prompt_len[:, None]
    cache_seg = cache.shape[1]
    cache_keys, cache_values = split_pairs(cache)
    cache_ok = (flat_at * cache_seg + jnp.arange(cache_seg))[None, :] < cache_len[:, None]
    tail_seg = tail_cache.shape[2]
    local_beams = tail_cache.shape[1]
    offset = (seq_at * tail_seg + jnp.arange(tail_seg))[None, :] - tail_len[:, None]
    all_beams = jnp.arange(beams)
    every_query, every_fresh = project_tokens(
        step_tokens, in_gain, w_query, w_keyval, q_gain, k_gain
    )
    every_query = every_query.reshape(steps, groups, beams, -1)
    every_fresh = every_fresh.reshape(steps, groups, beams, -1)
    everyone = lax.all_gather(tail_cache, "head", axis=1, tiled=True)
    local_ids = head_at * local_beams + jnp.arange(local_beams)
    n_dev = n_seq * n_head
    owner = jnp.broadcast_to(all_beams[None, :, None], (groups, beams, tail_seg))
    source = jnp.broadcast_to(all_beams[None, :], (groups, beams))
    ancestors = []
    shaped_all, scores_all, tails_all = [], [], []
    for step in range(steps):
        link = parents[step]
        source = jnp.take_along_axis(source, link, axis=1)
        ancestors = [jnp.take_along_axis(a, link, axis=1) for a in ancestors]
        ancestors.append(jnp.broadcast_to(all_beams[None, :], (groups, beams)))
        picks = lax.dynamic_slice_in_dim(source, head_at * local_beams, local_beams, 1)
        tail_state = jnp.take_along_axis(everyone, picks[:, :, None, None], axis=1)
        for back, anc in enumerate(ancestors):
            mine = lax.dynamic_slice_in_dim(anc, head_at * local_beams, local_beams, 1)
            written = jnp.take_along_axis(every_fresh[back], mine[:, :, None], axis=1)
            tail_state = jnp.where(
                (offset == back)[:, None, :, None], written[:, :, None, :], tail_state
            )
        tail_ok = (offset <= step)[:, None, None, :] & (
            owner[:, :, None, :] == local_ids[None, None, :, None]
        )
        shaped = every_query[step].reshape(groups, beams, KVH, repeat, HD)
        tail_keys, tail_values = split_pairs(tail_state)
        pre_scores = jnp.einsum(
            "gbkrd,gtkd->gbkrt", shaped[:pre], prompt_keys, preferred_element_type=f32
        )
        dec_scores = jnp.einsum(
            "gbkrd,gtkd->gbkrt", shaped[pre:], cache_keys, preferred_element_type=f32
        )
        tail_scores = jnp.einsum(
            "gbkrd,gctkd->gbkrct", shaped, tail_keys, preferred_element_type=f32
        )
        pre_scores = jnp.where(prompt_ok[:, None, None, None, :], pre_scores, NEG)
        dec_scores = jnp.where(cache_ok[:, None, None, None, :], dec_scores, NEG)
        tail_scores = jnp.where(tail_ok[:, :, None, None, :, :], tail_scores, NEG)
        top = jnp.concatenate([jnp.max(pre_scores, -1), jnp.max(dec_scores, -1)], 0)
        top = jnp.maximum(top, jnp.max(tail_scores, (-2, -1)))
        scores_all.append((pre_scores, dec_scores, tail_scores))
        tails_all.append((tail_ok, tail_values))
        shaped_all.append(top)
    top_all = lax.pmax(jnp.stack(shaped_all), ("seq", "head"))
    weighted_all, total_all = [], []
    for step in range(steps):
        pre_scores, dec_scores, tail_scores = scores_all[step]
        tail_ok, tail_values = tails_all[step]
        top = top_all[step]
        pre_mask = prompt_ok[:, None, None, None, :]
        dec_mask = cache_ok[:, None, None, None, :]
        tail_mask = tail_ok[:, :, None, None, :, :]
        pre_weights = jnp.where(pre_mask, jnp.exp(pre_scores - top[:pre, ..., None]), 0.0)
        dec_weights = jnp.where(dec_mask, jnp.exp(dec_scores - top[pre:, ..., None]), 0.0)
        tail_weights = jnp.where(tail_mask, jnp.exp(tail_scores - top[..., None, None]), 0.0)
        total = jnp.concatenate([jnp.sum(pre_weights, -1), jnp.sum(dec_weights, -1)], 0)
        total = total + jnp.sum(tail_weights, (-2, -1))
        weighted = jnp.concatenate(
            [
                jnp.einsum(
                    "gbkrt,gtkd->gbkrd",
                    pre_weights.astype(bf16),
                    prompt_values,
                    preferred_element_type=f32,
                ),
                jnp.einsum(
                    "gbkrt,gtkd->gbkrd",
                    dec_weights.astype(bf16),
                    cache_values,
                    preferred_element_type=f32,
                ),
            ],
            0,
        )
        weighted = weighted + jnp.einsum(
            "gbkrct,gctkd->gbkrd",
            tail_weights.astype(bf16),
            tail_values,
            preferred_element_type=f32,
        )
        weighted_all.append(weighted.reshape(groups * beams, -1))
        total_all.append(total.reshape(groups * beams, -1))
    weighted = jnp.concatenate(weighted_all, 0)
    total = jnp.concatenate(total_all, 0)
    rows = weighted.shape[0]
    piece = QD // n_seq
    piece_head = jnp.arange(n_seq) * piece // HD
    lanes = -(-rows // 128) * 128
    packed = jnp.concatenate(
        [
            jnp.transpose(weighted.reshape(rows, n_seq, piece), (1, 0, 2)).reshape(n_seq, -1),
            jnp.pad(jnp.transpose(total[:, piece_head]), ((0, 0), (0, lanes - rows))),
        ],
        1,
    )
    packed = lax.psum_scatter(packed, "seq", scatter_dimension=0, tiled=True)
    packed = lax.psum(packed, "head")
    share = packed[0, : rows * piece].reshape(rows, piece)
    own_total = packed[0, rows * piece : rows * piece + rows]
    attn = (share / own_total[:, None]).astype(bf16)
    partial_out = jnp.dot(attn, w_out, preferred_element_type=f32)
    per_dev = rows // n_seq
    out_proj = lax.psum_scatter(
        partial_out.reshape(n_seq, per_dev, -1), "seq", scatter_dimension=0, tiled=True
    )[0]
    out_sq = lax.psum(jnp.sum(out_proj * out_proj, -1), "head")
    x_all = step_tokens.reshape(rows, -1)
    x_f = lax.dynamic_slice_in_dim(x_all, seq_at * per_dev, per_dev, 0).astype(f32)
    state = (x_f + out_proj * lax.rsqrt(out_sq / D + EPS)[:, None] * post_gain).astype(bf16)
    state_all = lax.all_gather(state, "seq", axis=0, tiled=True)
    state_f = state_all.astype(f32)
    scaled_two = (state_f * ffn_gain).astype(bf16)
    gate_part = jnp.dot(scaled_two, w_gate, preferred_element_type=f32)
    up_part = jnp.dot(scaled_two, w_up, preferred_element_type=f32)
    gate_part, up_part, state_sq = lax.psum(
        (gate_part, up_part, jnp.sum(state_f * state_f, -1)), "head"
    )
    norm_s = lax.rsqrt(state_sq / D + EPS)[:, None]
    inner = (jax.nn.gelu(gate_part * norm_s, approximate=True) * (up_part * norm_s)).astype(bf16)
    ffn_out = lax.psum_scatter(
        jnp.dot(inner, w_down, preferred_element_type=f32).reshape(n_seq, per_dev, -1),
        "seq",
        scatter_dimension=0,
        tiled=True,
    )[0]
    ffn_sq = lax.psum(jnp.sum(ffn_out * ffn_out, -1), "head")
    result = (
        state.astype(f32) + ffn_out * lax.rsqrt(ffn_sq / D + EPS)[:, None] * final_gain
    ).astype(bf16)
    result = lax.all_gather(result, "seq", axis=0, tiled=True)
    return result.reshape(steps, groups, beams, -1)


def solution(mesh):
    return jax.shard_map(
        shards,
        mesh=mesh,
        in_specs=(
            P(None, None, None, "head"),
            P(),
            P(None, "head", "seq", None),
            P(),
            P(None, ("seq", "head"), None),
            P(),
            P(None, "seq", "head"),
            P(),
            P("head"),
            P("head", "seq"),
            P("head", "seq"),
            P(),
            P(),
            P("seq", "head"),
            P("head"),
            P("head"),
            P("head", "seq"),
            P("head", "seq"),
            P("seq", "head"),
            P("head"),
        ),
        out_specs=P(None, None, None, "head"),
        check_vma=False,
    )
```

```python
import jax
import jax.numpy as jnp
from jax import lax
from jax.sharding import PartitionSpec as P

D = 2560
QH = 8
KVH = 4
HD = 256
QD = 2048


EPS = 1e-06
NEG = -1e30
QSCALE = 0.0625


def norm_heads(values, gain, scale):
    shaped = values.reshape(values.shape[:-1] + (-1, gain.shape[0]))
    shaped = shaped * lax.rsqrt(jnp.mean(shaped * shaped, -1, keepdims=True) + EPS) * gain * scale
    return shaped.reshape(values.shape)


def finish_keys(pairs, k_gain):
    half = pairs.shape[-1] // 2
    keys = norm_heads(pairs[..., :half], k_gain, 1.0)
    return jnp.concatenate([keys, pairs[..., half:]], -1).astype(jnp.bfloat16)


def split_pairs(pairs):
    half = pairs.shape[-1] // 2
    keys = pairs[..., :half].reshape(pairs.shape[:-1] + (KVH, HD))
    values = pairs[..., half:].reshape(pairs.shape[:-1] + (KVH, HD))
    return (keys, values)


def exchange_sum(parts, axes):
    return jnp.sum(lax.all_to_all(parts, axes, 0, 0, tiled=True), 0)


def exchange_max(value, axes, count):
    spread = jnp.broadcast_to(value[None], (count,) + value.shape)
    return jnp.max(lax.all_to_all(spread, axes, 0, 0, tiled=True), 0)


def exchange_gather(piece, axes, count):
    spread = jnp.broadcast_to(piece[None], (count,) + piece.shape)
    return lax.all_to_all(spread, axes, 0, 0, tiled=True)


def project_tokens(tokens, in_gain, w_query, w_keyval, q_gain, k_gain):
    flat = tokens.reshape(-1, tokens.shape[-1]).astype(jnp.float32)
    scaled = (flat * in_gain).astype(jnp.bfloat16)
    q_part = jnp.dot(scaled, w_query, preferred_element_type=jnp.float32)
    kv_part = jnp.dot(scaled, w_keyval, preferred_element_type=jnp.float32)
    squares = jnp.sum(flat * flat, -1)
    q_part, kv_part, squares = lax.psum((q_part, kv_part, squares), "head")
    factor = lax.rsqrt(squares / D + EPS)[:, None]
    q_raw = (q_part * factor).astype(jnp.bfloat16)
    kv_raw = (kv_part * factor).astype(jnp.bfloat16)
    block = q_raw.shape[1]
    both = exchange_gather(jnp.concatenate([q_raw, kv_raw], 1), "seq", lax.axis_size("seq"))
    both = jnp.transpose(both, (1, 0, 2))
    q_raw = both[:, :, :block].reshape(both.shape[0], -1)
    kv_raw = both[:, :, block:].reshape(both.shape[0], -1)
    queries = norm_heads(q_raw.astype(jnp.float32), q_gain, QSCALE).astype(jnp.bfloat16)
    fresh = finish_keys(kv_raw.astype(jnp.float32), k_gain)
    return (queries, fresh)


def shards(
    step_tokens,
    parents,
    tail_cache,
    tail_len,
    cache,
    cache_len,
    prompt_states,
    prompt_len,
    in_gain,
    w_query,
    w_keyval,
    q_gain,
    k_gain,
    w_out,
    post_gain,
    ffn_gain,
    w_gate,
    w_up,
    w_down,
    final_gain,
):
    f32 = jnp.float32
    bf16 = jnp.bfloat16
    n_head = lax.axis_size("head")
    n_seq = lax.axis_size("seq")
    seq_at = lax.axis_index("seq")
    head_at = lax.axis_index("head")
    flat_at = seq_at * n_head + head_at
    steps, groups, beams, width = step_tokens.shape
    pre = prompt_states.shape[0]
    repeat = QH // KVH
    rows = jnp.transpose(prompt_states, (1, 0, 2)).astype(f32)
    prompt_scaled = (rows * in_gain).astype(bf16).reshape(-1, width)
    prompt_squares = jnp.sum(rows * rows, -1).reshape(-1)
    prompt_terms = jnp.dot(
        prompt_scaled,
        lax.all_gather(w_keyval, "seq", axis=1, tiled=True),
        preferred_element_type=f32,
    )
    prompt_sum, prompt_sq = (
        lax.psum_scatter(prompt_terms, "head", scatter_dimension=0, tiled=True),
        lax.psum_scatter(prompt_squares, "head", scatter_dimension=0, tiled=True),
    )
    prompt_pairs = finish_keys(prompt_sum * lax.rsqrt(prompt_sq / D + EPS)[:, None], k_gain)
    prompt_seg = prompt_pairs.shape[0] // pre
    prompt_pairs = jnp.transpose(prompt_pairs.reshape(prompt_seg, pre, -1), (1, 0, 2))
    prompt_keys, prompt_values = split_pairs(prompt_pairs)
    prompt_ok = (flat_at * prompt_seg + jnp.arange(prompt_seg))[None, :] < prompt_len[:, None]
    cache_seg = cache.shape[1]
    cache_keys, cache_values = split_pairs(cache)
    cache_ok = (flat_at * cache_seg + jnp.arange(cache_seg))[None, :] < cache_len[:, None]
    tail_seg = tail_cache.shape[2]
    local_beams = tail_cache.shape[1]
    offset = (seq_at * tail_seg + jnp.arange(tail_seg))[None, :] - tail_len[:, None]
    all_beams = jnp.arange(beams)
    every_query, every_fresh = project_tokens(
        step_tokens, in_gain, w_query, w_keyval, q_gain, k_gain
    )
    every_query = every_query.reshape(steps, groups, beams, -1)
    every_fresh = every_fresh.reshape(steps, groups, beams, -1)
    everyone = lax.all_gather(tail_cache, "head", axis=1, tiled=True)
    local_ids = head_at * local_beams + jnp.arange(local_beams)
    n_dev = n_seq * n_head
    owner = jnp.broadcast_to(all_beams[None, :, None], (groups, beams, tail_seg))
    source = jnp.broadcast_to(all_beams[None, :], (groups, beams))
    ancestors = []
    shaped_all, scores_all, tails_all = [], [], []
    for step in range(steps):
        link = parents[step]
        source = jnp.take_along_axis(source, link, axis=1)
        ancestors = [jnp.take_along_axis(a, link, axis=1) for a in ancestors]
        ancestors.append(jnp.broadcast_to(all_beams[None, :], (groups, beams)))
        picks = lax.dynamic_slice_in_dim(source, head_at * local_beams, local_beams, 1)
        tail_state = jnp.take_along_axis(everyone, picks[:, :, None, None], axis=1)
        for back, anc in enumerate(ancestors):
            mine = lax.dynamic_slice_in_dim(anc, head_at * local_beams, local_beams, 1)
            written = jnp.take_along_axis(every_fresh[back], mine[:, :, None], axis=1)
            tail_state = jnp.where(
                (offset == back)[:, None, :, None], written[:, :, None, :], tail_state
            )
        tail_ok = (offset <= step)[:, None, None, :] & (
            owner[:, :, None, :] == local_ids[None, None, :, None]
        )
        shaped = every_query[step].reshape(groups, beams, KVH, repeat, HD)
        tail_keys, tail_values = split_pairs(tail_state)
        pre_scores = jnp.einsum(
            "gbkrd,gtkd->gbkrt", shaped[:pre], prompt_keys, preferred_element_type=f32
        )
        dec_scores = jnp.einsum(
            "gbkrd,gtkd->gbkrt", shaped[pre:], cache_keys, preferred_element_type=f32
        )
        tail_scores = jnp.einsum(
            "gbkrd,gctkd->gbkrct", shaped, tail_keys, preferred_element_type=f32
        )
        pre_scores = jnp.where(prompt_ok[:, None, None, None, :], pre_scores, NEG)
        dec_scores = jnp.where(cache_ok[:, None, None, None, :], dec_scores, NEG)
        tail_scores = jnp.where(tail_ok[:, :, None, None, :, :], tail_scores, NEG)
        top = jnp.concatenate([jnp.max(pre_scores, -1), jnp.max(dec_scores, -1)], 0)
        top = jnp.maximum(top, jnp.max(tail_scores, (-2, -1)))
        scores_all.append((pre_scores, dec_scores, tail_scores))
        tails_all.append((tail_ok, tail_values))
        shaped_all.append(top)
    top_all = exchange_max(jnp.stack(shaped_all), ("seq", "head"), n_dev)
    weighted_all, total_all = [], []
    for step in range(steps):
        pre_scores, dec_scores, tail_scores = scores_all[step]
        tail_ok, tail_values = tails_all[step]
        top = top_all[step]
        pre_mask = prompt_ok[:, None, None, None, :]
        dec_mask = cache_ok[:, None, None, None, :]
        tail_mask = tail_ok[:, :, None, None, :, :]
        pre_weights = jnp.where(pre_mask, jnp.exp(pre_scores - top[:pre, ..., None]), 0.0)
        dec_weights = jnp.where(dec_mask, jnp.exp(dec_scores - top[pre:, ..., None]), 0.0)
        tail_weights = jnp.where(tail_mask, jnp.exp(tail_scores - top[..., None, None]), 0.0)
        total = jnp.concatenate([jnp.sum(pre_weights, -1), jnp.sum(dec_weights, -1)], 0)
        total = total + jnp.sum(tail_weights, (-2, -1))
        weighted = jnp.concatenate(
            [
                jnp.einsum(
                    "gbkrt,gtkd->gbkrd",
                    pre_weights.astype(bf16),
                    prompt_values,
                    preferred_element_type=f32,
                ),
                jnp.einsum(
                    "gbkrt,gtkd->gbkrd",
                    dec_weights.astype(bf16),
                    cache_values,
                    preferred_element_type=f32,
                ),
            ],
            0,
        )
        weighted = weighted + jnp.einsum(
            "gbkrct,gctkd->gbkrd",
            tail_weights.astype(bf16),
            tail_values,
            preferred_element_type=f32,
        )
        weighted_all.append(weighted.reshape(groups * beams, -1))
        total_all.append(total.reshape(groups * beams, -1))
    weighted = jnp.concatenate(weighted_all, 0)
    total = jnp.concatenate(total_all, 0)
    rows = weighted.shape[0]
    piece = QD // n_dev
    piece_head = jnp.arange(n_dev) * piece // HD
    lanes = -(-rows // 128) * 128
    packed = jnp.concatenate(
        [
            jnp.transpose(weighted.reshape(rows, n_dev, piece), (1, 0, 2)).reshape(n_dev, -1),
            jnp.pad(jnp.transpose(total[:, piece_head]), ((0, 0), (0, lanes - rows))),
        ],
        1,
    )
    packed = exchange_sum(packed, ("seq", "head"))
    share = packed[: rows * piece].reshape(rows, piece)
    own_total = packed[rows * piece : rows * piece + rows]
    attn = (share / own_total[:, None]).astype(bf16)
    attn = exchange_gather(attn, "head", n_head)
    attn = jnp.transpose(attn, (1, 0, 2)).reshape(rows, -1)
    partial_out = jnp.dot(attn, w_out, preferred_element_type=f32)
    per_dev = rows // n_seq
    out_proj = exchange_sum(partial_out.reshape(n_seq, per_dev, -1), "seq")
    out_sq = lax.psum(jnp.sum(out_proj * out_proj, -1), "head")
    x_all = step_tokens.reshape(rows, -1)
    x_f = lax.dynamic_slice_in_dim(x_all, seq_at * per_dev, per_dev, 0).astype(f32)
    state = (x_f + out_proj * lax.rsqrt(out_sq / D + EPS)[:, None] * post_gain).astype(bf16)
    state_all = exchange_gather(state, "seq", n_seq).reshape(rows, -1)
    state_f = state_all.astype(f32)
    scaled_two = (state_f * ffn_gain).astype(bf16)
    gate_part = jnp.dot(scaled_two, w_gate, preferred_element_type=f32)
    up_part = jnp.dot(scaled_two, w_up, preferred_element_type=f32)
    gate_part, up_part, state_sq = lax.psum(
        (gate_part, up_part, jnp.sum(state_f * state_f, -1)), "head"
    )
    norm_s = lax.rsqrt(state_sq / D + EPS)[:, None]
    inner = (jax.nn.gelu(gate_part * norm_s, approximate=True) * (up_part * norm_s)).astype(bf16)
    ffn_out = exchange_sum(
        jnp.dot(inner, w_down, preferred_element_type=f32).reshape(n_seq, per_dev, -1), "seq"
    )
    ffn_sq = lax.psum(jnp.sum(ffn_out * ffn_out, -1), "head")
    result = (
        state.astype(f32) + ffn_out * lax.rsqrt(ffn_sq / D + EPS)[:, None] * final_gain
    ).astype(bf16)
    result = exchange_gather(result, "seq", n_seq)
    return result.reshape(steps, groups, beams, -1)


def solution(mesh):
    return jax.shard_map(
        shards,
        mesh=mesh,
        in_specs=(
            P(None, None, None, "head"),
            P(),
            P(None, "head", "seq", None),
            P(),
            P(None, ("seq", "head"), None),
            P(),
            P(None, "seq", "head"),
            P(),
            P("head"),
            P("head", "seq"),
            P("head", "seq"),
            P(),
            P(),
            P("seq", "head"),
            P("head"),
            P("head"),
            P("head", "seq"),
            P("head", "seq"),
            P("seq", "head"),
            P("head"),
        ),
        out_specs=P(None, None, None, "head"),
        check_vma=False,
    )
```

```python
import jax
import jax.numpy as jnp
from jax import lax
from jax.sharding import PartitionSpec as P

D = 2560
QH = 8
KVH = 4
HD = 256
QD = 2048


EPS = 1e-06
NEG = -1e30
QSCALE = 0.0625


def norm_heads(values, gain, scale):
    shaped = values.reshape(values.shape[:-1] + (-1, gain.shape[0]))
    shaped = shaped * lax.rsqrt(jnp.mean(shaped * shaped, -1, keepdims=True) + EPS) * gain * scale
    return shaped.reshape(values.shape)


def finish_keys(pairs, k_gain):
    half = pairs.shape[-1] // 2
    keys = norm_heads(pairs[..., :half], k_gain, 1.0)
    return jnp.concatenate([keys, pairs[..., half:]], -1).astype(jnp.bfloat16)


def split_pairs(pairs):
    half = pairs.shape[-1] // 2
    keys = pairs[..., :half].reshape(pairs.shape[:-1] + (KVH, HD))
    values = pairs[..., half:].reshape(pairs.shape[:-1] + (KVH, HD))
    return (keys, values)


def exchange_sum(parts, axes):
    return jnp.sum(lax.all_to_all(parts, axes, 0, 0, tiled=True), 0)


def exchange_max(value, axes, count):
    spread = jnp.broadcast_to(value[None], (count,) + value.shape)
    return jnp.max(lax.all_to_all(spread, axes, 0, 0, tiled=True), 0)


def exchange_gather(piece, axes, count):
    spread = jnp.broadcast_to(piece[None], (count,) + piece.shape)
    return lax.all_to_all(spread, axes, 0, 0, tiled=True)


def project_tokens(tokens, in_gain, w_query, w_keyval, q_gain, k_gain):
    flat = tokens.reshape(-1, tokens.shape[-1]).astype(jnp.float32)
    scaled = (flat * in_gain).astype(jnp.bfloat16)
    q_part = jnp.dot(scaled, w_query, preferred_element_type=jnp.float32)
    kv_part = jnp.dot(scaled, w_keyval, preferred_element_type=jnp.float32)
    squares = jnp.sum(flat * flat, -1)
    n_head = lax.axis_size("head")
    n_seq = lax.axis_size("seq")
    rows = flat.shape[0]
    half = rows // n_head
    block = q_part.shape[1]
    packed = jnp.concatenate([q_part, kv_part, jnp.pad(squares[:, None], ((0, 0), (0, 127)))], 1)
    packed = exchange_sum(packed.reshape(n_head, half, -1), "head")
    factor = lax.rsqrt(packed[:, 2 * block] / D + EPS)[:, None]
    q_raw = (packed[:, :block] * factor).astype(jnp.bfloat16)
    kv_raw = (packed[:, block : 2 * block] * factor).astype(jnp.bfloat16)
    both = exchange_gather(
        jnp.concatenate([q_raw, kv_raw], 1), ("seq", "head"), n_seq * n_head
    ).reshape(n_seq, n_head, half, 2 * block)
    both = jnp.transpose(both, (1, 2, 0, 3)).reshape(rows, n_seq, 2 * block)
    q_raw = both[:, :, :block].reshape(rows, -1)
    kv_raw = both[:, :, block:].reshape(rows, -1)
    queries = norm_heads(q_raw.astype(jnp.float32), q_gain, QSCALE).astype(jnp.bfloat16)
    fresh = finish_keys(kv_raw.astype(jnp.float32), k_gain)
    return (queries, fresh)


def shards(
    step_tokens,
    parents,
    tail_cache,
    tail_len,
    cache,
    cache_len,
    prompt_states,
    prompt_len,
    in_gain,
    w_query,
    w_keyval,
    q_gain,
    k_gain,
    w_out,
    post_gain,
    ffn_gain,
    w_gate,
    w_up,
    w_down,
    final_gain,
):
    f32 = jnp.float32
    bf16 = jnp.bfloat16
    n_head = lax.axis_size("head")
    n_seq = lax.axis_size("seq")
    seq_at = lax.axis_index("seq")
    head_at = lax.axis_index("head")
    flat_at = seq_at * n_head + head_at
    steps, groups, beams, width = step_tokens.shape
    pre = prompt_states.shape[0]
    repeat = QH // KVH
    rows = jnp.transpose(prompt_states, (1, 0, 2)).astype(f32)
    prompt_scaled = (rows * in_gain).astype(bf16).reshape(-1, width)
    prompt_squares = jnp.sum(rows * rows, -1).reshape(-1)
    prompt_terms = jnp.dot(
        prompt_scaled,
        lax.all_gather(w_keyval, "seq", axis=1, tiled=True),
        preferred_element_type=f32,
    )
    prompt_sum, prompt_sq = (
        lax.psum_scatter(prompt_terms, "head", scatter_dimension=0, tiled=True),
        lax.psum_scatter(prompt_squares, "head", scatter_dimension=0, tiled=True),
    )
    prompt_pairs = finish_keys(prompt_sum * lax.rsqrt(prompt_sq / D + EPS)[:, None], k_gain)
    prompt_seg = prompt_pairs.shape[0] // pre
    prompt_pairs = jnp.transpose(prompt_pairs.reshape(prompt_seg, pre, -1), (1, 0, 2))
    prompt_keys, prompt_values = split_pairs(prompt_pairs)
    prompt_ok = (flat_at * prompt_seg + jnp.arange(prompt_seg))[None, :] < prompt_len[:, None]
    cache_seg = cache.shape[1]
    cache_keys, cache_values = split_pairs(cache)
    cache_ok = (flat_at * cache_seg + jnp.arange(cache_seg))[None, :] < cache_len[:, None]
    tail_seg = tail_cache.shape[2]
    local_beams = tail_cache.shape[1]
    offset = (seq_at * tail_seg + jnp.arange(tail_seg))[None, :] - tail_len[:, None]
    all_beams = jnp.arange(beams)
    every_query, every_fresh = project_tokens(
        step_tokens, in_gain, w_query, w_keyval, q_gain, k_gain
    )
    every_query = every_query.reshape(steps, groups, beams, -1)
    every_fresh = every_fresh.reshape(steps, groups, beams, -1)
    everyone = lax.all_gather(tail_cache, "head", axis=1, tiled=True)
    local_ids = head_at * local_beams + jnp.arange(local_beams)
    n_dev = n_seq * n_head
    owner = jnp.broadcast_to(all_beams[None, :, None], (groups, beams, tail_seg))
    source = jnp.broadcast_to(all_beams[None, :], (groups, beams))
    ancestors = []
    shaped_all, scores_all, tails_all = [], [], []
    for step in range(steps):
        link = parents[step]
        source = jnp.take_along_axis(source, link, axis=1)
        ancestors = [jnp.take_along_axis(a, link, axis=1) for a in ancestors]
        ancestors.append(jnp.broadcast_to(all_beams[None, :], (groups, beams)))
        picks = lax.dynamic_slice_in_dim(source, head_at * local_beams, local_beams, 1)
        tail_state = jnp.take_along_axis(everyone, picks[:, :, None, None], axis=1)
        for back, anc in enumerate(ancestors):
            mine = lax.dynamic_slice_in_dim(anc, head_at * local_beams, local_beams, 1)
            written = jnp.take_along_axis(every_fresh[back], mine[:, :, None], axis=1)
            tail_state = jnp.where(
                (offset == back)[:, None, :, None], written[:, :, None, :], tail_state
            )
        tail_ok = (offset <= step)[:, None, None, :] & (
            owner[:, :, None, :] == local_ids[None, None, :, None]
        )
        shaped = every_query[step].reshape(groups, beams, KVH, repeat, HD)
        tail_keys, tail_values = split_pairs(tail_state)
        pre_scores = jnp.einsum(
            "gbkrd,gtkd->gbkrt", shaped[:pre], prompt_keys, preferred_element_type=f32
        )
        dec_scores = jnp.einsum(
            "gbkrd,gtkd->gbkrt", shaped[pre:], cache_keys, preferred_element_type=f32
        )
        tail_scores = jnp.einsum(
            "gbkrd,gctkd->gbkrct", shaped, tail_keys, preferred_element_type=f32
        )
        pre_scores = jnp.where(prompt_ok[:, None, None, None, :], pre_scores, NEG)
        dec_scores = jnp.where(cache_ok[:, None, None, None, :], dec_scores, NEG)
        tail_scores = jnp.where(tail_ok[:, :, None, None, :, :], tail_scores, NEG)
        top = jnp.concatenate([jnp.max(pre_scores, -1), jnp.max(dec_scores, -1)], 0)
        top = jnp.maximum(top, jnp.max(tail_scores, (-2, -1)))
        scores_all.append((pre_scores, dec_scores, tail_scores))
        tails_all.append((tail_ok, tail_values))
        shaped_all.append(top)
    top_all = exchange_max(jnp.stack(shaped_all), ("seq", "head"), n_dev)
    weighted_all, total_all = [], []
    for step in range(steps):
        pre_scores, dec_scores, tail_scores = scores_all[step]
        tail_ok, tail_values = tails_all[step]
        top = top_all[step]
        pre_mask = prompt_ok[:, None, None, None, :]
        dec_mask = cache_ok[:, None, None, None, :]
        tail_mask = tail_ok[:, :, None, None, :, :]
        pre_weights = jnp.where(pre_mask, jnp.exp(pre_scores - top[:pre, ..., None]), 0.0)
        dec_weights = jnp.where(dec_mask, jnp.exp(dec_scores - top[pre:, ..., None]), 0.0)
        tail_weights = jnp.where(tail_mask, jnp.exp(tail_scores - top[..., None, None]), 0.0)
        total = jnp.concatenate([jnp.sum(pre_weights, -1), jnp.sum(dec_weights, -1)], 0)
        total = total + jnp.sum(tail_weights, (-2, -1))
        weighted = jnp.concatenate(
            [
                jnp.einsum(
                    "gbkrt,gtkd->gbkrd",
                    pre_weights.astype(bf16),
                    prompt_values,
                    preferred_element_type=f32,
                ),
                jnp.einsum(
                    "gbkrt,gtkd->gbkrd",
                    dec_weights.astype(bf16),
                    cache_values,
                    preferred_element_type=f32,
                ),
            ],
            0,
        )
        weighted = weighted + jnp.einsum(
            "gbkrct,gctkd->gbkrd",
            tail_weights.astype(bf16),
            tail_values,
            preferred_element_type=f32,
        )
        weighted_all.append(weighted.reshape(groups * beams, -1))
        total_all.append(total.reshape(groups * beams, -1))
    weighted = jnp.concatenate(weighted_all, 0)
    total = jnp.concatenate(total_all, 0)
    rows = weighted.shape[0]
    piece = QD // n_dev
    piece_head = jnp.arange(n_dev) * piece // HD
    lanes = -(-rows // 128) * 128
    packed = jnp.concatenate(
        [
            jnp.transpose(weighted.reshape(rows, n_dev, piece), (1, 0, 2)).reshape(n_dev, -1),
            jnp.pad(jnp.transpose(total[:, piece_head]), ((0, 0), (0, lanes - rows))),
        ],
        1,
    )
    packed = exchange_sum(packed, ("seq", "head"))
    share = packed[: rows * piece].reshape(rows, piece)
    own_total = packed[rows * piece : rows * piece + rows]
    attn = (share / own_total[:, None]).astype(bf16)
    attn = exchange_gather(attn, "head", n_head)
    attn = jnp.transpose(attn, (1, 0, 2)).reshape(rows, -1)
    partial_out = jnp.dot(attn, w_out, preferred_element_type=f32)
    per_dev = rows // n_seq
    out_proj = exchange_sum(partial_out.reshape(n_seq, per_dev, -1), "seq")
    out_sq = lax.psum(jnp.sum(out_proj * out_proj, -1), "head")
    x_all = step_tokens.reshape(rows, -1)
    x_f = lax.dynamic_slice_in_dim(x_all, seq_at * per_dev, per_dev, 0).astype(f32)
    state = (x_f + out_proj * lax.rsqrt(out_sq / D + EPS)[:, None] * post_gain).astype(bf16)
    state_all = exchange_gather(state, "seq", n_seq).reshape(rows, -1)
    state_f = state_all.astype(f32)
    scaled_two = (state_f * ffn_gain).astype(bf16)
    gate_part = jnp.dot(scaled_two, w_gate, preferred_element_type=f32)
    up_part = jnp.dot(scaled_two, w_up, preferred_element_type=f32)
    hidden = gate_part.shape[1]
    head_rows = rows // n_head
    packed = jnp.concatenate(
        [gate_part, up_part, jnp.pad(jnp.sum(state_f * state_f, -1)[:, None], ((0, 0), (0, 127)))],
        1,
    )
    packed = exchange_sum(packed.reshape(n_head, head_rows, -1), "head")
    norm_s = lax.rsqrt(packed[:, 2 * hidden] / D + EPS)[:, None]
    inner = (
        jax.nn.gelu(packed[:, :hidden] * norm_s, approximate=True)
        * (packed[:, hidden : 2 * hidden] * norm_s)
    ).astype(bf16)
    inner = exchange_gather(inner, "head", n_head).reshape(rows, hidden)
    ffn_out = exchange_sum(
        jnp.dot(inner, w_down, preferred_element_type=f32).reshape(n_seq, per_dev, -1), "seq"
    )
    ffn_sq = lax.psum(jnp.sum(ffn_out * ffn_out, -1), "head")
    result = (
        state.astype(f32) + ffn_out * lax.rsqrt(ffn_sq / D + EPS)[:, None] * final_gain
    ).astype(bf16)
    result = exchange_gather(result, "seq", n_seq)
    return result.reshape(steps, groups, beams, -1)


def solution(mesh):
    return jax.shard_map(
        shards,
        mesh=mesh,
        in_specs=(
            P(None, None, None, "head"),
            P(),
            P(None, "head", "seq", None),
            P(),
            P(None, ("seq", "head"), None),
            P(),
            P(None, "seq", "head"),
            P(),
            P("head"),
            P("head", "seq"),
            P("head", "seq"),
            P(),
            P(),
            P("seq", "head"),
            P("head"),
            P("head"),
            P("head", "seq"),
            P("head", "seq"),
            P("seq", "head"),
            P("head"),
        ),
        out_specs=P(None, None, None, "head"),
        check_vma=False,
    )
```

```python
import jax
import jax.numpy as jnp
from jax import lax
from jax.sharding import PartitionSpec as P

D = 2560
QH = 8
KVH = 4
HD = 256
QD = 2048


EPS = 1e-06
NEG = -1e30
QSCALE = 0.0625


def norm_heads(values, gain, scale):
    shaped = values.reshape(values.shape[:-1] + (-1, gain.shape[0]))
    shaped = shaped * lax.rsqrt(jnp.mean(shaped * shaped, -1, keepdims=True) + EPS) * gain * scale
    return shaped.reshape(values.shape)


def finish_keys(pairs, k_gain):
    half = pairs.shape[-1] // 2
    keys = norm_heads(pairs[..., :half], k_gain, 1.0)
    return jnp.concatenate([keys, pairs[..., half:]], -1).astype(jnp.bfloat16)


def split_pairs(pairs):
    half = pairs.shape[-1] // 2
    keys = pairs[..., :half].reshape(pairs.shape[:-1] + (KVH, HD))
    values = pairs[..., half:].reshape(pairs.shape[:-1] + (KVH, HD))
    return (keys, values)


def exchange_sum(parts, axes, narrow=False):
    if narrow:
        moved = lax.all_to_all(parts.astype(jnp.bfloat16), axes, 0, 0, tiled=True)
        return jnp.sum(moved.astype(jnp.float32), 0)
    return jnp.sum(lax.all_to_all(parts, axes, 0, 0, tiled=True), 0)


def exchange_max(value, axes, count):
    spread = jnp.broadcast_to(value[None], (count,) + value.shape)
    return jnp.max(lax.all_to_all(spread, axes, 0, 0, tiled=True), 0)


def exchange_gather(piece, axes, count):
    spread = jnp.broadcast_to(piece[None], (count,) + piece.shape)
    return lax.all_to_all(spread, axes, 0, 0, tiled=True)


def project_tokens(tokens, in_gain, w_query, w_keyval, q_gain, k_gain):
    flat = tokens.reshape(-1, tokens.shape[-1]).astype(jnp.float32)
    scaled = (flat * in_gain).astype(jnp.bfloat16)
    q_part = jnp.dot(scaled, w_query, preferred_element_type=jnp.float32)
    kv_part = jnp.dot(scaled, w_keyval, preferred_element_type=jnp.float32)
    squares = jnp.sum(flat * flat, -1)
    n_head = lax.axis_size("head")
    n_seq = lax.axis_size("seq")
    rows = flat.shape[0]
    half = rows // n_head
    block = q_part.shape[1]
    packed = jnp.concatenate([q_part, kv_part, jnp.pad(squares[:, None], ((0, 0), (0, 127)))], 1)
    packed = exchange_sum(packed.reshape(n_head, half, -1), "head")
    factor = lax.rsqrt(packed[:, 2 * block] / D + EPS)[:, None]
    q_raw = (packed[:, :block] * factor).astype(jnp.bfloat16)
    kv_raw = (packed[:, block : 2 * block] * factor).astype(jnp.bfloat16)
    both = exchange_gather(
        jnp.concatenate([q_raw, kv_raw], 1), ("seq", "head"), n_seq * n_head
    ).reshape(n_seq, n_head, half, 2 * block)
    both = jnp.transpose(both, (1, 2, 0, 3)).reshape(rows, n_seq, 2 * block)
    q_raw = both[:, :, :block].reshape(rows, -1)
    kv_raw = both[:, :, block:].reshape(rows, -1)
    queries = norm_heads(q_raw.astype(jnp.float32), q_gain, QSCALE).astype(jnp.bfloat16)
    fresh = finish_keys(kv_raw.astype(jnp.float32), k_gain)
    return (queries, fresh)


def shards(
    step_tokens,
    parents,
    tail_cache,
    tail_len,
    cache,
    cache_len,
    prompt_states,
    prompt_len,
    in_gain,
    w_query,
    w_keyval,
    q_gain,
    k_gain,
    w_out,
    post_gain,
    ffn_gain,
    w_gate,
    w_up,
    w_down,
    final_gain,
):
    f32 = jnp.float32
    bf16 = jnp.bfloat16
    n_head = lax.axis_size("head")
    n_seq = lax.axis_size("seq")
    seq_at = lax.axis_index("seq")
    head_at = lax.axis_index("head")
    flat_at = seq_at * n_head + head_at
    steps, groups, beams, width = step_tokens.shape
    pre = prompt_states.shape[0]
    repeat = QH // KVH
    rows = jnp.transpose(prompt_states, (1, 0, 2)).astype(f32)
    prompt_scaled = (rows * in_gain).astype(bf16).reshape(-1, width)
    prompt_squares = jnp.sum(rows * rows, -1).reshape(-1)
    prompt_terms = jnp.dot(
        prompt_scaled,
        lax.all_gather(w_keyval, "seq", axis=1, tiled=True),
        preferred_element_type=f32,
    )
    prompt_sum, prompt_sq = (
        lax.psum_scatter(prompt_terms, "head", scatter_dimension=0, tiled=True),
        lax.psum_scatter(prompt_squares, "head", scatter_dimension=0, tiled=True),
    )
    prompt_pairs = finish_keys(prompt_sum * lax.rsqrt(prompt_sq / D + EPS)[:, None], k_gain)
    prompt_seg = prompt_pairs.shape[0] // pre
    prompt_pairs = jnp.transpose(prompt_pairs.reshape(prompt_seg, pre, -1), (1, 0, 2))
    prompt_ok = (flat_at * prompt_seg + jnp.arange(prompt_seg))[None, :] < prompt_len[:, None]
    cache_seg = cache.shape[1]
    cache_ok = (flat_at * cache_seg + jnp.arange(cache_seg))[None, :] < cache_len[:, None]
    span = max(prompt_seg, cache_seg)
    shared = jnp.concatenate(
        [
            jnp.pad(prompt_pairs, ((0, 0), (0, span - prompt_seg), (0, 0))),
            jnp.pad(cache, ((0, 0), (0, span - cache_seg), (0, 0))),
        ],
        0,
    )
    shared_ok = jnp.concatenate(
        [
            jnp.pad(prompt_ok, ((0, 0), (0, span - prompt_seg))),
            jnp.pad(cache_ok, ((0, 0), (0, span - cache_seg))),
        ],
        0,
    )
    shared_keys, shared_values = split_pairs(shared)
    tail_seg = tail_cache.shape[2]
    local_beams = tail_cache.shape[1]
    offset = (seq_at * tail_seg + jnp.arange(tail_seg))[None, :] - tail_len[:, None]
    all_beams = jnp.arange(beams)
    every_query, every_fresh = project_tokens(
        step_tokens, in_gain, w_query, w_keyval, q_gain, k_gain
    )
    every_query = every_query.reshape(steps, groups, beams, -1)
    every_fresh = every_fresh.reshape(steps, groups, beams, -1)
    everyone = lax.all_gather(tail_cache, "head", axis=1, tiled=True)
    n_dev = n_seq * n_head
    first_beam = head_at * local_beams
    many = steps * beams * repeat
    grouped = jnp.transpose(
        every_query.reshape(steps, groups, beams, KVH, repeat, HD), (1, 3, 0, 2, 4, 5)
    ).reshape(groups, KVH, many, HD)
    scores = jnp.einsum("gkmd,gtkd->gkmt", grouped, shared_keys, preferred_element_type=f32)
    scores = jnp.where(shared_ok[:, None, None, :], scores, NEG)
    top = jnp.max(scores, -1).reshape(groups, KVH, steps, beams, repeat)
    source = jnp.broadcast_to(all_beams[None, :], (groups, beams))
    ancestors = []
    tail_parts = []
    tail_tops = []
    for step in range(steps):
        link = parents[step]
        source = jnp.take_along_axis(source, link, axis=1)
        ancestors = [jnp.take_along_axis(a, link, axis=1) for a in ancestors]
        ancestors.append(jnp.broadcast_to(all_beams[None, :], (groups, beams)))
        picks = lax.dynamic_slice_in_dim(source, first_beam, local_beams, 1)
        tail_state = jnp.take_along_axis(everyone, picks[:, :, None, None], axis=1)
        for back, anc in enumerate(ancestors):
            mine = lax.dynamic_slice_in_dim(anc, first_beam, local_beams, 1)
            written = jnp.take_along_axis(every_fresh[back], mine[:, :, None], axis=1)
            tail_state = jnp.where(
                (offset == back)[:, None, :, None], written[:, :, None, :], tail_state
            )
        tail_keys, tail_values = split_pairs(tail_state)
        local_query = lax.dynamic_slice_in_dim(every_query[step], first_beam, local_beams, 1)
        local_query = local_query.reshape(groups, local_beams, KVH, repeat, HD)
        tail_scores = jnp.einsum(
            "gckrd,gctkd->gckrt", local_query, tail_keys, preferred_element_type=f32
        )
        tail_ok = (offset <= step)[:, None, None, None, :]
        tail_scores = jnp.where(tail_ok, tail_scores, NEG)
        tail_parts.append((tail_scores, tail_ok, tail_values))
        tail_top = lax.dynamic_update_slice(
            jnp.full((groups, beams, KVH, repeat), NEG, f32),
            jnp.max(tail_scores, -1),
            (0, first_beam, 0, 0),
        )
        tail_tops.append(jnp.transpose(tail_top, (0, 2, 1, 3)))
    top = jnp.maximum(top, jnp.stack(tail_tops, 2))
    top = exchange_max(top, ("seq", "head"), n_dev)
    weights = jnp.where(
        shared_ok[:, None, None, :], jnp.exp(scores - top.reshape(groups, KVH, many)[..., None]), 0.0
    )
    total = jnp.sum(weights, -1).reshape(groups, KVH, steps, beams, repeat)
    weighted = jnp.einsum(
        "gkmt,gtkd->gkmd", weights.astype(bf16), shared_values, preferred_element_type=f32
    ).reshape(groups, KVH, steps, beams, repeat, HD)
    tail_totals, tail_weighted = [], []
    for step in range(steps):
        tail_scores, tail_ok, tail_values = tail_parts[step]
        local_top = lax.dynamic_slice_in_dim(top[:, :, step], first_beam, local_beams, 2)
        local_top = jnp.transpose(local_top, (0, 2, 1, 3))
        tail_weights = jnp.where(tail_ok, jnp.exp(tail_scores - local_top[..., None]), 0.0)
        tail_total = lax.dynamic_update_slice(
            jnp.zeros((groups, beams, KVH, repeat), f32),
            jnp.sum(tail_weights, -1),
            (0, first_beam, 0, 0),
        )
        tail_sum = lax.dynamic_update_slice(
            jnp.zeros((groups, beams, KVH, repeat, HD), f32),
            jnp.einsum(
                "gckrt,gctkd->gckrd",
                tail_weights.astype(bf16),
                tail_values,
                preferred_element_type=f32,
            ),
            (0, first_beam, 0, 0, 0),
        )
        tail_totals.append(jnp.transpose(tail_total, (0, 2, 1, 3)))
        tail_weighted.append(jnp.transpose(tail_sum, (0, 2, 1, 3, 4)))
    total = total + jnp.stack(tail_totals, 2)
    weighted = weighted + jnp.stack(tail_weighted, 2)
    rows = steps * groups * beams
    piece = QD // n_dev
    per_head = HD // piece
    weighted = jnp.transpose(
        weighted.reshape(groups, KVH, steps, beams, repeat, per_head, piece), (1, 4, 5, 2, 0, 3, 6)
    ).reshape(n_dev, -1)
    total = jnp.repeat(jnp.transpose(total, (1, 4, 2, 0, 3)).reshape(QH, rows), per_head, 0)
    lanes = -(-rows // 128) * 128
    packed = jnp.concatenate([weighted, jnp.pad(total, ((0, 0), (0, lanes - rows)))], 1)
    packed = exchange_sum(packed, ("seq", "head"))
    share = packed[: rows * piece].reshape(rows, piece)
    own_total = packed[rows * piece : rows * piece + rows]
    attn = (share / own_total[:, None]).astype(bf16)
    attn = exchange_gather(attn, "head", n_head)
    attn = jnp.transpose(attn, (1, 0, 2)).reshape(rows, -1)
    partial_out = jnp.dot(attn, w_out, preferred_element_type=f32)
    per_dev = rows // n_seq
    out_proj = exchange_sum(partial_out.reshape(n_seq, per_dev, -1), "seq")
    out_sq = lax.psum(jnp.sum(out_proj * out_proj, -1), "head")
    x_all = step_tokens.reshape(rows, -1)
    x_f = lax.dynamic_slice_in_dim(x_all, seq_at * per_dev, per_dev, 0).astype(f32)
    state = (x_f + out_proj * lax.rsqrt(out_sq / D + EPS)[:, None] * post_gain).astype(bf16)
    state_all = exchange_gather(state, "seq", n_seq).reshape(rows, -1)
    state_f = state_all.astype(f32)
    scaled_two = (state_f * ffn_gain).astype(bf16)
    gate_part = jnp.dot(scaled_two, w_gate, preferred_element_type=f32)
    up_part = jnp.dot(scaled_two, w_up, preferred_element_type=f32)
    hidden = gate_part.shape[1]
    head_rows = rows // n_head
    packed = jnp.concatenate(
        [gate_part, up_part, jnp.pad(jnp.sum(state_f * state_f, -1)[:, None], ((0, 0), (0, 127)))],
        1,
    )
    packed = exchange_sum(packed.reshape(n_head, head_rows, -1), "head")
    norm_s = lax.rsqrt(packed[:, 2 * hidden] / D + EPS)[:, None]
    inner = (
        jax.nn.gelu(packed[:, :hidden] * norm_s, approximate=True)
        * (packed[:, hidden : 2 * hidden] * norm_s)
    ).astype(bf16)
    inner = exchange_gather(inner, "head", n_head).reshape(rows, hidden)
    ffn_out = exchange_sum(
        jnp.dot(inner, w_down, preferred_element_type=f32).reshape(n_seq, per_dev, -1), "seq"
    )
    ffn_sq = lax.psum(jnp.sum(ffn_out * ffn_out, -1), "head")
    result = (
        state.astype(f32) + ffn_out * lax.rsqrt(ffn_sq / D + EPS)[:, None] * final_gain
    ).astype(bf16)
    result = exchange_gather(result, "seq", n_seq)
    return result.reshape(steps, groups, beams, -1)


def solution(mesh):
    return jax.shard_map(
        shards,
        mesh=mesh,
        in_specs=(
            P(None, None, None, "head"),
            P(),
            P(None, "head", "seq", None),
            P(),
            P(None, ("seq", "head"), None),
            P(),
            P(None, "seq", "head"),
            P(),
            P("head"),
            P("head", "seq"),
            P("head", "seq"),
            P(),
            P(),
            P("seq", "head"),
            P("head"),
            P("head"),
            P("head", "seq"),
            P("head", "seq"),
            P("seq", "head"),
            P("head"),
        ),
        out_specs=P(None, None, None, "head"),
        check_vma=False,
    )
```

```python
import jax
import jax.numpy as jnp
from jax import lax
from jax.sharding import PartitionSpec as P

D = 2560
QH = 8
KVH = 4
HD = 256
QD = 2048


SEQ = ("seq", "pair")
ALL = ("seq", "pair", "head")

EPS = 1e-06
NEG = -1e30
QSCALE = 0.0625


def norm_heads(values, gain, scale):
    shaped = values.reshape(values.shape[:-1] + (-1, gain.shape[0]))
    shaped = shaped * lax.rsqrt(jnp.mean(shaped * shaped, -1, keepdims=True) + EPS) * gain * scale
    return shaped.reshape(values.shape)


def finish_keys(pairs, k_gain):
    half = pairs.shape[-1] // 2
    keys = norm_heads(pairs[..., :half], k_gain, 1.0)
    return jnp.concatenate([keys, pairs[..., half:]], -1).astype(jnp.bfloat16)


def split_pairs(pairs):
    half = pairs.shape[-1] // 2
    keys = pairs[..., :half].reshape(pairs.shape[:-1] + (KVH, HD))
    values = pairs[..., half:].reshape(pairs.shape[:-1] + (KVH, HD))
    return (keys, values)


def exchange_sum(parts, axes, narrow=False):
    if narrow:
        moved = lax.all_to_all(parts.astype(jnp.bfloat16), axes, 0, 0, tiled=True)
        return jnp.sum(moved.astype(jnp.float32), 0)
    return jnp.sum(lax.all_to_all(parts, axes, 0, 0, tiled=True), 0)


def exchange_max(value, axes, count):
    spread = jnp.broadcast_to(value[None], (count,) + value.shape)
    return jnp.max(lax.all_to_all(spread, axes, 0, 0, tiled=True), 0)


def exchange_gather(piece, axes, count):
    spread = jnp.broadcast_to(piece[None], (count,) + piece.shape)
    return lax.all_to_all(spread, axes, 0, 0, tiled=True)


def seq_sum(parts):
    pair = lax.axis_size("pair")
    parts = parts.reshape((parts.shape[0] // pair, pair) + parts.shape[1:])
    parts = exchange_sum(jnp.swapaxes(parts, 0, 1), "pair")
    return exchange_sum(parts, "seq")


def seq_gather(piece):
    pair = lax.axis_size("pair")
    outer = lax.axis_size("seq")
    got = exchange_gather(exchange_gather(piece, "seq", outer), "pair", pair)
    return jnp.swapaxes(got, 0, 1).reshape((outer * pair,) + piece.shape)


def project_tokens(tokens, in_gain, w_query, w_keyval, q_gain, k_gain):
    flat = tokens.reshape(-1, tokens.shape[-1]).astype(jnp.float32)
    scaled = (flat * in_gain).astype(jnp.bfloat16)
    q_part = jnp.dot(scaled, w_query, preferred_element_type=jnp.float32)
    kv_part = jnp.dot(scaled, w_keyval, preferred_element_type=jnp.float32)
    squares = jnp.sum(flat * flat, -1)
    n_head = lax.axis_size("head")
    n_seq = lax.axis_size("seq") * lax.axis_size("pair")
    rows = flat.shape[0]
    half = rows // n_head
    block = q_part.shape[1]
    packed = jnp.concatenate([q_part, kv_part, jnp.pad(squares[:, None], ((0, 0), (0, 127)))], 1)
    packed = exchange_sum(packed.reshape(n_head, half, -1), "head")
    factor = lax.rsqrt(packed[:, 2 * block] / D + EPS)[:, None]
    q_raw = (packed[:, :block] * factor).astype(jnp.bfloat16)
    kv_raw = (packed[:, block : 2 * block] * factor).astype(jnp.bfloat16)
    both = exchange_gather(
        jnp.concatenate([q_raw, kv_raw], 1), ALL, n_seq * n_head
    ).reshape(n_seq, n_head, half, 2 * block)
    both = jnp.transpose(both, (1, 2, 0, 3)).reshape(rows, n_seq, 2 * block)
    q_raw = both[:, :, :block].reshape(rows, -1)
    kv_raw = both[:, :, block:].reshape(rows, -1)
    queries = norm_heads(q_raw.astype(jnp.float32), q_gain, QSCALE).astype(jnp.bfloat16)
    fresh = finish_keys(kv_raw.astype(jnp.float32), k_gain)
    return (queries, fresh)


def shards(
    step_tokens,
    parents,
    tail_cache,
    tail_len,
    cache,
    cache_len,
    prompt_states,
    prompt_len,
    in_gain,
    w_query,
    w_keyval,
    q_gain,
    k_gain,
    w_out,
    post_gain,
    ffn_gain,
    w_gate,
    w_up,
    w_down,
    final_gain,
):
    f32 = jnp.float32
    bf16 = jnp.bfloat16
    n_head = lax.axis_size("head")
    n_seq = lax.axis_size("seq") * lax.axis_size("pair")
    seq_at = lax.axis_index("seq") * lax.axis_size("pair") + lax.axis_index("pair")
    head_at = lax.axis_index("head")
    flat_at = seq_at * n_head + head_at
    steps, groups, beams, width = step_tokens.shape
    pre = prompt_states.shape[0]
    repeat = QH // KVH
    rows = jnp.transpose(prompt_states, (1, 0, 2)).astype(f32)
    prompt_scaled = (rows * in_gain).astype(bf16).reshape(-1, width)
    prompt_squares = jnp.sum(rows * rows, -1).reshape(-1)
    prompt_terms = jnp.dot(
        prompt_scaled,
        lax.all_gather(w_keyval, SEQ, axis=1, tiled=True),
        preferred_element_type=f32,
    )
    prompt_sum, prompt_sq = (
        lax.psum_scatter(prompt_terms, "head", scatter_dimension=0, tiled=True),
        lax.psum_scatter(prompt_squares, "head", scatter_dimension=0, tiled=True),
    )
    prompt_pairs = finish_keys(prompt_sum * lax.rsqrt(prompt_sq / D + EPS)[:, None], k_gain)
    prompt_seg = prompt_pairs.shape[0] // pre
    prompt_pairs = jnp.transpose(prompt_pairs.reshape(prompt_seg, pre, -1), (1, 0, 2))
    prompt_ok = (flat_at * prompt_seg + jnp.arange(prompt_seg))[None, :] < prompt_len[:, None]
    cache_seg = cache.shape[1]
    cache_ok = (flat_at * cache_seg + jnp.arange(cache_seg))[None, :] < cache_len[:, None]
    span = max(prompt_seg, cache_seg)
    shared = jnp.concatenate(
        [
            jnp.pad(prompt_pairs, ((0, 0), (0, span - prompt_seg), (0, 0))),
            jnp.pad(cache, ((0, 0), (0, span - cache_seg), (0, 0))),
        ],
        0,
    )
    shared_ok = jnp.concatenate(
        [
            jnp.pad(prompt_ok, ((0, 0), (0, span - prompt_seg))),
            jnp.pad(cache_ok, ((0, 0), (0, span - cache_seg))),
        ],
        0,
    )
    shared_keys, shared_values = split_pairs(shared)
    tail_seg = tail_cache.shape[2]
    local_beams = tail_cache.shape[1]
    offset = (seq_at * tail_seg + jnp.arange(tail_seg))[None, :] - tail_len[:, None]
    all_beams = jnp.arange(beams)
    every_query, every_fresh = project_tokens(
        step_tokens, in_gain, w_query, w_keyval, q_gain, k_gain
    )
    every_query = every_query.reshape(steps, groups, beams, -1)
    every_fresh = every_fresh.reshape(steps, groups, beams, -1)
    everyone = lax.all_gather(tail_cache, "head", axis=1, tiled=True)
    n_dev = n_seq * n_head
    first_beam = head_at * local_beams
    many = steps * beams * repeat
    grouped = jnp.transpose(
        every_query.reshape(steps, groups, beams, KVH, repeat, HD), (1, 3, 0, 2, 4, 5)
    ).reshape(groups, KVH, many, HD)
    scores = jnp.einsum("gkmd,gtkd->gkmt", grouped, shared_keys, preferred_element_type=f32)
    scores = jnp.where(shared_ok[:, None, None, :], scores, NEG)
    top = jnp.max(scores, -1).reshape(groups, KVH, steps, beams, repeat)
    source = jnp.broadcast_to(all_beams[None, :], (groups, beams))
    ancestors = []
    tail_parts = []
    tail_tops = []
    for step in range(steps):
        link = parents[step]
        source = jnp.take_along_axis(source, link, axis=1)
        ancestors = [jnp.take_along_axis(a, link, axis=1) for a in ancestors]
        ancestors.append(jnp.broadcast_to(all_beams[None, :], (groups, beams)))
        picks = lax.dynamic_slice_in_dim(source, first_beam, local_beams, 1)
        tail_state = jnp.take_along_axis(everyone, picks[:, :, None, None], axis=1)
        for back, anc in enumerate(ancestors):
            mine = lax.dynamic_slice_in_dim(anc, first_beam, local_beams, 1)
            written = jnp.take_along_axis(every_fresh[back], mine[:, :, None], axis=1)
            tail_state = jnp.where(
                (offset == back)[:, None, :, None], written[:, :, None, :], tail_state
            )
        tail_keys, tail_values = split_pairs(tail_state)
        local_query = lax.dynamic_slice_in_dim(every_query[step], first_beam, local_beams, 1)
        local_query = local_query.reshape(groups, local_beams, KVH, repeat, HD)
        tail_scores = jnp.einsum(
            "gckrd,gctkd->gckrt", local_query, tail_keys, preferred_element_type=f32
        )
        tail_ok = (offset <= step)[:, None, None, None, :]
        tail_scores = jnp.where(tail_ok, tail_scores, NEG)
        tail_parts.append((tail_scores, tail_ok, tail_values))
        tail_top = lax.dynamic_update_slice(
            jnp.full((groups, beams, KVH, repeat), NEG, f32),
            jnp.max(tail_scores, -1),
            (0, first_beam, 0, 0),
        )
        tail_tops.append(jnp.transpose(tail_top, (0, 2, 1, 3)))
    top = jnp.maximum(top, jnp.stack(tail_tops, 2))
    top = exchange_max(top, ALL, n_dev)
    weights = jnp.where(
        shared_ok[:, None, None, :], jnp.exp(scores - top.reshape(groups, KVH, many)[..., None]), 0.0
    )
    total = jnp.sum(weights, -1).reshape(groups, KVH, steps, beams, repeat)
    weighted = jnp.einsum(
        "gkmt,gtkd->gkmd", weights.astype(bf16), shared_values, preferred_element_type=f32
    ).reshape(groups, KVH, steps, beams, repeat, HD)
    tail_totals, tail_weighted = [], []
    for step in range(steps):
        tail_scores, tail_ok, tail_values = tail_parts[step]
        local_top = lax.dynamic_slice_in_dim(top[:, :, step], first_beam, local_beams, 2)
        local_top = jnp.transpose(local_top, (0, 2, 1, 3))
        tail_weights = jnp.where(tail_ok, jnp.exp(tail_scores - local_top[..., None]), 0.0)
        tail_total = lax.dynamic_update_slice(
            jnp.zeros((groups, beams, KVH, repeat), f32),
            jnp.sum(tail_weights, -1),
            (0, first_beam, 0, 0),
        )
        tail_sum = lax.dynamic_update_slice(
            jnp.zeros((groups, beams, KVH, repeat, HD), f32),
            jnp.einsum(
                "gckrt,gctkd->gckrd",
                tail_weights.astype(bf16),
                tail_values,
                preferred_element_type=f32,
            ),
            (0, first_beam, 0, 0, 0),
        )
        tail_totals.append(jnp.transpose(tail_total, (0, 2, 1, 3)))
        tail_weighted.append(jnp.transpose(tail_sum, (0, 2, 1, 3, 4)))
    total = total + jnp.stack(tail_totals, 2)
    weighted = weighted + jnp.stack(tail_weighted, 2)
    rows = steps * groups * beams
    piece = QD // n_dev
    per_head = HD // piece
    weighted = jnp.transpose(
        weighted.reshape(groups, KVH, steps, beams, repeat, per_head, piece), (1, 4, 5, 2, 0, 3, 6)
    ).reshape(n_dev, -1)
    total = jnp.repeat(jnp.transpose(total, (1, 4, 2, 0, 3)).reshape(QH, rows), per_head, 0)
    lanes = -(-rows // 128) * 128
    packed = jnp.concatenate([weighted, jnp.pad(total, ((0, 0), (0, lanes - rows)))], 1)
    pair = lax.axis_size("pair")
    packed = packed.reshape(n_seq // pair, pair, n_head, -1)
    packed = exchange_sum(jnp.swapaxes(packed, 0, 1), "pair").reshape(n_dev // pair, -1)
    packed = exchange_sum(packed, ("seq", "head"))
    share = packed[: rows * piece].reshape(rows, piece)
    own_total = packed[rows * piece : rows * piece + rows]
    attn = (share / own_total[:, None]).astype(bf16)
    attn = exchange_gather(attn, "head", n_head)
    attn = jnp.transpose(attn, (1, 0, 2)).reshape(rows, -1)
    partial_out = jnp.dot(attn, w_out, preferred_element_type=f32)
    per_dev = rows // n_seq
    out_proj = seq_sum(partial_out.reshape(n_seq, per_dev, -1))
    out_sq = lax.psum(jnp.sum(out_proj * out_proj, -1), "head")
    x_all = step_tokens.reshape(rows, -1)
    x_f = lax.dynamic_slice_in_dim(x_all, seq_at * per_dev, per_dev, 0).astype(f32)
    state = (x_f + out_proj * lax.rsqrt(out_sq / D + EPS)[:, None] * post_gain).astype(bf16)
    state_all = seq_gather(state).reshape(rows, -1)
    state_f = state_all.astype(f32)
    scaled_two = (state_f * ffn_gain).astype(bf16)
    gate_part = jnp.dot(scaled_two, w_gate, preferred_element_type=f32)
    up_part = jnp.dot(scaled_two, w_up, preferred_element_type=f32)
    hidden = gate_part.shape[1]
    head_rows = rows // n_head
    packed = jnp.concatenate(
        [gate_part, up_part, jnp.pad(jnp.sum(state_f * state_f, -1)[:, None], ((0, 0), (0, 127)))],
        1,
    )
    packed = exchange_sum(packed.reshape(n_head, head_rows, -1), "head")
    norm_s = lax.rsqrt(packed[:, 2 * hidden] / D + EPS)[:, None]
    inner = (
        jax.nn.gelu(packed[:, :hidden] * norm_s, approximate=True)
        * (packed[:, hidden : 2 * hidden] * norm_s)
    ).astype(bf16)
    inner = exchange_gather(inner, "head", n_head).reshape(rows, hidden)
    ffn_out = seq_sum(jnp.dot(inner, w_down, preferred_element_type=f32).reshape(n_seq, per_dev, -1))
    ffn_sq = lax.psum(jnp.sum(ffn_out * ffn_out, -1), "head")
    result = (
        state.astype(f32) + ffn_out * lax.rsqrt(ffn_sq / D + EPS)[:, None] * final_gain
    ).astype(bf16)
    result = seq_gather(result)
    return result.reshape(steps, groups, beams, -1)


def solution(mesh):
    devices = mesh.devices
    fine = jax.sharding.Mesh(
        devices.reshape(devices.shape[0] // 2, 2, devices.shape[1]), ("seq", "pair", "head")
    )
    return jax.shard_map(
        shards,
        mesh=fine,
        in_specs=(
            P(None, None, None, "head"),
            P(),
            P(None, "head", SEQ, None),
            P(),
            P(None, ALL, None),
            P(),
            P(None, SEQ, "head"),
            P(),
            P("head"),
            P("head", SEQ),
            P("head", SEQ),
            P(),
            P(),
            P(SEQ, "head"),
            P("head"),
            P("head"),
            P("head", SEQ),
            P("head", SEQ),
            P(SEQ, "head"),
            P("head"),
        ),
        out_specs=P(None, None, None, "head"),
        check_vma=False,
    )
```

```python
import jax
import jax.numpy as jnp
from jax import lax
from jax.sharding import PartitionSpec as P

D = 2560
QH = 8
KVH = 4
HD = 256
QD = 2048


SEQ = ("seq", "mid", "pair")
ALL = ("seq", "mid", "pair", "head")
LEVELS = ("pair", "mid")

EPS = 1e-06
NEG = -1e30
QSCALE = 0.0625


def norm_heads(values, gain, scale):
    shaped = values.reshape(values.shape[:-1] + (-1, gain.shape[0]))
    shaped = shaped * lax.rsqrt(jnp.mean(shaped * shaped, -1, keepdims=True) + EPS) * gain * scale
    return shaped.reshape(values.shape)


def finish_keys(pairs, k_gain):
    half = pairs.shape[-1] // 2
    keys = norm_heads(pairs[..., :half], k_gain, 1.0)
    return jnp.concatenate([keys, pairs[..., half:]], -1).astype(jnp.bfloat16)


def split_pairs(pairs):
    half = pairs.shape[-1] // 2
    keys = pairs[..., :half].reshape(pairs.shape[:-1] + (KVH, HD))
    values = pairs[..., half:].reshape(pairs.shape[:-1] + (KVH, HD))
    return (keys, values)


def exchange_sum(parts, axes, narrow=False):
    if narrow:
        moved = lax.all_to_all(parts.astype(jnp.bfloat16), axes, 0, 0, tiled=True)
        return jnp.sum(moved.astype(jnp.float32), 0)
    return jnp.sum(lax.all_to_all(parts, axes, 0, 0, tiled=True), 0)


def exchange_max(value, axes, count):
    spread = jnp.broadcast_to(value[None], (count,) + value.shape)
    return jnp.max(lax.all_to_all(spread, axes, 0, 0, tiled=True), 0)


def exchange_gather(piece, axes, count):
    spread = jnp.broadcast_to(piece[None], (count,) + piece.shape)
    return lax.all_to_all(spread, axes, 0, 0, tiled=True)


def seq_size():
    size = lax.axis_size("seq")
    for level in LEVELS:
        size = size * lax.axis_size(level)
    return size


def seq_sum(parts):
    for level in LEVELS:
        parts = parts.reshape((-1, lax.axis_size(level)) + parts.shape[1:])
        parts = exchange_sum(jnp.swapaxes(parts, 0, 1), level)
    return exchange_sum(parts, "seq")


def seq_gather(piece):
    got = exchange_gather(piece, "seq", lax.axis_size("seq"))
    for level in LEVELS[::-1]:
        got = exchange_gather(got, level, lax.axis_size(level))
        got = jnp.swapaxes(got, 0, 1).reshape((-1,) + piece.shape)
    return got


def project_tokens(tokens, in_gain, w_query, w_keyval, q_gain, k_gain):
    flat = tokens.reshape(-1, tokens.shape[-1]).astype(jnp.float32)
    scaled = (flat * in_gain).astype(jnp.bfloat16)
    q_part = jnp.dot(scaled, w_query, preferred_element_type=jnp.float32)
    kv_part = jnp.dot(scaled, w_keyval, preferred_element_type=jnp.float32)
    squares = jnp.sum(flat * flat, -1)
    n_head = lax.axis_size("head")
    n_seq = seq_size()
    rows = flat.shape[0]
    half = rows // n_head
    block = q_part.shape[1]
    packed = jnp.concatenate([q_part, kv_part, jnp.pad(squares[:, None], ((0, 0), (0, 127)))], 1)
    packed = exchange_sum(packed.reshape(n_head, half, -1), "head")
    factor = lax.rsqrt(packed[:, 2 * block] / D + EPS)[:, None]
    q_raw = (packed[:, :block] * factor).astype(jnp.bfloat16)
    kv_raw = (packed[:, block : 2 * block] * factor).astype(jnp.bfloat16)
    both = exchange_gather(
        jnp.concatenate([q_raw, kv_raw], 1), ALL, n_seq * n_head
    ).reshape(n_seq, n_head, half, 2 * block)
    both = jnp.transpose(both, (1, 2, 0, 3)).reshape(rows, n_seq, 2 * block)
    q_raw = both[:, :, :block].reshape(rows, -1)
    kv_raw = both[:, :, block:].reshape(rows, -1)
    queries = norm_heads(q_raw.astype(jnp.float32), q_gain, QSCALE).astype(jnp.bfloat16)
    fresh = finish_keys(kv_raw.astype(jnp.float32), k_gain)
    return (queries, fresh)


def shards(
    step_tokens,
    parents,
    tail_cache,
    tail_len,
    cache,
    cache_len,
    prompt_states,
    prompt_len,
    in_gain,
    w_query,
    w_keyval,
    q_gain,
    k_gain,
    w_out,
    post_gain,
    ffn_gain,
    w_gate,
    w_up,
    w_down,
    final_gain,
):
    f32 = jnp.float32
    bf16 = jnp.bfloat16
    n_head = lax.axis_size("head")
    n_seq = seq_size()
    seq_at = lax.axis_index("seq")
    for level in LEVELS[::-1]:
        seq_at = seq_at * lax.axis_size(level) + lax.axis_index(level)
    head_at = lax.axis_index("head")
    flat_at = seq_at * n_head + head_at
    steps, groups, beams, width = step_tokens.shape
    pre = prompt_states.shape[0]
    repeat = QH // KVH
    rows = jnp.transpose(prompt_states, (1, 0, 2)).astype(f32)
    prompt_scaled = (rows * in_gain).astype(bf16).reshape(-1, width)
    prompt_squares = jnp.sum(rows * rows, -1).reshape(-1)
    prompt_terms = jnp.dot(
        prompt_scaled,
        lax.all_gather(w_keyval, SEQ, axis=1, tiled=True),
        preferred_element_type=f32,
    )
    prompt_sum, prompt_sq = (
        lax.psum_scatter(prompt_terms, "head", scatter_dimension=0, tiled=True),
        lax.psum_scatter(prompt_squares, "head", scatter_dimension=0, tiled=True),
    )
    prompt_pairs = finish_keys(prompt_sum * lax.rsqrt(prompt_sq / D + EPS)[:, None], k_gain)
    prompt_seg = prompt_pairs.shape[0] // pre
    prompt_pairs = jnp.transpose(prompt_pairs.reshape(prompt_seg, pre, -1), (1, 0, 2))
    prompt_ok = (flat_at * prompt_seg + jnp.arange(prompt_seg))[None, :] < prompt_len[:, None]
    cache_seg = cache.shape[1]
    cache_ok = (flat_at * cache_seg + jnp.arange(cache_seg))[None, :] < cache_len[:, None]
    span = max(prompt_seg, cache_seg)
    shared = jnp.concatenate(
        [
            jnp.pad(prompt_pairs, ((0, 0), (0, span - prompt_seg), (0, 0))),
            jnp.pad(cache, ((0, 0), (0, span - cache_seg), (0, 0))),
        ],
        0,
    )
    shared_ok = jnp.concatenate(
        [
            jnp.pad(prompt_ok, ((0, 0), (0, span - prompt_seg))),
            jnp.pad(cache_ok, ((0, 0), (0, span - cache_seg))),
        ],
        0,
    )
    shared_keys, shared_values = split_pairs(shared)
    tail_seg = tail_cache.shape[2]
    local_beams = tail_cache.shape[1]
    offset = (seq_at * tail_seg + jnp.arange(tail_seg))[None, :] - tail_len[:, None]
    all_beams = jnp.arange(beams)
    every_query, every_fresh = project_tokens(
        step_tokens, in_gain, w_query, w_keyval, q_gain, k_gain
    )
    every_query = every_query.reshape(steps, groups, beams, -1)
    every_fresh = every_fresh.reshape(steps, groups, beams, -1)
    everyone = lax.all_gather(tail_cache, "head", axis=1, tiled=True)
    n_dev = n_seq * n_head
    first_beam = head_at * local_beams
    many = steps * beams * repeat
    grouped = jnp.transpose(
        every_query.reshape(steps, groups, beams, KVH, repeat, HD), (1, 3, 0, 2, 4, 5)
    ).reshape(groups, KVH, many, HD)
    scores = jnp.einsum("gkmd,gtkd->gkmt", grouped, shared_keys, preferred_element_type=f32)
    scores = jnp.where(shared_ok[:, None, None, :], scores, NEG)
    top = jnp.max(scores, -1).reshape(groups, KVH, steps, beams, repeat)
    source = jnp.broadcast_to(all_beams[None, :], (groups, beams))
    ancestors = []
    tail_parts = []
    tail_tops = []
    for step in range(steps):
        link = parents[step]
        source = jnp.take_along_axis(source, link, axis=1)
        ancestors = [jnp.take_along_axis(a, link, axis=1) for a in ancestors]
        ancestors.append(jnp.broadcast_to(all_beams[None, :], (groups, beams)))
        picks = lax.dynamic_slice_in_dim(source, first_beam, local_beams, 1)
        tail_state = jnp.take_along_axis(everyone, picks[:, :, None, None], axis=1)
        for back, anc in enumerate(ancestors):
            mine = lax.dynamic_slice_in_dim(anc, first_beam, local_beams, 1)
            written = jnp.take_along_axis(every_fresh[back], mine[:, :, None], axis=1)
            tail_state = jnp.where(
                (offset == back)[:, None, :, None], written[:, :, None, :], tail_state
            )
        tail_keys, tail_values = split_pairs(tail_state)
        local_query = lax.dynamic_slice_in_dim(every_query[step], first_beam, local_beams, 1)
        local_query = local_query.reshape(groups, local_beams, KVH, repeat, HD)
        tail_scores = jnp.einsum(
            "gckrd,gctkd->gckrt", local_query, tail_keys, preferred_element_type=f32
        )
        tail_ok = (offset <= step)[:, None, None, None, :]
        tail_scores = jnp.where(tail_ok, tail_scores, NEG)
        tail_parts.append((tail_scores, tail_ok, tail_values))
        tail_top = lax.dynamic_update_slice(
            jnp.full((groups, beams, KVH, repeat), NEG, f32),
            jnp.max(tail_scores, -1),
            (0, first_beam, 0, 0),
        )
        tail_tops.append(jnp.transpose(tail_top, (0, 2, 1, 3)))
    top = jnp.maximum(top, jnp.stack(tail_tops, 2))
    top = exchange_max(top, ALL, n_dev)
    weights = jnp.where(
        shared_ok[:, None, None, :], jnp.exp(scores - top.reshape(groups, KVH, many)[..., None]), 0.0
    )
    total = jnp.sum(weights, -1).reshape(groups, KVH, steps, beams, repeat)
    weighted = jnp.einsum(
        "gkmt,gtkd->gkmd", weights.astype(bf16), shared_values, preferred_element_type=f32
    ).reshape(groups, KVH, steps, beams, repeat, HD)
    tail_totals, tail_weighted = [], []
    for step in range(steps):
        tail_scores, tail_ok, tail_values = tail_parts[step]
        local_top = lax.dynamic_slice_in_dim(top[:, :, step], first_beam, local_beams, 2)
        local_top = jnp.transpose(local_top, (0, 2, 1, 3))
        tail_weights = jnp.where(tail_ok, jnp.exp(tail_scores - local_top[..., None]), 0.0)
        tail_total = lax.dynamic_update_slice(
            jnp.zeros((groups, beams, KVH, repeat), f32),
            jnp.sum(tail_weights, -1),
            (0, first_beam, 0, 0),
        )
        tail_sum = lax.dynamic_update_slice(
            jnp.zeros((groups, beams, KVH, repeat, HD), f32),
            jnp.einsum(
                "gckrt,gctkd->gckrd",
                tail_weights.astype(bf16),
                tail_values,
                preferred_element_type=f32,
            ),
            (0, first_beam, 0, 0, 0),
        )
        tail_totals.append(jnp.transpose(tail_total, (0, 2, 1, 3)))
        tail_weighted.append(jnp.transpose(tail_sum, (0, 2, 1, 3, 4)))
    total = total + jnp.stack(tail_totals, 2)
    weighted = weighted + jnp.stack(tail_weighted, 2)
    rows = steps * groups * beams
    piece = QD // n_dev
    per_head = HD // piece
    weighted = jnp.transpose(
        weighted.reshape(groups, KVH, steps, beams, repeat, per_head, piece), (1, 4, 5, 2, 0, 3, 6)
    ).reshape(n_dev, -1)
    total = jnp.repeat(jnp.transpose(total, (1, 4, 2, 0, 3)).reshape(QH, rows), per_head, 0)
    lanes = -(-rows // 128) * 128
    packed = jnp.concatenate([weighted, jnp.pad(total, ((0, 0), (0, lanes - rows)))], 1)
    for level in LEVELS:
        packed = packed.reshape(-1, lax.axis_size(level), n_head, packed.shape[-1])
        packed = exchange_sum(jnp.swapaxes(packed, 0, 1), level).reshape(-1, packed.shape[-1])
    packed = exchange_sum(packed, ("seq", "head"))
    share = packed[: rows * piece].reshape(rows, piece)
    own_total = packed[rows * piece : rows * piece + rows]
    attn = (share / own_total[:, None]).astype(bf16)
    attn = exchange_gather(attn, "head", n_head)
    attn = jnp.transpose(attn, (1, 0, 2)).reshape(rows, -1)
    partial_out = jnp.dot(attn, w_out, preferred_element_type=f32)
    per_dev = rows // n_seq
    out_proj = seq_sum(partial_out.reshape(n_seq, per_dev, -1))
    out_sq = lax.psum(jnp.sum(out_proj * out_proj, -1), "head")
    x_all = step_tokens.reshape(rows, -1)
    x_f = lax.dynamic_slice_in_dim(x_all, seq_at * per_dev, per_dev, 0).astype(f32)
    state = (x_f + out_proj * lax.rsqrt(out_sq / D + EPS)[:, None] * post_gain).astype(bf16)
    state_all = seq_gather(state).reshape(rows, -1)
    state_f = state_all.astype(f32)
    scaled_two = (state_f * ffn_gain).astype(bf16)
    gate_part = jnp.dot(scaled_two, w_gate, preferred_element_type=f32)
    up_part = jnp.dot(scaled_two, w_up, preferred_element_type=f32)
    hidden = gate_part.shape[1]
    head_rows = rows // n_head
    packed = jnp.concatenate(
        [gate_part, up_part, jnp.pad(jnp.sum(state_f * state_f, -1)[:, None], ((0, 0), (0, 127)))],
        1,
    )
    packed = exchange_sum(packed.reshape(n_head, head_rows, -1), "head")
    norm_s = lax.rsqrt(packed[:, 2 * hidden] / D + EPS)[:, None]
    inner = (
        jax.nn.gelu(packed[:, :hidden] * norm_s, approximate=True)
        * (packed[:, hidden : 2 * hidden] * norm_s)
    ).astype(bf16)
    inner = exchange_gather(inner, "head", n_head).reshape(rows, hidden)
    ffn_out = seq_sum(jnp.dot(inner, w_down, preferred_element_type=f32).reshape(n_seq, per_dev, -1))
    ffn_sq = lax.psum(jnp.sum(ffn_out * ffn_out, -1), "head")
    result = (
        state.astype(f32) + ffn_out * lax.rsqrt(ffn_sq / D + EPS)[:, None] * final_gain
    ).astype(bf16)
    result = seq_gather(result)
    return result.reshape(steps, groups, beams, -1)


def solution(mesh):
    devices = mesh.devices
    fine = jax.sharding.Mesh(
        devices.reshape(devices.shape[0] // 4, 2, 2, devices.shape[1]), ALL
    )
    return jax.shard_map(
        shards,
        mesh=fine,
        in_specs=(
            P(None, None, None, "head"),
            P(),
            P(None, "head", SEQ, None),
            P(),
            P(None, ALL, None),
            P(),
            P(None, SEQ, "head"),
            P(),
            P("head"),
            P("head", SEQ),
            P("head", SEQ),
            P(),
            P(),
            P(SEQ, "head"),
            P("head"),
            P("head"),
            P("head", SEQ),
            P("head", SEQ),
            P(SEQ, "head"),
            P("head"),
        ),
        out_specs=P(None, None, None, "head"),
        check_vma=False,
    )
```

```python
import jax
import jax.numpy as jnp
from jax import lax
from jax.sharding import PartitionSpec as P

D = 2560
QH = 8
KVH = 4
HD = 256
QD = 2048


SEQ = ("seq", "pair")
ALL = ("seq", "pair", "head")

EPS = 1e-06
NEG = -1e30
QSCALE = 0.0625


def norm_heads(values, gain, scale):
    shaped = values.reshape(values.shape[:-1] + (-1, gain.shape[0]))
    shaped = shaped * lax.rsqrt(jnp.mean(shaped * shaped, -1, keepdims=True) + EPS) * gain * scale
    return shaped.reshape(values.shape)


def finish_keys(pairs, k_gain):
    half = pairs.shape[-1] // 2
    keys = norm_heads(pairs[..., :half], k_gain, 1.0)
    return jnp.concatenate([keys, pairs[..., half:]], -1).astype(jnp.bfloat16)


def split_pairs(pairs):
    half = pairs.shape[-1] // 2
    keys = pairs[..., :half].reshape(pairs.shape[:-1] + (KVH, HD))
    values = pairs[..., half:].reshape(pairs.shape[:-1] + (KVH, HD))
    return (keys, values)


def exchange_sum(parts, axes, narrow=False):
    if narrow:
        moved = lax.all_to_all(parts.astype(jnp.bfloat16), axes, 0, 0, tiled=True)
        return jnp.sum(moved.astype(jnp.float32), 0)
    return jnp.sum(lax.all_to_all(parts, axes, 0, 0, tiled=True), 0)


def exchange_max(value, axes, count):
    spread = jnp.broadcast_to(value[None], (count,) + value.shape)
    return jnp.max(lax.all_to_all(spread, axes, 0, 0, tiled=True), 0)


def exchange_gather(piece, axes, count):
    spread = jnp.broadcast_to(piece[None], (count,) + piece.shape)
    return lax.all_to_all(spread, axes, 0, 0, tiled=True)


def seq_sum(parts):
    pair = lax.axis_size("pair")
    parts = parts.reshape((parts.shape[0] // pair, pair) + parts.shape[1:])
    parts = exchange_sum(jnp.swapaxes(parts, 0, 1), "pair")
    return exchange_sum(parts, "seq")


def seq_gather(piece):
    pair = lax.axis_size("pair")
    outer = lax.axis_size("seq")
    got = exchange_gather(exchange_gather(piece, "seq", outer), "pair", pair)
    return jnp.swapaxes(got, 0, 1).reshape((outer * pair,) + piece.shape)


def project_tokens(tokens, in_gain, w_query, w_keyval, q_gain, k_gain):
    flat = tokens.reshape(-1, tokens.shape[-1]).astype(jnp.float32)
    scaled = (flat * in_gain).astype(jnp.bfloat16)
    q_part = jnp.dot(scaled, w_query, preferred_element_type=jnp.float32)
    kv_part = jnp.dot(scaled, w_keyval, preferred_element_type=jnp.float32)
    squares = jnp.sum(flat * flat, -1)
    n_head = lax.axis_size("head")
    n_seq = lax.axis_size("seq") * lax.axis_size("pair")
    rows = flat.shape[0]
    half = rows // n_head
    block = q_part.shape[1]
    packed = jnp.concatenate([q_part, kv_part, jnp.pad(squares[:, None], ((0, 0), (0, 127)))], 1)
    packed = exchange_sum(packed.reshape(n_head, half, -1), "head")
    factor = lax.rsqrt(packed[:, 2 * block] / D + EPS)[:, None]
    q_raw = (packed[:, :block] * factor).astype(jnp.bfloat16)
    kv_raw = (packed[:, block : 2 * block] * factor).astype(jnp.bfloat16)
    both = exchange_gather(
        jnp.concatenate([q_raw, kv_raw], 1), ALL, n_seq * n_head
    ).reshape(n_seq, n_head, half, 2 * block)
    both = jnp.transpose(both, (1, 2, 0, 3)).reshape(rows, n_seq, 2 * block)
    q_raw = both[:, :, :block].reshape(rows, -1)
    kv_raw = both[:, :, block:].reshape(rows, -1)
    queries = norm_heads(q_raw.astype(jnp.float32), q_gain, QSCALE).astype(jnp.bfloat16)
    fresh = finish_keys(kv_raw.astype(jnp.float32), k_gain)
    return (queries, fresh)


def shards(
    step_tokens,
    parents,
    tail_cache,
    tail_len,
    cache,
    cache_len,
    prompt_states,
    prompt_len,
    in_gain,
    w_query,
    w_keyval,
    q_gain,
    k_gain,
    w_out,
    post_gain,
    ffn_gain,
    w_gate,
    w_up,
    w_down,
    final_gain,
):
    f32 = jnp.float32
    bf16 = jnp.bfloat16
    n_head = lax.axis_size("head")
    n_seq = lax.axis_size("seq") * lax.axis_size("pair")
    seq_at = lax.axis_index("seq") * lax.axis_size("pair") + lax.axis_index("pair")
    head_at = lax.axis_index("head")
    flat_at = seq_at * n_head + head_at
    steps, groups, beams, width = step_tokens.shape
    pre = prompt_states.shape[0]
    repeat = QH // KVH
    owners = n_seq * n_head
    prompt_all = lax.all_gather(prompt_states, SEQ, axis=1, tiled=True).astype(f32)
    prompt_seg = prompt_all.shape[1] // owners
    prompt_scaled = (prompt_all * in_gain).astype(bf16).reshape(-1, width)
    prompt_terms = jnp.dot(prompt_scaled, w_keyval, preferred_element_type=f32)
    kv_cols = prompt_terms.shape[1]
    prompt_terms = jnp.transpose(
        prompt_terms.reshape(pre, owners, prompt_seg, kv_cols), (1, 0, 2, 3)
    ).reshape(owners, -1)
    prompt_squares = jnp.transpose(
        jnp.sum(prompt_all * prompt_all, -1).reshape(pre, owners, prompt_seg), (1, 0, 2)
    ).reshape(owners, -1)
    own_rows = pre * prompt_seg
    pad_rows = -(-own_rows // 128) * 128
    prompt_terms = jnp.concatenate(
        [prompt_terms, jnp.pad(prompt_squares, ((0, 0), (0, pad_rows - own_rows)))], 1
    )
    prompt_terms = lax.all_to_all(prompt_terms, ALL, 0, 0, tiled=True)
    prompt_terms = jnp.sum(prompt_terms.reshape(n_seq, n_head, -1), 1)
    prompt_sq = prompt_terms[0, own_rows * kv_cols : own_rows * kv_cols + own_rows]
    prompt_sum = jnp.transpose(
        prompt_terms[:, : own_rows * kv_cols].reshape(n_seq, own_rows, kv_cols), (1, 0, 2)
    ).reshape(own_rows, -1)
    prompt_pairs = finish_keys(prompt_sum * lax.rsqrt(prompt_sq / D + EPS)[:, None], k_gain)
    prompt_pairs = prompt_pairs.reshape(pre, prompt_seg, -1)
    prompt_ok = (flat_at * prompt_seg + jnp.arange(prompt_seg))[None, :] < prompt_len[:, None]
    cache_seg = cache.shape[1]
    cache_ok = (flat_at * cache_seg + jnp.arange(cache_seg))[None, :] < cache_len[:, None]
    span = max(prompt_seg, cache_seg)
    shared = jnp.concatenate(
        [
            jnp.pad(prompt_pairs, ((0, 0), (0, span - prompt_seg), (0, 0))),
            jnp.pad(cache, ((0, 0), (0, span - cache_seg), (0, 0))),
        ],
        0,
    )
    shared_ok = jnp.concatenate(
        [
            jnp.pad(prompt_ok, ((0, 0), (0, span - prompt_seg))),
            jnp.pad(cache_ok, ((0, 0), (0, span - cache_seg))),
        ],
        0,
    )
    shared_keys, shared_values = split_pairs(shared)
    tail_seg = tail_cache.shape[2]
    local_beams = tail_cache.shape[1]
    offset = (seq_at * tail_seg + jnp.arange(tail_seg))[None, :] - tail_len[:, None]
    all_beams = jnp.arange(beams)
    every_query, every_fresh = project_tokens(
        step_tokens, in_gain, w_query, w_keyval, q_gain, k_gain
    )
    every_query = every_query.reshape(steps, groups, beams, -1)
    every_fresh = every_fresh.reshape(steps, groups, beams, -1)
    everyone = lax.all_gather(tail_cache, "head", axis=1, tiled=True)
    n_dev = n_seq * n_head
    first_beam = head_at * local_beams
    many = steps * beams * repeat
    grouped = jnp.transpose(
        every_query.reshape(steps, groups, beams, KVH, repeat, HD), (1, 3, 0, 2, 4, 5)
    ).reshape(groups, KVH, many, HD)
    scores = jnp.einsum("gkmd,gtkd->gkmt", grouped, shared_keys, preferred_element_type=f32)
    scores = jnp.where(shared_ok[:, None, None, :], scores, NEG)
    top = jnp.max(scores, -1).reshape(groups, KVH, steps, beams, repeat)
    source = jnp.broadcast_to(all_beams[None, :], (groups, beams))
    ancestors = []
    tail_parts = []
    tail_tops = []
    for step in range(steps):
        link = parents[step]
        source = jnp.take_along_axis(source, link, axis=1)
        ancestors = [jnp.take_along_axis(a, link, axis=1) for a in ancestors]
        ancestors.append(jnp.broadcast_to(all_beams[None, :], (groups, beams)))
        picks = lax.dynamic_slice_in_dim(source, first_beam, local_beams, 1)
        tail_state = jnp.take_along_axis(everyone, picks[:, :, None, None], axis=1)
        for back, anc in enumerate(ancestors):
            mine = lax.dynamic_slice_in_dim(anc, first_beam, local_beams, 1)
            written = jnp.take_along_axis(every_fresh[back], mine[:, :, None], axis=1)
            tail_state = jnp.where(
                (offset == back)[:, None, :, None], written[:, :, None, :], tail_state
            )
        tail_keys, tail_values = split_pairs(tail_state)
        local_query = lax.dynamic_slice_in_dim(every_query[step], first_beam, local_beams, 1)
        local_query = local_query.reshape(groups, local_beams, KVH, repeat, HD)
        tail_scores = jnp.einsum(
            "gckrd,gctkd->gckrt", local_query, tail_keys, preferred_element_type=f32
        )
        tail_ok = (offset <= step)[:, None, None, None, :]
        tail_scores = jnp.where(tail_ok, tail_scores, NEG)
        tail_parts.append((tail_scores, tail_ok, tail_values))
        tail_top = lax.dynamic_update_slice(
            jnp.full((groups, beams, KVH, repeat), NEG, f32),
            jnp.max(tail_scores, -1),
            (0, first_beam, 0, 0),
        )
        tail_tops.append(jnp.transpose(tail_top, (0, 2, 1, 3)))
    top = jnp.maximum(top, jnp.stack(tail_tops, 2))
    top = exchange_max(top, ALL, n_dev)
    weights = jnp.where(
        shared_ok[:, None, None, :], jnp.exp(scores - top.reshape(groups, KVH, many)[..., None]), 0.0
    )
    total = jnp.sum(weights, -1).reshape(groups, KVH, steps, beams, repeat)
    weighted = jnp.einsum(
        "gkmt,gtkd->gkmd", weights.astype(bf16), shared_values, preferred_element_type=f32
    ).reshape(groups, KVH, steps, beams, repeat, HD)
    tail_totals, tail_weighted = [], []
    for step in range(steps):
        tail_scores, tail_ok, tail_values = tail_parts[step]
        local_top = lax.dynamic_slice_in_dim(top[:, :, step], first_beam, local_beams, 2)
        local_top = jnp.transpose(local_top, (0, 2, 1, 3))
        tail_weights = jnp.where(tail_ok, jnp.exp(tail_scores - local_top[..., None]), 0.0)
        tail_total = lax.dynamic_update_slice(
            jnp.zeros((groups, beams, KVH, repeat), f32),
            jnp.sum(tail_weights, -1),
            (0, first_beam, 0, 0),
        )
        tail_sum = lax.dynamic_update_slice(
            jnp.zeros((groups, beams, KVH, repeat, HD), f32),
            jnp.einsum(
                "gckrt,gctkd->gckrd",
                tail_weights.astype(bf16),
                tail_values,
                preferred_element_type=f32,
            ),
            (0, first_beam, 0, 0, 0),
        )
        tail_totals.append(jnp.transpose(tail_total, (0, 2, 1, 3)))
        tail_weighted.append(jnp.transpose(tail_sum, (0, 2, 1, 3, 4)))
    total = total + jnp.stack(tail_totals, 2)
    weighted = weighted + jnp.stack(tail_weighted, 2)
    rows = steps * groups * beams
    piece = QD // n_dev
    per_head = HD // piece
    weighted = jnp.transpose(
        weighted.reshape(groups, KVH, steps, beams, repeat, per_head, piece), (1, 4, 5, 2, 0, 3, 6)
    ).reshape(n_dev, -1)
    total = jnp.repeat(jnp.transpose(total, (1, 4, 2, 0, 3)).reshape(QH, rows), per_head, 0)
    lanes = -(-rows // 128) * 128
    packed = jnp.concatenate([weighted, jnp.pad(total, ((0, 0), (0, lanes - rows)))], 1)
    pair = lax.axis_size("pair")
    packed = packed.reshape(n_seq // pair, pair, n_head, -1)
    packed = exchange_sum(jnp.swapaxes(packed, 0, 1), "pair").reshape(n_dev // pair, -1)
    packed = exchange_sum(packed, ("seq", "head"))
    share = packed[: rows * piece].reshape(rows, piece)
    own_total = packed[rows * piece : rows * piece + rows]
    attn = (share / own_total[:, None]).astype(bf16)
    attn = exchange_gather(attn, "head", n_head)
    attn = jnp.transpose(attn, (1, 0, 2)).reshape(rows, -1)
    partial_out = jnp.dot(attn, w_out, preferred_element_type=f32)
    per_dev = rows // n_seq
    out_proj = seq_sum(partial_out.reshape(n_seq, per_dev, -1))
    out_sq = lax.psum(jnp.sum(out_proj * out_proj, -1), "head")
    x_all = step_tokens.reshape(rows, -1)
    x_f = lax.dynamic_slice_in_dim(x_all, seq_at * per_dev, per_dev, 0).astype(f32)
    state = (x_f + out_proj * lax.rsqrt(out_sq / D + EPS)[:, None] * post_gain).astype(bf16)
    state_all = seq_gather(state).reshape(rows, -1)
    state_f = state_all.astype(f32)
    scaled_two = (state_f * ffn_gain).astype(bf16)
    gate_part = jnp.dot(scaled_two, w_gate, preferred_element_type=f32)
    up_part = jnp.dot(scaled_two, w_up, preferred_element_type=f32)
    hidden = gate_part.shape[1]
    head_rows = rows // n_head
    packed = jnp.concatenate(
        [gate_part, up_part, jnp.pad(jnp.sum(state_f * state_f, -1)[:, None], ((0, 0), (0, 127)))],
        1,
    )
    packed = exchange_sum(packed.reshape(n_head, head_rows, -1), "head")
    norm_s = lax.rsqrt(packed[:, 2 * hidden] / D + EPS)[:, None]
    inner = (
        jax.nn.gelu(packed[:, :hidden] * norm_s, approximate=True)
        * (packed[:, hidden : 2 * hidden] * norm_s)
    ).astype(bf16)
    inner = exchange_gather(inner, "head", n_head).reshape(rows, hidden)
    ffn_out = seq_sum(jnp.dot(inner, w_down, preferred_element_type=f32).reshape(n_seq, per_dev, -1))
    ffn_sq = lax.psum(jnp.sum(ffn_out * ffn_out, -1), "head")
    result = (
        state.astype(f32) + ffn_out * lax.rsqrt(ffn_sq / D + EPS)[:, None] * final_gain
    ).astype(bf16)
    result = seq_gather(result)
    return result.reshape(steps, groups, beams, -1)


def solution(mesh):
    devices = mesh.devices
    fine = jax.sharding.Mesh(
        devices.reshape(devices.shape[0] // 2, 2, devices.shape[1]), ("seq", "pair", "head")
    )
    return jax.shard_map(
        shards,
        mesh=fine,
        in_specs=(
            P(None, None, None, "head"),
            P(),
            P(None, "head", SEQ, None),
            P(),
            P(None, ALL, None),
            P(),
            P(None, SEQ, "head"),
            P(),
            P("head"),
            P("head", SEQ),
            P("head", SEQ),
            P(),
            P(),
            P(SEQ, "head"),
            P("head"),
            P("head"),
            P("head", SEQ),
            P("head", SEQ),
            P(SEQ, "head"),
            P("head"),
        ),
        out_specs=P(None, None, None, "head"),
        check_vma=False,
    )
```

```python
import jax
import jax.numpy as jnp
from jax import lax
from jax.sharding import PartitionSpec as P

D = 2560
QH = 8
KVH = 4
HD = 256
QD = 2048


SEQ = ("seq", "pair")
ALL = ("seq", "pair", "head")

EPS = 1e-06
NEG = -1e30
QSCALE = 0.0625


def norm_heads(values, gain, scale):
    shaped = values.reshape(values.shape[:-1] + (-1, gain.shape[0]))
    shaped = shaped * lax.rsqrt(jnp.mean(shaped * shaped, -1, keepdims=True) + EPS) * gain * scale
    return shaped.reshape(values.shape)


def finish_keys(pairs, k_gain):
    half = pairs.shape[-1] // 2
    keys = norm_heads(pairs[..., :half], k_gain, 1.0)
    return jnp.concatenate([keys, pairs[..., half:]], -1).astype(jnp.bfloat16)


def split_pairs(pairs):
    half = pairs.shape[-1] // 2
    keys = pairs[..., :half].reshape(pairs.shape[:-1] + (KVH, HD))
    values = pairs[..., half:].reshape(pairs.shape[:-1] + (KVH, HD))
    return (keys, values)


def exchange_sum(parts, axes, narrow=False):
    if narrow:
        moved = lax.all_to_all(parts.astype(jnp.bfloat16), axes, 0, 0, tiled=True)
        return jnp.sum(moved.astype(jnp.float32), 0)
    return jnp.sum(lax.all_to_all(parts, axes, 0, 0, tiled=True), 0)


def exchange_max(value, axes, count):
    spread = jnp.broadcast_to(value[None], (count,) + value.shape)
    return jnp.max(lax.all_to_all(spread, axes, 0, 0, tiled=True), 0)


def exchange_gather(piece, axes, count):
    spread = jnp.broadcast_to(piece[None], (count,) + piece.shape)
    return lax.all_to_all(spread, axes, 0, 0, tiled=True)


def seq_sum(parts):
    pair = lax.axis_size("pair")
    parts = parts.reshape((parts.shape[0] // pair, pair) + parts.shape[1:])
    parts = exchange_sum(jnp.swapaxes(parts, 0, 1), "pair")
    return exchange_sum(parts, "seq")


def seq_gather(piece):
    pair = lax.axis_size("pair")
    outer = lax.axis_size("seq")
    got = exchange_gather(exchange_gather(piece, "seq", outer), "pair", pair)
    return jnp.swapaxes(got, 0, 1).reshape((outer * pair,) + piece.shape)


def project_tokens(tokens, in_gain, w_query, w_keyval, q_gain, k_gain):
    flat = tokens.reshape(-1, tokens.shape[-1]).astype(jnp.float32)
    scaled = (flat * in_gain).astype(jnp.bfloat16)
    q_part = jnp.dot(scaled, w_query, preferred_element_type=jnp.float32)
    kv_part = jnp.dot(scaled, w_keyval, preferred_element_type=jnp.float32)
    squares = jnp.sum(flat * flat, -1)
    n_head = lax.axis_size("head")
    n_seq = lax.axis_size("seq") * lax.axis_size("pair")
    rows = flat.shape[0]
    half = rows // n_head
    block = q_part.shape[1]
    packed = jnp.concatenate([q_part, kv_part, jnp.pad(squares[:, None], ((0, 0), (0, 127)))], 1)
    packed = exchange_sum(packed.reshape(n_head, half, -1), "head")
    factor = lax.rsqrt(packed[:, 2 * block] / D + EPS)[:, None]
    q_raw = (packed[:, :block] * factor).astype(jnp.bfloat16)
    kv_raw = (packed[:, block : 2 * block] * factor).astype(jnp.bfloat16)
    both = exchange_gather(
        jnp.concatenate([q_raw, kv_raw], 1), ALL, n_seq * n_head
    ).reshape(n_seq, n_head, half, 2 * block)
    both = jnp.transpose(both, (1, 2, 0, 3)).reshape(rows, n_seq, 2 * block)
    q_raw = both[:, :, :block].reshape(rows, -1)
    kv_raw = both[:, :, block:].reshape(rows, -1)
    queries = norm_heads(q_raw.astype(jnp.float32), q_gain, QSCALE).astype(jnp.bfloat16)
    fresh = finish_keys(kv_raw.astype(jnp.float32), k_gain)
    return (queries, fresh)


def shards(
    step_tokens,
    parents,
    tail_cache,
    tail_len,
    cache,
    cache_len,
    prompt_states,
    prompt_len,
    in_gain,
    w_query,
    w_keyval,
    q_gain,
    k_gain,
    w_out,
    post_gain,
    ffn_gain,
    w_gate,
    w_up,
    w_down,
    final_gain,
):
    f32 = jnp.float32
    bf16 = jnp.bfloat16
    n_head = lax.axis_size("head")
    n_seq = lax.axis_size("seq") * lax.axis_size("pair")
    seq_at = lax.axis_index("seq") * lax.axis_size("pair") + lax.axis_index("pair")
    head_at = lax.axis_index("head")
    flat_at = seq_at * n_head + head_at
    steps, groups, beams, width = step_tokens.shape
    pre = prompt_states.shape[0]
    repeat = QH // KVH
    rows = jnp.transpose(prompt_states, (1, 0, 2)).astype(f32)
    prompt_scaled = (rows * in_gain).astype(bf16).reshape(-1, width)
    prompt_squares = jnp.sum(rows * rows, -1).reshape(-1)
    prompt_terms = jnp.dot(
        prompt_scaled,
        lax.all_gather(w_keyval, SEQ, axis=1, tiled=True),
        preferred_element_type=f32,
    )
    prompt_sum, prompt_sq = (
        lax.psum_scatter(prompt_terms, "head", scatter_dimension=0, tiled=True),
        lax.psum_scatter(prompt_squares, "head", scatter_dimension=0, tiled=True),
    )
    prompt_pairs = finish_keys(prompt_sum * lax.rsqrt(prompt_sq / D + EPS)[:, None], k_gain)
    prompt_seg = prompt_pairs.shape[0] // pre
    prompt_pairs = jnp.transpose(prompt_pairs.reshape(prompt_seg, pre, -1), (1, 0, 2))
    prompt_ok = (flat_at * prompt_seg + jnp.arange(prompt_seg))[None, :] < prompt_len[:, None]
    cache_seg = cache.shape[1]
    cache_ok = (flat_at * cache_seg + jnp.arange(cache_seg))[None, :] < cache_len[:, None]
    span = max(prompt_seg, cache_seg)
    shared = jnp.concatenate(
        [
            jnp.pad(prompt_pairs, ((0, 0), (0, span - prompt_seg), (0, 0))),
            jnp.pad(cache, ((0, 0), (0, span - cache_seg), (0, 0))),
        ],
        0,
    )
    shared_ok = jnp.concatenate(
        [
            jnp.pad(prompt_ok, ((0, 0), (0, span - prompt_seg))),
            jnp.pad(cache_ok, ((0, 0), (0, span - cache_seg))),
        ],
        0,
    )
    shared_keys, shared_values = split_pairs(shared)
    tail_seg = tail_cache.shape[2]
    local_beams = tail_cache.shape[1]
    offset = (seq_at * tail_seg + jnp.arange(tail_seg))[None, :] - tail_len[:, None]
    all_beams = jnp.arange(beams)
    every_query, every_fresh = project_tokens(
        step_tokens, in_gain, w_query, w_keyval, q_gain, k_gain
    )
    every_query = every_query.reshape(steps, groups, beams, -1)
    every_fresh = every_fresh.reshape(steps, groups, beams, -1)
    everyone = lax.all_gather(tail_cache, "head", axis=1, tiled=True)
    n_dev = n_seq * n_head
    first_beam = head_at * local_beams
    many = steps * beams * repeat
    grouped = jnp.transpose(
        every_query.reshape(steps, groups, beams, KVH, repeat, HD), (1, 3, 0, 2, 4, 5)
    ).reshape(groups, KVH, many, HD)
    source = jnp.broadcast_to(all_beams[None, :], (groups, beams))
    ancestors = []
    tail_states = []
    for step in range(steps):
        link = parents[step]
        source = jnp.take_along_axis(source, link, axis=1)
        ancestors = [jnp.take_along_axis(a, link, axis=1) for a in ancestors]
        ancestors.append(jnp.broadcast_to(all_beams[None, :], (groups, beams)))
        picks = lax.dynamic_slice_in_dim(source, first_beam, local_beams, 1)
        tail_state = jnp.take_along_axis(everyone, picks[:, :, None, None], axis=1)
        for back, anc in enumerate(ancestors):
            mine = lax.dynamic_slice_in_dim(anc, first_beam, local_beams, 1)
            written = jnp.take_along_axis(every_fresh[back], mine[:, :, None], axis=1)
            tail_state = jnp.where(
                (offset == back)[:, None, :, None], written[:, :, None, :], tail_state
            )
        tail_states.append(tail_state)
    tails = jnp.stack(tail_states, 1).reshape(groups, steps * local_beams * tail_seg, -1)
    all_keys, all_values = split_pairs(jnp.concatenate([shared, tails], 1))
    step_id = jnp.arange(steps)
    same_step = step_id[:, None, None, None, None, None] == step_id[None, None, None, :, None, None]
    same_beam = (
        all_beams[None, :, None, None, None, None]
        == (first_beam + jnp.arange(local_beams))[None, None, None, None, :, None]
    )
    live = offset[:, None, None, None, None, None, :] <= step_id[None, None, None, None, :, None, None]
    tail_mask = jnp.broadcast_to(
        (same_step & same_beam)[None] & live,
        (groups, steps, beams, repeat, steps, local_beams, tail_seg),
    ).reshape(groups, many, -1)
    mask = jnp.concatenate(
        [jnp.broadcast_to(shared_ok[:, None, :], (groups, many, span)), tail_mask], -1
    )[:, None]
    scores = jnp.einsum("gkmd,gtkd->gkmt", grouped, all_keys, preferred_element_type=f32)
    scores = jnp.where(mask, scores, NEG)
    top = jnp.max(scores, -1).reshape(groups, KVH, steps, beams, repeat)
    top = exchange_max(top, ALL, n_dev)
    weights = jnp.where(mask, jnp.exp(scores - top.reshape(groups, KVH, many)[..., None]), 0.0)
    total = jnp.sum(weights, -1).reshape(groups, KVH, steps, beams, repeat)
    weighted = jnp.einsum(
        "gkmt,gtkd->gkmd", weights.astype(bf16), all_values, preferred_element_type=f32
    ).reshape(groups, KVH, steps, beams, repeat, HD)
    rows = steps * groups * beams
    piece = QD // n_dev
    per_head = HD // piece
    weighted = jnp.transpose(
        weighted.reshape(groups, KVH, steps, beams, repeat, per_head, piece), (1, 4, 5, 2, 0, 3, 6)
    ).reshape(n_dev, -1)
    total = jnp.repeat(jnp.transpose(total, (1, 4, 2, 0, 3)).reshape(QH, rows), per_head, 0)
    lanes = -(-rows // 128) * 128
    packed = jnp.concatenate([weighted, jnp.pad(total, ((0, 0), (0, lanes - rows)))], 1)
    pair = lax.axis_size("pair")
    packed = packed.reshape(n_seq // pair, pair, n_head, -1)
    packed = exchange_sum(jnp.swapaxes(packed, 0, 1), "pair").reshape(n_dev // pair, -1)
    packed = exchange_sum(packed, ("seq", "head"))
    share = packed[: rows * piece].reshape(rows, piece)
    own_total = packed[rows * piece : rows * piece + rows]
    attn = (share / own_total[:, None]).astype(bf16)
    attn = exchange_gather(attn, "head", n_head)
    attn = jnp.transpose(attn, (1, 0, 2)).reshape(rows, -1)
    partial_out = jnp.dot(attn, w_out, preferred_element_type=f32)
    per_dev = rows // n_seq
    out_proj = seq_sum(partial_out.reshape(n_seq, per_dev, -1))
    out_sq = lax.psum(jnp.sum(out_proj * out_proj, -1), "head")
    x_all = step_tokens.reshape(rows, -1)
    x_f = lax.dynamic_slice_in_dim(x_all, seq_at * per_dev, per_dev, 0).astype(f32)
    state = (x_f + out_proj * lax.rsqrt(out_sq / D + EPS)[:, None] * post_gain).astype(bf16)
    state_all = seq_gather(state).reshape(rows, -1)
    state_f = state_all.astype(f32)
    scaled_two = (state_f * ffn_gain).astype(bf16)
    gate_part = jnp.dot(scaled_two, w_gate, preferred_element_type=f32)
    up_part = jnp.dot(scaled_two, w_up, preferred_element_type=f32)
    hidden = gate_part.shape[1]
    head_rows = rows // n_head
    packed = jnp.concatenate(
        [gate_part, up_part, jnp.pad(jnp.sum(state_f * state_f, -1)[:, None], ((0, 0), (0, 127)))],
        1,
    )
    packed = exchange_sum(packed.reshape(n_head, head_rows, -1), "head")
    norm_s = lax.rsqrt(packed[:, 2 * hidden] / D + EPS)[:, None]
    inner = (
        jax.nn.gelu(packed[:, :hidden] * norm_s, approximate=True)
        * (packed[:, hidden : 2 * hidden] * norm_s)
    ).astype(bf16)
    inner = exchange_gather(inner, "head", n_head).reshape(rows, hidden)
    ffn_out = seq_sum(jnp.dot(inner, w_down, preferred_element_type=f32).reshape(n_seq, per_dev, -1))
    ffn_sq = lax.psum(jnp.sum(ffn_out * ffn_out, -1), "head")
    result = (
        state.astype(f32) + ffn_out * lax.rsqrt(ffn_sq / D + EPS)[:, None] * final_gain
    ).astype(bf16)
    result = seq_gather(result)
    return result.reshape(steps, groups, beams, -1)


def solution(mesh):
    devices = mesh.devices
    fine = jax.sharding.Mesh(
        devices.reshape(devices.shape[0] // 2, 2, devices.shape[1]), ("seq", "pair", "head")
    )
    return jax.shard_map(
        shards,
        mesh=fine,
        in_specs=(
            P(None, None, None, "head"),
            P(),
            P(None, "head", SEQ, None),
            P(),
            P(None, ALL, None),
            P(),
            P(None, SEQ, "head"),
            P(),
            P("head"),
            P("head", SEQ),
            P("head", SEQ),
            P(),
            P(),
            P(SEQ, "head"),
            P("head"),
            P("head"),
            P("head", SEQ),
            P("head", SEQ),
            P(SEQ, "head"),
            P("head"),
        ),
        out_specs=P(None, None, None, "head"),
        check_vma=False,
    )
```

```python
import jax
import jax.numpy as jnp
from jax import lax
from jax.sharding import PartitionSpec as P

D = 2560
QH = 8
KVH = 4
HD = 256
QD = 2048


SEQ = ("seq", "pair")
ALL = ("seq", "pair", "head")

EPS = 1e-06
NEG = -1e30
QSCALE = 0.0625


def norm_heads(values, gain, scale):
    shaped = values.reshape(values.shape[:-1] + (-1, gain.shape[0]))
    shaped = shaped * lax.rsqrt(jnp.mean(shaped * shaped, -1, keepdims=True) + EPS) * gain * scale
    return shaped.reshape(values.shape)


def finish_keys(pairs, k_gain):
    half = pairs.shape[-1] // 2
    keys = norm_heads(pairs[..., :half], k_gain, 1.0)
    return jnp.concatenate([keys, pairs[..., half:]], -1).astype(jnp.bfloat16)


def split_pairs(pairs):
    half = pairs.shape[-1] // 2
    keys = pairs[..., :half].reshape(pairs.shape[:-1] + (KVH, HD))
    values = pairs[..., half:].reshape(pairs.shape[:-1] + (KVH, HD))
    return (keys, values)


def exchange_sum(parts, axes, narrow=False):
    if narrow:
        moved = lax.all_to_all(parts.astype(jnp.bfloat16), axes, 0, 0, tiled=True)
        return jnp.sum(moved.astype(jnp.float32), 0)
    return jnp.sum(lax.all_to_all(parts, axes, 0, 0, tiled=True), 0)


def exchange_max(value, axes, count):
    spread = jnp.broadcast_to(value[None], (count,) + value.shape)
    return jnp.max(lax.all_to_all(spread, axes, 0, 0, tiled=True), 0)


def exchange_gather(piece, axes, count):
    spread = jnp.broadcast_to(piece[None], (count,) + piece.shape)
    return lax.all_to_all(spread, axes, 0, 0, tiled=True)


def seq_sum(parts):
    pair = lax.axis_size("pair")
    parts = parts.reshape((parts.shape[0] // pair, pair) + parts.shape[1:])
    parts = exchange_sum(jnp.swapaxes(parts, 0, 1), "pair")
    return exchange_sum(parts, "seq")


def seq_gather(piece):
    pair = lax.axis_size("pair")
    outer = lax.axis_size("seq")
    got = exchange_gather(exchange_gather(piece, "seq", outer), "pair", pair)
    return jnp.swapaxes(got, 0, 1).reshape((outer * pair,) + piece.shape)


def project_tokens(tokens, in_gain, w_query, w_keyval, q_gain, k_gain):
    flat = tokens.reshape(-1, tokens.shape[-1]).astype(jnp.float32)
    scaled = (flat * in_gain).astype(jnp.bfloat16)
    q_part = jnp.dot(scaled, w_query, preferred_element_type=jnp.float32)
    kv_part = jnp.dot(scaled, w_keyval, preferred_element_type=jnp.float32)
    squares = jnp.sum(flat * flat, -1)
    n_head = lax.axis_size("head")
    n_seq = lax.axis_size("seq") * lax.axis_size("pair")
    rows = flat.shape[0]
    half = rows // n_head
    block = q_part.shape[1]
    packed = jnp.concatenate([q_part, kv_part, jnp.pad(squares[:, None], ((0, 0), (0, 127)))], 1)
    packed = exchange_sum(packed.reshape(n_head, half, -1), "head")
    factor = lax.rsqrt(packed[:, 2 * block] / D + EPS)[:, None]
    q_raw = (packed[:, :block] * factor).astype(jnp.bfloat16)
    kv_raw = (packed[:, block : 2 * block] * factor).astype(jnp.bfloat16)
    both = exchange_gather(
        jnp.concatenate([q_raw, kv_raw], 1), ALL, n_seq * n_head
    ).reshape(n_seq, n_head, half, 2 * block)
    both = jnp.transpose(both, (1, 2, 0, 3)).reshape(rows, n_seq, 2 * block)
    q_raw = both[:, :, :block].reshape(rows, -1)
    kv_raw = both[:, :, block:].reshape(rows, -1)
    queries = norm_heads(q_raw.astype(jnp.float32), q_gain, QSCALE).astype(jnp.bfloat16)
    fresh = finish_keys(kv_raw.astype(jnp.float32), k_gain)
    return (queries, fresh)


def shards(
    step_tokens,
    parents,
    tail_cache,
    tail_len,
    cache,
    cache_len,
    prompt_states,
    prompt_len,
    in_gain,
    w_query,
    w_keyval,
    q_gain,
    k_gain,
    w_out,
    post_gain,
    ffn_gain,
    w_gate,
    w_up,
    w_down,
    final_gain,
):
    f32 = jnp.float32
    bf16 = jnp.bfloat16
    n_head = lax.axis_size("head")
    n_seq = lax.axis_size("seq") * lax.axis_size("pair")
    seq_at = lax.axis_index("seq") * lax.axis_size("pair") + lax.axis_index("pair")
    head_at = lax.axis_index("head")
    flat_at = seq_at * n_head + head_at
    steps, groups, beams, width = step_tokens.shape
    pre = prompt_states.shape[0]
    repeat = QH // KVH
    every_query, every_fresh = project_tokens(
        step_tokens, in_gain, w_query, w_keyval, q_gain, k_gain
    )
    every_query = every_query.reshape(steps, groups, beams, -1)
    every_fresh = every_fresh.reshape(steps, groups, beams, -1)
    owners = n_seq * n_head
    prompt_all = lax.all_gather(prompt_states, SEQ, axis=1, tiled=True)
    prompt_all, every_query, every_fresh = lax.optimization_barrier(
        (prompt_all, every_query, every_fresh)
    )
    prompt_all = prompt_all.astype(f32)
    prompt_seg = prompt_all.shape[1] // owners
    prompt_scaled = (prompt_all * in_gain).astype(bf16).reshape(-1, width)
    prompt_terms = jnp.dot(prompt_scaled, w_keyval, preferred_element_type=f32)
    kv_cols = prompt_terms.shape[1]
    prompt_terms = jnp.transpose(
        prompt_terms.reshape(pre, owners, prompt_seg, kv_cols), (1, 0, 2, 3)
    ).reshape(owners, -1)
    prompt_squares = jnp.transpose(
        jnp.sum(prompt_all * prompt_all, -1).reshape(pre, owners, prompt_seg), (1, 0, 2)
    ).reshape(owners, -1)
    own_rows = pre * prompt_seg
    pad_rows = -(-own_rows // 128) * 128
    prompt_terms = jnp.concatenate(
        [prompt_terms, jnp.pad(prompt_squares, ((0, 0), (0, pad_rows - own_rows)))], 1
    )
    prompt_terms = lax.all_to_all(prompt_terms, ALL, 0, 0, tiled=True)
    prompt_terms = jnp.sum(prompt_terms.reshape(n_seq, n_head, -1), 1)
    prompt_sq = prompt_terms[0, own_rows * kv_cols : own_rows * kv_cols + own_rows]
    prompt_sum = jnp.transpose(
        prompt_terms[:, : own_rows * kv_cols].reshape(n_seq, own_rows, kv_cols), (1, 0, 2)
    ).reshape(own_rows, -1)
    prompt_pairs = finish_keys(prompt_sum * lax.rsqrt(prompt_sq / D + EPS)[:, None], k_gain)
    prompt_pairs = prompt_pairs.reshape(pre, prompt_seg, -1)
    prompt_ok = (flat_at * prompt_seg + jnp.arange(prompt_seg))[None, :] < prompt_len[:, None]
    cache_seg = cache.shape[1]
    cache_ok = (flat_at * cache_seg + jnp.arange(cache_seg))[None, :] < cache_len[:, None]
    span = max(prompt_seg, cache_seg)
    shared = jnp.concatenate(
        [
            jnp.pad(prompt_pairs, ((0, 0), (0, span - prompt_seg), (0, 0))),
            jnp.pad(cache, ((0, 0), (0, span - cache_seg), (0, 0))),
        ],
        0,
    )
    shared_ok = jnp.concatenate(
        [
            jnp.pad(prompt_ok, ((0, 0), (0, span - prompt_seg))),
            jnp.pad(cache_ok, ((0, 0), (0, span - cache_seg))),
        ],
        0,
    )
    shared_keys, shared_values = split_pairs(shared)
    tail_seg = tail_cache.shape[2]
    local_beams = tail_cache.shape[1]
    offset = (seq_at * tail_seg + jnp.arange(tail_seg))[None, :] - tail_len[:, None]
    all_beams = jnp.arange(beams)
    everyone = lax.all_gather(tail_cache, "head", axis=1, tiled=True)
    n_dev = n_seq * n_head
    first_beam = head_at * local_beams
    many = steps * beams * repeat
    grouped = jnp.transpose(
        every_query.reshape(steps, groups, beams, KVH, repeat, HD), (1, 3, 0, 2, 4, 5)
    ).reshape(groups, KVH, many, HD)
    source = jnp.broadcast_to(all_beams[None, :], (groups, beams))
    ancestors = []
    tail_states = []
    for step in range(steps):
        link = parents[step]
        source = jnp.take_along_axis(source, link, axis=1)
        ancestors = [jnp.take_along_axis(a, link, axis=1) for a in ancestors]
        ancestors.append(jnp.broadcast_to(all_beams[None, :], (groups, beams)))
        picks = lax.dynamic_slice_in_dim(source, first_beam, local_beams, 1)
        tail_state = jnp.take_along_axis(everyone, picks[:, :, None, None], axis=1)
        for back, anc in enumerate(ancestors):
            mine = lax.dynamic_slice_in_dim(anc, first_beam, local_beams, 1)
            written = jnp.take_along_axis(every_fresh[back], mine[:, :, None], axis=1)
            tail_state = jnp.where(
                (offset == back)[:, None, :, None], written[:, :, None, :], tail_state
            )
        tail_states.append(tail_state)
    tails = jnp.stack(tail_states, 1).reshape(groups, steps * local_beams * tail_seg, -1)
    all_keys, all_values = split_pairs(jnp.concatenate([shared, tails], 1))
    step_id = jnp.arange(steps)
    same_step = step_id[:, None, None, None, None, None] == step_id[None, None, None, :, None, None]
    same_beam = (
        all_beams[None, :, None, None, None, None]
        == (first_beam + jnp.arange(local_beams))[None, None, None, None, :, None]
    )
    live = offset[:, None, None, None, None, None, :] <= step_id[None, None, None, None, :, None, None]
    tail_mask = jnp.broadcast_to(
        (same_step & same_beam)[None] & live,
        (groups, steps, beams, repeat, steps, local_beams, tail_seg),
    ).reshape(groups, many, -1)
    mask = jnp.concatenate(
        [jnp.broadcast_to(shared_ok[:, None, :], (groups, many, span)), tail_mask], -1
    )[:, None]
    scores = jnp.einsum("gkmd,gtkd->gkmt", grouped, all_keys, preferred_element_type=f32)
    scores = jnp.where(mask, scores, NEG)
    top = jnp.max(scores, -1).reshape(groups, KVH, steps, beams, repeat)
    top = exchange_max(top, ALL, n_dev)
    weights = jnp.where(mask, jnp.exp(scores - top.reshape(groups, KVH, many)[..., None]), 0.0)
    total = jnp.sum(weights, -1).reshape(groups, KVH, steps, beams, repeat)
    weighted = jnp.einsum(
        "gkmt,gtkd->gkmd", weights.astype(bf16), all_values, preferred_element_type=f32
    ).reshape(groups, KVH, steps, beams, repeat, HD)
    rows = steps * groups * beams
    piece = QD // n_dev
    per_head = HD // piece
    weighted = jnp.transpose(
        weighted.reshape(groups, KVH, steps, beams, repeat, per_head, piece), (1, 4, 5, 2, 0, 3, 6)
    ).reshape(n_dev, -1)
    total = jnp.repeat(jnp.transpose(total, (1, 4, 2, 0, 3)).reshape(QH, rows), per_head, 0)
    lanes = -(-rows // 128) * 128
    packed = jnp.concatenate([weighted, jnp.pad(total, ((0, 0), (0, lanes - rows)))], 1)
    pair = lax.axis_size("pair")
    packed = packed.reshape(n_seq // pair, pair, n_head, -1)
    packed = exchange_sum(jnp.swapaxes(packed, 0, 1), "pair").reshape(n_dev // pair, -1)
    packed = exchange_sum(packed, ("seq", "head"))
    share = packed[: rows * piece].reshape(rows, piece)
    own_total = packed[rows * piece : rows * piece + rows]
    attn = (share / own_total[:, None]).astype(bf16)
    attn = exchange_gather(attn, "head", n_head)
    attn = jnp.transpose(attn, (1, 0, 2)).reshape(rows, -1)
    partial_out = jnp.dot(attn, w_out, preferred_element_type=f32)
    per_dev = rows // n_seq
    out_proj = seq_sum(partial_out.reshape(n_seq, per_dev, -1))
    out_sq = lax.psum(jnp.sum(out_proj * out_proj, -1), "head")
    x_all = step_tokens.reshape(rows, -1)
    x_f = lax.dynamic_slice_in_dim(x_all, seq_at * per_dev, per_dev, 0).astype(f32)
    state = (x_f + out_proj * lax.rsqrt(out_sq / D + EPS)[:, None] * post_gain).astype(bf16)
    state_all = seq_gather(state).reshape(rows, -1)
    state_f = state_all.astype(f32)
    scaled_two = (state_f * ffn_gain).astype(bf16)
    gate_part = jnp.dot(scaled_two, w_gate, preferred_element_type=f32)
    up_part = jnp.dot(scaled_two, w_up, preferred_element_type=f32)
    hidden = gate_part.shape[1]
    head_rows = rows // n_head
    packed = jnp.concatenate(
        [gate_part, up_part, jnp.pad(jnp.sum(state_f * state_f, -1)[:, None], ((0, 0), (0, 127)))],
        1,
    )
    packed = exchange_sum(packed.reshape(n_head, head_rows, -1), "head")
    norm_s = lax.rsqrt(packed[:, 2 * hidden] / D + EPS)[:, None]
    inner = (
        jax.nn.gelu(packed[:, :hidden] * norm_s, approximate=True)
        * (packed[:, hidden : 2 * hidden] * norm_s)
    ).astype(bf16)
    inner = exchange_gather(inner, "head", n_head).reshape(rows, hidden)
    ffn_out = seq_sum(jnp.dot(inner, w_down, preferred_element_type=f32).reshape(n_seq, per_dev, -1))
    ffn_sq = lax.psum(jnp.sum(ffn_out * ffn_out, -1), "head")
    result = (
        state.astype(f32) + ffn_out * lax.rsqrt(ffn_sq / D + EPS)[:, None] * final_gain
    ).astype(bf16)
    result = seq_gather(result)
    return result.reshape(steps, groups, beams, -1)


def solution(mesh):
    devices = mesh.devices
    fine = jax.sharding.Mesh(
        devices.reshape(devices.shape[0] // 2, 2, devices.shape[1]), ("seq", "pair", "head")
    )
    return jax.shard_map(
        shards,
        mesh=fine,
        in_specs=(
            P(None, None, None, "head"),
            P(),
            P(None, "head", SEQ, None),
            P(),
            P(None, ALL, None),
            P(),
            P(None, SEQ, "head"),
            P(),
            P("head"),
            P("head", SEQ),
            P("head", SEQ),
            P(),
            P(),
            P(SEQ, "head"),
            P("head"),
            P("head"),
            P("head", SEQ),
            P("head", SEQ),
            P(SEQ, "head"),
            P("head"),
        ),
        out_specs=P(None, None, None, "head"),
        check_vma=False,
    )
```

```python
import jax
import jax.numpy as jnp
from jax import lax
from jax.sharding import PartitionSpec as P

D = 2560
QH = 8
KVH = 4
HD = 256
QD = 2048


SEQ = ("seq", "pair")
ALL = ("seq", "pair", "head")

EPS = 1e-06
NEG = -1e30
QSCALE = 0.0625


def norm_heads(values, gain, scale):
    shaped = values.reshape(values.shape[:-1] + (-1, gain.shape[0]))
    shaped = shaped * lax.rsqrt(jnp.mean(shaped * shaped, -1, keepdims=True) + EPS) * gain * scale
    return shaped.reshape(values.shape)


def finish_keys(pairs, k_gain):
    half = pairs.shape[-1] // 2
    keys = norm_heads(pairs[..., :half], k_gain, 1.0)
    return jnp.concatenate([keys, pairs[..., half:]], -1).astype(jnp.bfloat16)


def split_pairs(pairs):
    half = pairs.shape[-1] // 2
    keys = pairs[..., :half].reshape(pairs.shape[:-1] + (KVH, HD))
    values = pairs[..., half:].reshape(pairs.shape[:-1] + (KVH, HD))
    return (keys, values)


def exchange_sum(parts, axes, narrow=False):
    if narrow:
        moved = lax.all_to_all(parts.astype(jnp.bfloat16), axes, 0, 0, tiled=True)
        return jnp.sum(moved.astype(jnp.float32), 0)
    return jnp.sum(lax.all_to_all(parts, axes, 0, 0, tiled=True), 0)


def exchange_max(value, axes, count):
    flat = value.reshape(-1, 128)
    spread = jnp.broadcast_to(flat[None], (count,) + flat.shape)
    return jnp.max(lax.all_to_all(spread, axes, 0, 0, tiled=True), 0).reshape(value.shape)


def exchange_gather(piece, axes, count):
    spread = jnp.broadcast_to(piece[None], (count,) + piece.shape)
    return lax.all_to_all(spread, axes, 0, 0, tiled=True)


def seq_sum(parts):
    pair = lax.axis_size("pair")
    parts = parts.reshape((parts.shape[0] // pair, pair) + parts.shape[1:])
    parts = exchange_sum(jnp.swapaxes(parts, 0, 1), "pair")
    return exchange_sum(parts, "seq")


def seq_gather(piece):
    pair = lax.axis_size("pair")
    outer = lax.axis_size("seq")
    got = exchange_gather(exchange_gather(piece, "seq", outer), "pair", pair)
    return jnp.swapaxes(got, 0, 1).reshape((outer * pair,) + piece.shape)


def project_tokens(tokens, in_gain, w_query, w_keyval, q_gain, k_gain):
    flat = tokens.reshape(-1, tokens.shape[-1]).astype(jnp.float32)
    scaled = (flat * in_gain).astype(jnp.bfloat16)
    q_part = jnp.dot(scaled, w_query, preferred_element_type=jnp.float32)
    kv_part = jnp.dot(scaled, w_keyval, preferred_element_type=jnp.float32)
    squares = jnp.sum(flat * flat, -1)
    n_head = lax.axis_size("head")
    n_seq = lax.axis_size("seq") * lax.axis_size("pair")
    rows = flat.shape[0]
    half = rows // n_head
    block = q_part.shape[1]
    packed = jnp.concatenate([q_part, kv_part, jnp.pad(squares[:, None], ((0, 0), (0, 127)))], 1)
    packed = exchange_sum(packed.reshape(n_head, half, -1), "head")
    factor = lax.rsqrt(packed[:, 2 * block] / D + EPS)[:, None]
    q_raw = (packed[:, :block] * factor).astype(jnp.bfloat16)
    kv_raw = (packed[:, block : 2 * block] * factor).astype(jnp.bfloat16)
    both = exchange_gather(
        jnp.concatenate([q_raw, kv_raw], 1), ALL, n_seq * n_head
    ).reshape(n_seq, n_head, half, 2 * block)
    both = jnp.transpose(both, (1, 2, 0, 3)).reshape(rows, n_seq, 2 * block)
    q_raw = both[:, :, :block].reshape(rows, -1)
    kv_raw = both[:, :, block:].reshape(rows, -1)
    queries = norm_heads(q_raw.astype(jnp.float32), q_gain, QSCALE).astype(jnp.bfloat16)
    fresh = finish_keys(kv_raw.astype(jnp.float32), k_gain)
    return (queries, fresh)


def shards(
    step_tokens,
    parents,
    tail_cache,
    tail_len,
    cache,
    cache_len,
    prompt_states,
    prompt_len,
    in_gain,
    w_query,
    w_keyval,
    q_gain,
    k_gain,
    w_out,
    post_gain,
    ffn_gain,
    w_gate,
    w_up,
    w_down,
    final_gain,
):
    f32 = jnp.float32
    bf16 = jnp.bfloat16
    n_head = lax.axis_size("head")
    n_seq = lax.axis_size("seq") * lax.axis_size("pair")
    seq_at = lax.axis_index("seq") * lax.axis_size("pair") + lax.axis_index("pair")
    head_at = lax.axis_index("head")
    flat_at = seq_at * n_head + head_at
    steps, groups, beams, width = step_tokens.shape
    pre = prompt_states.shape[0]
    repeat = QH // KVH
    rows = jnp.transpose(prompt_states, (1, 0, 2)).astype(f32)
    prompt_scaled = (rows * in_gain).astype(bf16).reshape(-1, width)
    prompt_squares = jnp.sum(rows * rows, -1).reshape(-1)
    prompt_terms = jnp.dot(
        prompt_scaled,
        lax.all_gather(w_keyval, SEQ, axis=1, tiled=True),
        preferred_element_type=f32,
    )
    prompt_sum, prompt_sq = (
        lax.psum_scatter(prompt_terms, "head", scatter_dimension=0, tiled=True),
        lax.psum_scatter(prompt_squares, "head", scatter_dimension=0, tiled=True),
    )
    prompt_pairs = finish_keys(prompt_sum * lax.rsqrt(prompt_sq / D + EPS)[:, None], k_gain)
    prompt_seg = prompt_pairs.shape[0] // pre
    prompt_pairs = jnp.transpose(prompt_pairs.reshape(prompt_seg, pre, -1), (1, 0, 2))
    prompt_ok = (flat_at * prompt_seg + jnp.arange(prompt_seg))[None, :] < prompt_len[:, None]
    cache_seg = cache.shape[1]
    cache_ok = (flat_at * cache_seg + jnp.arange(cache_seg))[None, :] < cache_len[:, None]
    span = max(prompt_seg, cache_seg)
    shared = jnp.concatenate(
        [
            jnp.pad(prompt_pairs, ((0, 0), (0, span - prompt_seg), (0, 0))),
            jnp.pad(cache, ((0, 0), (0, span - cache_seg), (0, 0))),
        ],
        0,
    )
    shared_ok = jnp.concatenate(
        [
            jnp.pad(prompt_ok, ((0, 0), (0, span - prompt_seg))),
            jnp.pad(cache_ok, ((0, 0), (0, span - cache_seg))),
        ],
        0,
    )
    shared_keys, shared_values = split_pairs(shared)
    tail_seg = tail_cache.shape[2]
    local_beams = tail_cache.shape[1]
    offset = (seq_at * tail_seg + jnp.arange(tail_seg))[None, :] - tail_len[:, None]
    all_beams = jnp.arange(beams)
    every_query, every_fresh = project_tokens(
        step_tokens, in_gain, w_query, w_keyval, q_gain, k_gain
    )
    every_query = every_query.reshape(steps, groups, beams, -1)
    every_fresh = every_fresh.reshape(steps, groups, beams, -1)
    everyone = lax.all_gather(tail_cache, "head", axis=1, tiled=True)
    n_dev = n_seq * n_head
    first_beam = head_at * local_beams
    many = steps * beams * repeat
    grouped = jnp.transpose(
        every_query.reshape(steps, groups, beams, KVH, repeat, HD), (1, 3, 0, 2, 4, 5)
    ).reshape(groups, KVH, many, HD)
    source = jnp.broadcast_to(all_beams[None, :], (groups, beams))
    ancestors = []
    tail_states = []
    for step in range(steps):
        link = parents[step]
        source = jnp.take_along_axis(source, link, axis=1)
        ancestors = [jnp.take_along_axis(a, link, axis=1) for a in ancestors]
        ancestors.append(jnp.broadcast_to(all_beams[None, :], (groups, beams)))
        picks = lax.dynamic_slice_in_dim(source, first_beam, local_beams, 1)
        tail_state = jnp.take_along_axis(everyone, picks[:, :, None, None], axis=1)
        for back, anc in enumerate(ancestors):
            mine = lax.dynamic_slice_in_dim(anc, first_beam, local_beams, 1)
            written = jnp.take_along_axis(every_fresh[back], mine[:, :, None], axis=1)
            tail_state = jnp.where(
                (offset == back)[:, None, :, None], written[:, :, None, :], tail_state
            )
        tail_states.append(tail_state)
    tails = jnp.stack(tail_states, 1).reshape(groups, steps * local_beams * tail_seg, -1)
    all_keys, all_values = split_pairs(jnp.concatenate([shared, tails], 1))
    step_id = jnp.arange(steps)
    same_step = step_id[:, None, None, None, None, None] == step_id[None, None, None, :, None, None]
    same_beam = (
        all_beams[None, :, None, None, None, None]
        == (first_beam + jnp.arange(local_beams))[None, None, None, None, :, None]
    )
    live = offset[:, None, None, None, None, None, :] <= step_id[None, None, None, None, :, None, None]
    tail_mask = jnp.broadcast_to(
        (same_step & same_beam)[None] & live,
        (groups, steps, beams, repeat, steps, local_beams, tail_seg),
    ).reshape(groups, many, -1)
    mask = jnp.concatenate(
        [jnp.broadcast_to(shared_ok[:, None, :], (groups, many, span)), tail_mask], -1
    )[:, None]
    scores = jnp.einsum("gkmd,gtkd->gkmt", grouped, all_keys, preferred_element_type=f32)
    scores = jnp.where(mask, scores, NEG)
    top = jnp.max(scores, -1).reshape(groups, KVH, steps, beams, repeat)
    top = exchange_max(top, ALL, n_dev)
    weights = jnp.where(mask, jnp.exp(scores - top.reshape(groups, KVH, many)[..., None]), 0.0)
    total = jnp.sum(weights, -1).reshape(groups, KVH, steps, beams, repeat)
    weighted = jnp.einsum(
        "gkmt,gtkd->gkmd", weights.astype(bf16), all_values, preferred_element_type=f32
    ).reshape(groups, KVH, steps, beams, repeat, HD)
    rows = steps * groups * beams
    piece = QD // n_dev
    per_head = HD // piece
    weighted = jnp.transpose(
        weighted.reshape(groups, KVH, steps, beams, repeat, per_head, piece), (1, 4, 5, 2, 0, 3, 6)
    ).reshape(n_dev, -1)
    total = jnp.repeat(jnp.transpose(total, (1, 4, 2, 0, 3)).reshape(QH, rows), per_head, 0)
    lanes = -(-rows // 128) * 128
    packed = jnp.concatenate([weighted, jnp.pad(total, ((0, 0), (0, lanes - rows)))], 1)
    pair = lax.axis_size("pair")
    packed = packed.reshape(n_seq // pair, pair, n_head, -1, 128)
    packed = exchange_sum(jnp.swapaxes(packed, 0, 1), "pair").reshape(n_dev // pair, -1, 128)
    packed = exchange_sum(packed, ("seq", "head")).reshape(-1)
    share = packed[: rows * piece].reshape(rows, piece)
    own_total = packed[rows * piece : rows * piece + rows]
    attn = (share / own_total[:, None]).astype(bf16)
    attn = exchange_gather(attn, "head", n_head)
    attn = jnp.transpose(attn, (1, 0, 2)).reshape(rows, -1)
    partial_out = jnp.dot(attn, w_out, preferred_element_type=f32)
    per_dev = rows // n_seq
    out_proj = seq_sum(partial_out.reshape(n_seq, per_dev, -1))
    out_sq = lax.psum(jnp.sum(out_proj * out_proj, -1), "head")
    x_all = step_tokens.reshape(rows, -1)
    x_f = lax.dynamic_slice_in_dim(x_all, seq_at * per_dev, per_dev, 0).astype(f32)
    state = (x_f + out_proj * lax.rsqrt(out_sq / D + EPS)[:, None] * post_gain).astype(bf16)
    state_all = seq_gather(state).reshape(rows, -1)
    state_f = state_all.astype(f32)
    scaled_two = (state_f * ffn_gain).astype(bf16)
    gate_part = jnp.dot(scaled_two, w_gate, preferred_element_type=f32)
    up_part = jnp.dot(scaled_two, w_up, preferred_element_type=f32)
    hidden = gate_part.shape[1]
    head_rows = rows // n_head
    packed = jnp.concatenate(
        [gate_part, up_part, jnp.pad(jnp.sum(state_f * state_f, -1)[:, None], ((0, 0), (0, 127)))],
        1,
    )
    packed = exchange_sum(packed.reshape(n_head, head_rows, -1), "head")
    norm_s = lax.rsqrt(packed[:, 2 * hidden] / D + EPS)[:, None]
    inner = (
        jax.nn.gelu(packed[:, :hidden] * norm_s, approximate=True)
        * (packed[:, hidden : 2 * hidden] * norm_s)
    ).astype(bf16)
    inner = exchange_gather(inner, "head", n_head).reshape(rows, hidden)
    ffn_out = seq_sum(jnp.dot(inner, w_down, preferred_element_type=f32).reshape(n_seq, per_dev, -1))
    ffn_sq = lax.psum(jnp.sum(ffn_out * ffn_out, -1), "head")
    result = (
        state.astype(f32) + ffn_out * lax.rsqrt(ffn_sq / D + EPS)[:, None] * final_gain
    ).astype(bf16)
    result = seq_gather(result)
    return result.reshape(steps, groups, beams, -1)


def solution(mesh):
    devices = mesh.devices
    fine = jax.sharding.Mesh(
        devices.reshape(devices.shape[0] // 2, 2, devices.shape[1]), ("seq", "pair", "head")
    )
    return jax.shard_map(
        shards,
        mesh=fine,
        in_specs=(
            P(None, None, None, "head"),
            P(),
            P(None, "head", SEQ, None),
            P(),
            P(None, ALL, None),
            P(),
            P(None, SEQ, "head"),
            P(),
            P("head"),
            P("head", SEQ),
            P("head", SEQ),
            P(),
            P(),
            P(SEQ, "head"),
            P("head"),
            P("head"),
            P("head", SEQ),
            P("head", SEQ),
            P(SEQ, "head"),
            P("head"),
        ),
        out_specs=P(None, None, None, "head"),
        check_vma=False,
    )
```

```python
import jax
import jax.numpy as jnp
from jax import lax
from jax.sharding import PartitionSpec as P

D = 2560
QH = 8
KVH = 4
HD = 256
QD = 2048


SEQ = ("seq", "pair")
ALL = ("seq", "pair", "head")

EPS = 1e-06
NEG = -1e30
QSCALE = 0.0625


def norm_heads(values, gain, scale):
    shaped = values.reshape(values.shape[:-1] + (-1, gain.shape[0]))
    shaped = shaped * lax.rsqrt(jnp.mean(shaped * shaped, -1, keepdims=True) + EPS) * gain * scale
    return shaped.reshape(values.shape)


def finish_keys(pairs, k_gain):
    half = pairs.shape[-1] // 2
    keys = norm_heads(pairs[..., :half], k_gain, 1.0)
    return jnp.concatenate([keys, pairs[..., half:]], -1).astype(jnp.bfloat16)


def split_pairs(pairs):
    half = pairs.shape[-1] // 2
    keys = pairs[..., :half].reshape(pairs.shape[:-1] + (KVH, HD))
    values = pairs[..., half:].reshape(pairs.shape[:-1] + (KVH, HD))
    return (keys, values)


def lane_shape(shape, dtype):
    rows = 8 if jnp.dtype(dtype).itemsize == 4 else 16
    size = 1
    for n in shape:
        size = size * n
    aligned = len(shape) >= 2 and shape[-1] % 128 == 0 and shape[-2] % rows == 0
    if aligned or size % 128:
        return shape
    return (size // 128, 128)


def exchange_sum(parts, axes):
    shape = lane_shape(parts.shape[1:], parts.dtype)
    moved = lax.all_to_all(parts.reshape((parts.shape[0],) + shape), axes, 0, 0, tiled=True)
    return jnp.sum(moved, 0).reshape(parts.shape[1:])


def exchange_max(value, axes, count):
    flat = value.reshape(-1, 128)
    spread = jnp.broadcast_to(flat[None], (count,) + flat.shape)
    return jnp.max(lax.all_to_all(spread, axes, 0, 0, tiled=True), 0).reshape(value.shape)


def exchange_gather(piece, axes, count):
    flat = piece.reshape(lane_shape(piece.shape, piece.dtype))
    spread = jnp.broadcast_to(flat[None], (count,) + flat.shape)
    return lax.all_to_all(spread, axes, 0, 0, tiled=True).reshape((count,) + piece.shape)


def seq_sum(parts):
    pair = lax.axis_size("pair")
    parts = parts.reshape((parts.shape[0] // pair, pair) + parts.shape[1:])
    parts = exchange_sum(jnp.swapaxes(parts, 0, 1), "pair")
    return exchange_sum(parts, "seq")


def seq_gather(piece):
    pair = lax.axis_size("pair")
    outer = lax.axis_size("seq")
    got = exchange_gather(exchange_gather(piece, "seq", outer), "pair", pair)
    return jnp.swapaxes(got, 0, 1).reshape((outer * pair,) + piece.shape)


def project_tokens(tokens, in_gain, w_query, w_keyval, q_gain, k_gain):
    flat = tokens.reshape(-1, tokens.shape[-1]).astype(jnp.float32)
    scaled = (flat * in_gain).astype(jnp.bfloat16)
    q_part = jnp.dot(scaled, w_query, preferred_element_type=jnp.float32)
    kv_part = jnp.dot(scaled, w_keyval, preferred_element_type=jnp.float32)
    squares = jnp.sum(flat * flat, -1)
    n_head = lax.axis_size("head")
    n_seq = lax.axis_size("seq") * lax.axis_size("pair")
    rows = flat.shape[0]
    half = rows // n_head
    block = q_part.shape[1]
    packed = jnp.concatenate([q_part, kv_part, jnp.pad(squares[:, None], ((0, 0), (0, 127)))], 1)
    packed = exchange_sum(packed.reshape(n_head, half, -1), "head")
    factor = lax.rsqrt(packed[:, 2 * block] / D + EPS)[:, None]
    q_raw = (packed[:, :block] * factor).astype(jnp.bfloat16)
    kv_raw = (packed[:, block : 2 * block] * factor).astype(jnp.bfloat16)
    both = exchange_gather(
        jnp.concatenate([q_raw, kv_raw], 1), ALL, n_seq * n_head
    ).reshape(n_seq, n_head, half, 2 * block)
    both = jnp.transpose(both, (1, 2, 0, 3)).reshape(rows, n_seq, 2 * block)
    q_raw = both[:, :, :block].reshape(rows, -1)
    kv_raw = both[:, :, block:].reshape(rows, -1)
    queries = norm_heads(q_raw.astype(jnp.float32), q_gain, QSCALE).astype(jnp.bfloat16)
    fresh = finish_keys(kv_raw.astype(jnp.float32), k_gain)
    return (queries, fresh)


def shards(
    step_tokens,
    parents,
    tail_cache,
    tail_len,
    cache,
    cache_len,
    prompt_states,
    prompt_len,
    in_gain,
    w_query,
    w_keyval,
    q_gain,
    k_gain,
    w_out,
    post_gain,
    ffn_gain,
    w_gate,
    w_up,
    w_down,
    final_gain,
):
    f32 = jnp.float32
    bf16 = jnp.bfloat16
    n_head = lax.axis_size("head")
    n_seq = lax.axis_size("seq") * lax.axis_size("pair")
    seq_at = lax.axis_index("seq") * lax.axis_size("pair") + lax.axis_index("pair")
    head_at = lax.axis_index("head")
    flat_at = seq_at * n_head + head_at
    steps, groups, beams, width = step_tokens.shape
    pre = prompt_states.shape[0]
    repeat = QH // KVH
    rows = jnp.transpose(prompt_states, (1, 0, 2)).astype(f32)
    prompt_scaled = (rows * in_gain).astype(bf16).reshape(-1, width)
    prompt_squares = jnp.sum(rows * rows, -1).reshape(-1)
    prompt_terms = jnp.dot(
        prompt_scaled,
        lax.all_gather(w_keyval, SEQ, axis=1, tiled=True),
        preferred_element_type=f32,
    )
    prompt_sum, prompt_sq = (
        lax.psum_scatter(prompt_terms, "head", scatter_dimension=0, tiled=True),
        lax.psum_scatter(prompt_squares, "head", scatter_dimension=0, tiled=True),
    )
    prompt_pairs = finish_keys(prompt_sum * lax.rsqrt(prompt_sq / D + EPS)[:, None], k_gain)
    prompt_seg = prompt_pairs.shape[0] // pre
    prompt_pairs = jnp.transpose(prompt_pairs.reshape(prompt_seg, pre, -1), (1, 0, 2))
    prompt_ok = (flat_at * prompt_seg + jnp.arange(prompt_seg))[None, :] < prompt_len[:, None]
    cache_seg = cache.shape[1]
    cache_ok = (flat_at * cache_seg + jnp.arange(cache_seg))[None, :] < cache_len[:, None]
    span = max(prompt_seg, cache_seg)
    shared = jnp.concatenate(
        [
            jnp.pad(prompt_pairs, ((0, 0), (0, span - prompt_seg), (0, 0))),
            jnp.pad(cache, ((0, 0), (0, span - cache_seg), (0, 0))),
        ],
        0,
    )
    shared_ok = jnp.concatenate(
        [
            jnp.pad(prompt_ok, ((0, 0), (0, span - prompt_seg))),
            jnp.pad(cache_ok, ((0, 0), (0, span - cache_seg))),
        ],
        0,
    )
    shared_keys, shared_values = split_pairs(shared)
    tail_seg = tail_cache.shape[2]
    local_beams = tail_cache.shape[1]
    offset = (seq_at * tail_seg + jnp.arange(tail_seg))[None, :] - tail_len[:, None]
    all_beams = jnp.arange(beams)
    every_query, every_fresh = project_tokens(
        step_tokens, in_gain, w_query, w_keyval, q_gain, k_gain
    )
    every_query = every_query.reshape(steps, groups, beams, -1)
    every_fresh = every_fresh.reshape(steps, groups, beams, -1)
    everyone = lax.all_gather(tail_cache, "head", axis=1, tiled=True)
    n_dev = n_seq * n_head
    first_beam = head_at * local_beams
    many = steps * beams * repeat
    grouped = jnp.transpose(
        every_query.reshape(steps, groups, beams, KVH, repeat, HD), (1, 3, 0, 2, 4, 5)
    ).reshape(groups, KVH, many, HD)
    source = jnp.broadcast_to(all_beams[None, :], (groups, beams))
    ancestors = []
    tail_states = []
    for step in range(steps):
        link = parents[step]
        source = jnp.take_along_axis(source, link, axis=1)
        ancestors = [jnp.take_along_axis(a, link, axis=1) for a in ancestors]
        ancestors.append(jnp.broadcast_to(all_beams[None, :], (groups, beams)))
        picks = lax.dynamic_slice_in_dim(source, first_beam, local_beams, 1)
        tail_state = jnp.take_along_axis(everyone, picks[:, :, None, None], axis=1)
        for back, anc in enumerate(ancestors):
            mine = lax.dynamic_slice_in_dim(anc, first_beam, local_beams, 1)
            written = jnp.take_along_axis(every_fresh[back], mine[:, :, None], axis=1)
            tail_state = jnp.where(
                (offset == back)[:, None, :, None], written[:, :, None, :], tail_state
            )
        tail_states.append(tail_state)
    tails = jnp.stack(tail_states, 1).reshape(groups, steps * local_beams * tail_seg, -1)
    all_keys, all_values = split_pairs(jnp.concatenate([shared, tails], 1))
    step_id = jnp.arange(steps)
    same_step = step_id[:, None, None, None, None, None] == step_id[None, None, None, :, None, None]
    same_beam = (
        all_beams[None, :, None, None, None, None]
        == (first_beam + jnp.arange(local_beams))[None, None, None, None, :, None]
    )
    live = offset[:, None, None, None, None, None, :] <= step_id[None, None, None, None, :, None, None]
    tail_mask = jnp.broadcast_to(
        (same_step & same_beam)[None] & live,
        (groups, steps, beams, repeat, steps, local_beams, tail_seg),
    ).reshape(groups, many, -1)
    mask = jnp.concatenate(
        [jnp.broadcast_to(shared_ok[:, None, :], (groups, many, span)), tail_mask], -1
    )[:, None]
    scores = jnp.einsum("gkmd,gtkd->gkmt", grouped, all_keys, preferred_element_type=f32)
    scores = jnp.where(mask, scores, NEG)
    top = jnp.max(scores, -1).reshape(groups, KVH, steps, beams, repeat)
    top = exchange_max(top, ALL, n_dev)
    weights = jnp.where(mask, jnp.exp(scores - top.reshape(groups, KVH, many)[..., None]), 0.0)
    total = jnp.sum(weights, -1).reshape(groups, KVH, steps, beams, repeat)
    weighted = jnp.einsum(
        "gkmt,gtkd->gkmd", weights.astype(bf16), all_values, preferred_element_type=f32
    ).reshape(groups, KVH, steps, beams, repeat, HD)
    rows = steps * groups * beams
    piece = QD // n_dev
    per_head = HD // piece
    weighted = jnp.transpose(
        weighted.reshape(groups, KVH, steps, beams, repeat, per_head, piece), (1, 4, 5, 2, 0, 3, 6)
    ).reshape(n_dev, -1)
    total = jnp.repeat(jnp.transpose(total, (1, 4, 2, 0, 3)).reshape(QH, rows), per_head, 0)
    lanes = -(-rows // 128) * 128
    packed = jnp.concatenate([weighted, jnp.pad(total, ((0, 0), (0, lanes - rows)))], 1)
    pair = lax.axis_size("pair")
    packed = packed.reshape(n_seq // pair, pair, n_head, -1, 128)
    packed = exchange_sum(jnp.swapaxes(packed, 0, 1), "pair").reshape(n_dev // pair, -1, 128)
    packed = exchange_sum(packed, ("seq", "head")).reshape(-1)
    share = packed[: rows * piece].reshape(rows, piece)
    own_total = packed[rows * piece : rows * piece + rows]
    attn = (share / own_total[:, None]).astype(bf16)
    attn = exchange_gather(attn, "head", n_head)
    attn = jnp.transpose(attn, (1, 0, 2)).reshape(rows, -1)
    partial_out = jnp.dot(attn, w_out, preferred_element_type=f32)
    per_dev = rows // n_seq
    out_proj = seq_sum(partial_out.reshape(n_seq, per_dev, -1))
    out_sq = lax.psum(jnp.sum(out_proj * out_proj, -1), "head")
    x_all = step_tokens.reshape(rows, -1)
    x_f = lax.dynamic_slice_in_dim(x_all, seq_at * per_dev, per_dev, 0).astype(f32)
    state = (x_f + out_proj * lax.rsqrt(out_sq / D + EPS)[:, None] * post_gain).astype(bf16)
    state_all = seq_gather(state).reshape(rows, -1)
    state_f = state_all.astype(f32)
    scaled_two = (state_f * ffn_gain).astype(bf16)
    gate_part = jnp.dot(scaled_two, w_gate, preferred_element_type=f32)
    up_part = jnp.dot(scaled_two, w_up, preferred_element_type=f32)
    hidden = gate_part.shape[1]
    head_rows = rows // n_head
    packed = jnp.concatenate(
        [gate_part, up_part, jnp.pad(jnp.sum(state_f * state_f, -1)[:, None], ((0, 0), (0, 127)))],
        1,
    )
    packed = exchange_sum(packed.reshape(n_head, head_rows, -1), "head")
    norm_s = lax.rsqrt(packed[:, 2 * hidden] / D + EPS)[:, None]
    inner = (
        jax.nn.gelu(packed[:, :hidden] * norm_s, approximate=True)
        * (packed[:, hidden : 2 * hidden] * norm_s)
    ).astype(bf16)
    inner = exchange_gather(inner, "head", n_head).reshape(rows, hidden)
    ffn_out = seq_sum(jnp.dot(inner, w_down, preferred_element_type=f32).reshape(n_seq, per_dev, -1))
    ffn_sq = lax.psum(jnp.sum(ffn_out * ffn_out, -1), "head")
    result = (
        state.astype(f32) + ffn_out * lax.rsqrt(ffn_sq / D + EPS)[:, None] * final_gain
    ).astype(bf16)
    result = seq_gather(result)
    return result.reshape(steps, groups, beams, -1)


def solution(mesh):
    devices = mesh.devices
    fine = jax.sharding.Mesh(
        devices.reshape(devices.shape[0] // 2, 2, devices.shape[1]), ("seq", "pair", "head")
    )
    return jax.shard_map(
        shards,
        mesh=fine,
        in_specs=(
            P(None, None, None, "head"),
            P(),
            P(None, "head", SEQ, None),
            P(),
            P(None, ALL, None),
            P(),
            P(None, SEQ, "head"),
            P(),
            P("head"),
            P("head", SEQ),
            P("head", SEQ),
            P(),
            P(),
            P(SEQ, "head"),
            P("head"),
            P("head"),
            P("head", SEQ),
            P("head", SEQ),
            P(SEQ, "head"),
            P("head"),
        ),
        out_specs=P(None, None, None, "head"),
        check_vma=False,
    )
```

```python
import jax
import jax.numpy as jnp
from jax import lax
from jax.sharding import PartitionSpec as P

D = 2560
QH = 8
KVH = 4
HD = 256
QD = 2048


SEQ = ("seq", "pair")
ALL = ("seq", "pair", "head")

EPS = 1e-06
NEG = -1e30
QSCALE = 0.0625


def norm_heads(values, gain, scale):
    shaped = values.reshape(values.shape[:-1] + (-1, gain.shape[0]))
    shaped = shaped * lax.rsqrt(jnp.mean(shaped * shaped, -1, keepdims=True) + EPS) * gain * scale
    return shaped.reshape(values.shape)


def finish_keys(pairs, k_gain):
    half = pairs.shape[-1] // 2
    keys = norm_heads(pairs[..., :half], k_gain, 1.0)
    return jnp.concatenate([keys, pairs[..., half:]], -1).astype(jnp.bfloat16)


def split_pairs(pairs):
    half = pairs.shape[-1] // 2
    keys = pairs[..., :half].reshape(pairs.shape[:-1] + (KVH, HD))
    values = pairs[..., half:].reshape(pairs.shape[:-1] + (KVH, HD))
    return (keys, values)


def lane_shape(shape):
    size = 1
    for n in shape:
        size = size * n
    return shape if size % 128 else (size // 128, 128)


def exchange_sum(parts, axes, align=False):
    shape = lane_shape(parts.shape[1:]) if align else parts.shape[1:]
    moved = lax.all_to_all(parts.reshape((parts.shape[0],) + shape), axes, 0, 0, tiled=True)
    return jnp.sum(moved, 0).reshape(parts.shape[1:])


def exchange_max(value, axes, count):
    flat = value.reshape(-1, 128)
    spread = jnp.broadcast_to(flat[None], (count,) + flat.shape)
    return jnp.max(lax.all_to_all(spread, axes, 0, 0, tiled=True), 0).reshape(value.shape)


def exchange_gather(piece, axes, count, align=False):
    flat = piece.reshape(lane_shape(piece.shape)) if align else piece
    spread = jnp.broadcast_to(flat[None], (count,) + flat.shape)
    return lax.all_to_all(spread, axes, 0, 0, tiled=True).reshape((count,) + piece.shape)


def seq_sum(parts):
    pair = lax.axis_size("pair")
    parts = parts.reshape((parts.shape[0] // pair, pair) + parts.shape[1:])
    parts = exchange_sum(jnp.swapaxes(parts, 0, 1), "pair")
    return exchange_sum(parts, "seq", True)


def seq_gather(piece):
    pair = lax.axis_size("pair")
    outer = lax.axis_size("seq")
    got = exchange_gather(exchange_gather(piece, "seq", outer, True), "pair", pair)
    return jnp.swapaxes(got, 0, 1).reshape((outer * pair,) + piece.shape)


def project_tokens(tokens, in_gain, w_query, w_keyval, q_gain, k_gain):
    flat = tokens.reshape(-1, tokens.shape[-1]).astype(jnp.float32)
    scaled = (flat * in_gain).astype(jnp.bfloat16)
    q_part = jnp.dot(scaled, w_query, preferred_element_type=jnp.float32)
    kv_part = jnp.dot(scaled, w_keyval, preferred_element_type=jnp.float32)
    squares = jnp.sum(flat * flat, -1)
    n_head = lax.axis_size("head")
    n_seq = lax.axis_size("seq") * lax.axis_size("pair")
    rows = flat.shape[0]
    half = rows // n_head
    block = q_part.shape[1]
    packed = jnp.concatenate([q_part, kv_part, jnp.pad(squares[:, None], ((0, 0), (0, 127)))], 1)
    packed = exchange_sum(packed.reshape(n_head, half, -1), "head")
    factor = lax.rsqrt(packed[:, 2 * block] / D + EPS)[:, None]
    q_raw = (packed[:, :block] * factor).astype(jnp.bfloat16)
    kv_raw = (packed[:, block : 2 * block] * factor).astype(jnp.bfloat16)
    both = exchange_gather(
        jnp.concatenate([q_raw, kv_raw], 1), ALL, n_seq * n_head
    ).reshape(n_seq, n_head, half, 2 * block)
    both = jnp.transpose(both, (1, 2, 0, 3)).reshape(rows, n_seq, 2 * block)
    q_raw = both[:, :, :block].reshape(rows, -1)
    kv_raw = both[:, :, block:].reshape(rows, -1)
    queries = norm_heads(q_raw.astype(jnp.float32), q_gain, QSCALE).astype(jnp.bfloat16)
    fresh = finish_keys(kv_raw.astype(jnp.float32), k_gain)
    return (queries, fresh)


def shards(
    step_tokens,
    parents,
    tail_cache,
    tail_len,
    cache,
    cache_len,
    prompt_states,
    prompt_len,
    in_gain,
    w_query,
    w_keyval,
    q_gain,
    k_gain,
    w_out,
    post_gain,
    ffn_gain,
    w_gate,
    w_up,
    w_down,
    final_gain,
):
    f32 = jnp.float32
    bf16 = jnp.bfloat16
    n_head = lax.axis_size("head")
    n_seq = lax.axis_size("seq") * lax.axis_size("pair")
    seq_at = lax.axis_index("seq") * lax.axis_size("pair") + lax.axis_index("pair")
    head_at = lax.axis_index("head")
    flat_at = seq_at * n_head + head_at
    steps, groups, beams, width = step_tokens.shape
    pre = prompt_states.shape[0]
    repeat = QH // KVH
    rows = jnp.transpose(prompt_states, (1, 0, 2)).astype(f32)
    prompt_scaled = (rows * in_gain).astype(bf16).reshape(-1, width)
    prompt_squares = jnp.sum(rows * rows, -1).reshape(-1)
    prompt_terms = jnp.dot(
        prompt_scaled,
        lax.all_gather(w_keyval, SEQ, axis=1, tiled=True),
        preferred_element_type=f32,
    )
    prompt_sum, prompt_sq = (
        lax.psum_scatter(prompt_terms, "head", scatter_dimension=0, tiled=True),
        lax.psum_scatter(prompt_squares, "head", scatter_dimension=0, tiled=True),
    )
    prompt_pairs = finish_keys(prompt_sum * lax.rsqrt(prompt_sq / D + EPS)[:, None], k_gain)
    prompt_seg = prompt_pairs.shape[0] // pre
    prompt_pairs = jnp.transpose(prompt_pairs.reshape(prompt_seg, pre, -1), (1, 0, 2))
    prompt_ok = (flat_at * prompt_seg + jnp.arange(prompt_seg))[None, :] < prompt_len[:, None]
    cache_seg = cache.shape[1]
    cache_ok = (flat_at * cache_seg + jnp.arange(cache_seg))[None, :] < cache_len[:, None]
    span = max(prompt_seg, cache_seg)
    shared = jnp.concatenate(
        [
            jnp.pad(prompt_pairs, ((0, 0), (0, span - prompt_seg), (0, 0))),
            jnp.pad(cache, ((0, 0), (0, span - cache_seg), (0, 0))),
        ],
        0,
    )
    shared_ok = jnp.concatenate(
        [
            jnp.pad(prompt_ok, ((0, 0), (0, span - prompt_seg))),
            jnp.pad(cache_ok, ((0, 0), (0, span - cache_seg))),
        ],
        0,
    )
    shared_keys, shared_values = split_pairs(shared)
    tail_seg = tail_cache.shape[2]
    local_beams = tail_cache.shape[1]
    offset = (seq_at * tail_seg + jnp.arange(tail_seg))[None, :] - tail_len[:, None]
    all_beams = jnp.arange(beams)
    every_query, every_fresh = project_tokens(
        step_tokens, in_gain, w_query, w_keyval, q_gain, k_gain
    )
    every_query = every_query.reshape(steps, groups, beams, -1)
    every_fresh = every_fresh.reshape(steps, groups, beams, -1)
    everyone = lax.all_gather(tail_cache, "head", axis=1, tiled=True)
    n_dev = n_seq * n_head
    first_beam = head_at * local_beams
    many = steps * beams * repeat
    grouped = jnp.transpose(
        every_query.reshape(steps, groups, beams, KVH, repeat, HD), (1, 3, 0, 2, 4, 5)
    ).reshape(groups, KVH, many, HD)
    source = jnp.broadcast_to(all_beams[None, :], (groups, beams))
    ancestors = []
    tail_states = []
    for step in range(steps):
        link = parents[step]
        source = jnp.take_along_axis(source, link, axis=1)
        ancestors = [jnp.take_along_axis(a, link, axis=1) for a in ancestors]
        ancestors.append(jnp.broadcast_to(all_beams[None, :], (groups, beams)))
        picks = lax.dynamic_slice_in_dim(source, first_beam, local_beams, 1)
        tail_state = jnp.take_along_axis(everyone, picks[:, :, None, None], axis=1)
        for back, anc in enumerate(ancestors):
            mine = lax.dynamic_slice_in_dim(anc, first_beam, local_beams, 1)
            written = jnp.take_along_axis(every_fresh[back], mine[:, :, None], axis=1)
            tail_state = jnp.where(
                (offset == back)[:, None, :, None], written[:, :, None, :], tail_state
            )
        tail_states.append(tail_state)
    tails = jnp.stack(tail_states, 1).reshape(groups, steps * local_beams * tail_seg, -1)
    all_keys, all_values = split_pairs(jnp.concatenate([shared, tails], 1))
    step_id = jnp.arange(steps)
    same_step = step_id[:, None, None, None, None, None] == step_id[None, None, None, :, None, None]
    same_beam = (
        all_beams[None, :, None, None, None, None]
        == (first_beam + jnp.arange(local_beams))[None, None, None, None, :, None]
    )
    live = offset[:, None, None, None, None, None, :] <= step_id[None, None, None, None, :, None, None]
    tail_mask = jnp.broadcast_to(
        (same_step & same_beam)[None] & live,
        (groups, steps, beams, repeat, steps, local_beams, tail_seg),
    ).reshape(groups, many, -1)
    mask = jnp.concatenate(
        [jnp.broadcast_to(shared_ok[:, None, :], (groups, many, span)), tail_mask], -1
    )[:, None]
    scores = jnp.einsum("gkmd,gtkd->gkmt", grouped, all_keys, preferred_element_type=f32)
    scores = jnp.where(mask, scores, NEG)
    top = jnp.max(scores, -1).reshape(groups, KVH, steps, beams, repeat)
    top = exchange_max(top, ALL, n_dev)
    weights = jnp.where(mask, jnp.exp(scores - top.reshape(groups, KVH, many)[..., None]), 0.0)
    total = jnp.sum(weights, -1).reshape(groups, KVH, steps, beams, repeat)
    weighted = jnp.einsum(
        "gkmt,gtkd->gkmd", weights.astype(bf16), all_values, preferred_element_type=f32
    ).reshape(groups, KVH, steps, beams, repeat, HD)
    rows = steps * groups * beams
    piece = QD // n_dev
    per_head = HD // piece
    weighted = jnp.transpose(
        weighted.reshape(groups, KVH, steps, beams, repeat, per_head, piece), (1, 4, 5, 2, 0, 3, 6)
    ).reshape(n_dev, -1)
    total = jnp.repeat(jnp.transpose(total, (1, 4, 2, 0, 3)).reshape(QH, rows), per_head, 0)
    lanes = -(-rows // 128) * 128
    packed = jnp.concatenate([weighted, jnp.pad(total, ((0, 0), (0, lanes - rows)))], 1)
    pair = lax.axis_size("pair")
    packed = packed.reshape(n_seq // pair, pair, n_head, -1, 128)
    packed = exchange_sum(jnp.swapaxes(packed, 0, 1), "pair").reshape(n_dev // pair, -1, 128)
    packed = exchange_sum(packed, ("seq", "head")).reshape(-1)
    share = packed[: rows * piece].reshape(rows, piece)
    own_total = packed[rows * piece : rows * piece + rows]
    attn = (share / own_total[:, None]).astype(bf16)
    attn = exchange_gather(attn, "head", n_head)
    attn = jnp.transpose(attn, (1, 0, 2)).reshape(rows, -1)
    partial_out = jnp.dot(attn, w_out, preferred_element_type=f32)
    per_dev = rows // n_seq
    out_proj = seq_sum(partial_out.reshape(n_seq, per_dev, -1))
    out_sq = lax.psum(jnp.sum(out_proj * out_proj, -1), "head")
    x_all = step_tokens.reshape(rows, -1)
    x_f = lax.dynamic_slice_in_dim(x_all, seq_at * per_dev, per_dev, 0).astype(f32)
    state = (x_f + out_proj * lax.rsqrt(out_sq / D + EPS)[:, None] * post_gain).astype(bf16)
    state_all = seq_gather(state).reshape(rows, -1)
    state_f = state_all.astype(f32)
    scaled_two = (state_f * ffn_gain).astype(bf16)
    gate_part = jnp.dot(scaled_two, w_gate, preferred_element_type=f32)
    up_part = jnp.dot(scaled_two, w_up, preferred_element_type=f32)
    hidden = gate_part.shape[1]
    head_rows = rows // n_head
    packed = jnp.concatenate(
        [gate_part, up_part, jnp.pad(jnp.sum(state_f * state_f, -1)[:, None], ((0, 0), (0, 127)))],
        1,
    )
    packed = exchange_sum(packed.reshape(n_head, head_rows, -1), "head")
    norm_s = lax.rsqrt(packed[:, 2 * hidden] / D + EPS)[:, None]
    inner = (
        jax.nn.gelu(packed[:, :hidden] * norm_s, approximate=True)
        * (packed[:, hidden : 2 * hidden] * norm_s)
    ).astype(bf16)
    inner = exchange_gather(inner, "head", n_head).reshape(rows, hidden)
    ffn_out = seq_sum(jnp.dot(inner, w_down, preferred_element_type=f32).reshape(n_seq, per_dev, -1))
    ffn_sq = lax.psum(jnp.sum(ffn_out * ffn_out, -1), "head")
    result = (
        state.astype(f32) + ffn_out * lax.rsqrt(ffn_sq / D + EPS)[:, None] * final_gain
    ).astype(bf16)
    result = seq_gather(result)
    return result.reshape(steps, groups, beams, -1)


def solution(mesh):
    devices = mesh.devices
    fine = jax.sharding.Mesh(
        devices.reshape(devices.shape[0] // 2, 2, devices.shape[1]), ("seq", "pair", "head")
    )
    return jax.shard_map(
        shards,
        mesh=fine,
        in_specs=(
            P(None, None, None, "head"),
            P(),
            P(None, "head", SEQ, None),
            P(),
            P(None, ALL, None),
            P(),
            P(None, SEQ, "head"),
            P(),
            P("head"),
            P("head", SEQ),
            P("head", SEQ),
            P(),
            P(),
            P(SEQ, "head"),
            P("head"),
            P("head"),
            P("head", SEQ),
            P("head", SEQ),
            P(SEQ, "head"),
            P("head"),
        ),
        out_specs=P(None, None, None, "head"),
        check_vma=False,
    )
```

```python
import jax
import jax.numpy as jnp
from jax import lax
from jax.sharding import PartitionSpec as P

D = 2560
QH = 8
KVH = 4
HD = 256
QD = 2048


SEQ = ("seq", "pair")
ALL = ("seq", "pair", "head")

EPS = 1e-06
NEG = -1e30
QSCALE = 0.0625


def norm_heads(values, gain, scale):
    shaped = values.reshape(values.shape[:-1] + (-1, gain.shape[0]))
    shaped = shaped * lax.rsqrt(jnp.mean(shaped * shaped, -1, keepdims=True) + EPS) * gain * scale
    return shaped.reshape(values.shape)


def finish_keys(pairs, k_gain):
    half = pairs.shape[-1] // 2
    keys = norm_heads(pairs[..., :half], k_gain, 1.0)
    return jnp.concatenate([keys, pairs[..., half:]], -1).astype(jnp.bfloat16)


def split_pairs(pairs):
    half = pairs.shape[-1] // 2
    keys = pairs[..., :half].reshape(pairs.shape[:-1] + (KVH, HD))
    values = pairs[..., half:].reshape(pairs.shape[:-1] + (KVH, HD))
    return (keys, values)


def lane_shape(shape):
    size = 1
    for n in shape:
        size = size * n
    return shape if size % 128 else (size // 128, 128)


def exchange_sum(parts, axes, align=False):
    shape = lane_shape(parts.shape[1:]) if align else parts.shape[1:]
    moved = lax.all_to_all(parts.reshape((parts.shape[0],) + shape), axes, 0, 0, tiled=True)
    return jnp.sum(moved, 0).reshape(parts.shape[1:])


def exchange_max(value, axes, count):
    flat = value.reshape(-1, 128)
    spread = jnp.broadcast_to(flat[None], (count,) + flat.shape)
    return jnp.max(lax.all_to_all(spread, axes, 0, 0, tiled=True), 0).reshape(value.shape)


def exchange_gather(piece, axes, count, align=False):
    flat = piece.reshape(lane_shape(piece.shape)) if align else piece
    spread = jnp.broadcast_to(flat[None], (count,) + flat.shape)
    return lax.all_to_all(spread, axes, 0, 0, tiled=True).reshape((count,) + piece.shape)


def seq_sum(parts):
    pair = lax.axis_size("pair")
    parts = parts.reshape((parts.shape[0] // pair, pair) + parts.shape[1:])
    parts = exchange_sum(jnp.swapaxes(parts, 0, 1), "pair")
    return exchange_sum(parts, "seq", True)


def seq_gather(piece):
    pair = lax.axis_size("pair")
    outer = lax.axis_size("seq")
    got = exchange_gather(exchange_gather(piece, "seq", outer, True), "pair", pair)
    return jnp.swapaxes(got, 0, 1).reshape((outer * pair,) + piece.shape)


def project_tokens(tokens, in_gain, w_query, w_keyval, q_gain, k_gain):
    flat = tokens.reshape(-1, tokens.shape[-1]).astype(jnp.float32)
    scaled = (flat * in_gain).astype(jnp.bfloat16)
    q_part = jnp.dot(scaled, w_query, preferred_element_type=jnp.float32)
    kv_part = jnp.dot(scaled, w_keyval, preferred_element_type=jnp.float32)
    squares = jnp.sum(flat * flat, -1)
    n_head = lax.axis_size("head")
    n_seq = lax.axis_size("seq") * lax.axis_size("pair")
    rows = flat.shape[0]
    half = rows // n_head
    block = q_part.shape[1]
    packed = jnp.concatenate([q_part, kv_part, jnp.pad(squares[:, None], ((0, 0), (0, 127)))], 1)
    packed = exchange_sum(packed.reshape(n_head, half, -1), "head")
    factor = lax.rsqrt(packed[:, 2 * block] / D + EPS)[:, None]
    q_raw = (packed[:, :block] * factor).astype(jnp.bfloat16)
    kv_raw = (packed[:, block : 2 * block] * factor).astype(jnp.bfloat16)
    both = exchange_gather(
        jnp.concatenate([q_raw, kv_raw], 1), ALL, n_seq * n_head
    ).reshape(n_seq, n_head, half, 2 * block)
    both = jnp.transpose(both, (1, 2, 0, 3)).reshape(rows, n_seq, 2 * block)
    q_raw = both[:, :, :block].reshape(rows, -1)
    kv_raw = both[:, :, block:].reshape(rows, -1)
    queries = norm_heads(q_raw.astype(jnp.float32), q_gain, QSCALE).astype(jnp.bfloat16)
    fresh = finish_keys(kv_raw.astype(jnp.float32), k_gain)
    return (queries, fresh)


def shards(
    step_tokens,
    parents,
    tail_cache,
    tail_len,
    cache,
    cache_len,
    prompt_states,
    prompt_len,
    in_gain,
    w_query,
    w_keyval,
    q_gain,
    k_gain,
    w_out,
    post_gain,
    ffn_gain,
    w_gate,
    w_up,
    w_down,
    final_gain,
):
    f32 = jnp.float32
    bf16 = jnp.bfloat16
    n_head = lax.axis_size("head")
    n_seq = lax.axis_size("seq") * lax.axis_size("pair")
    seq_at = lax.axis_index("seq") * lax.axis_size("pair") + lax.axis_index("pair")
    head_at = lax.axis_index("head")
    flat_at = seq_at * n_head + head_at
    steps, groups, beams, width = step_tokens.shape
    pre = prompt_states.shape[0]
    repeat = QH // KVH
    rows = jnp.transpose(prompt_states, (1, 0, 2)).astype(f32)
    prompt_scaled = (rows * in_gain).astype(bf16).reshape(-1, width)
    prompt_squares = jnp.sum(rows * rows, -1).reshape(-1)
    prompt_terms = jnp.dot(
        prompt_scaled,
        lax.all_gather(w_keyval, SEQ, axis=1, tiled=True),
        preferred_element_type=f32,
    )
    prompt_sum, prompt_sq = (
        lax.psum_scatter(prompt_terms, "head", scatter_dimension=0, tiled=True),
        lax.psum_scatter(prompt_squares, "head", scatter_dimension=0, tiled=True),
    )
    prompt_pairs = finish_keys(prompt_sum * lax.rsqrt(prompt_sq / D + EPS)[:, None], k_gain)
    prompt_seg = prompt_pairs.shape[0] // pre
    prompt_pairs = jnp.transpose(prompt_pairs.reshape(prompt_seg, pre, -1), (1, 0, 2))
    prompt_ok = (flat_at * prompt_seg + jnp.arange(prompt_seg))[None, :] < prompt_len[:, None]
    cache_seg = cache.shape[1]
    cache_ok = (flat_at * cache_seg + jnp.arange(cache_seg))[None, :] < cache_len[:, None]
    span = max(prompt_seg, cache_seg)
    shared = jnp.concatenate(
        [
            jnp.pad(prompt_pairs, ((0, 0), (0, span - prompt_seg), (0, 0))),
            jnp.pad(cache, ((0, 0), (0, span - cache_seg), (0, 0))),
        ],
        0,
    )
    shared_ok = jnp.concatenate(
        [
            jnp.pad(prompt_ok, ((0, 0), (0, span - prompt_seg))),
            jnp.pad(cache_ok, ((0, 0), (0, span - cache_seg))),
        ],
        0,
    )
    shared_keys, shared_values = split_pairs(shared)
    tail_seg = tail_cache.shape[2]
    local_beams = tail_cache.shape[1]
    offset = (seq_at * tail_seg + jnp.arange(tail_seg))[None, :] - tail_len[:, None]
    all_beams = jnp.arange(beams)
    every_query, every_fresh = project_tokens(
        step_tokens, in_gain, w_query, w_keyval, q_gain, k_gain
    )
    every_query = every_query.reshape(steps, groups, beams, -1)
    every_fresh = every_fresh.reshape(steps, groups, beams, -1)
    everyone = lax.all_gather(tail_cache, "head", axis=1, tiled=True)
    n_dev = n_seq * n_head
    first_beam = head_at * local_beams
    many = steps * beams * repeat
    grouped = jnp.transpose(
        every_query.reshape(steps, groups, beams, KVH, repeat, HD), (1, 3, 0, 2, 4, 5)
    ).reshape(groups, KVH, many, HD)
    source = jnp.broadcast_to(all_beams[None, :], (groups, beams))
    ancestors = []
    tail_states = []
    for step in range(steps):
        link = parents[step]
        source = jnp.take_along_axis(source, link, axis=1)
        ancestors = [jnp.take_along_axis(a, link, axis=1) for a in ancestors]
        ancestors.append(jnp.broadcast_to(all_beams[None, :], (groups, beams)))
        picks = lax.dynamic_slice_in_dim(source, first_beam, local_beams, 1)
        tail_state = jnp.take_along_axis(everyone, picks[:, :, None, None], axis=1)
        for back, anc in enumerate(ancestors):
            mine = lax.dynamic_slice_in_dim(anc, first_beam, local_beams, 1)
            written = jnp.take_along_axis(every_fresh[back], mine[:, :, None], axis=1)
            tail_state = jnp.where(
                (offset == back)[:, None, :, None], written[:, :, None, :], tail_state
            )
        tail_states.append(tail_state)
    tails = jnp.stack(tail_states, 1).reshape(groups, steps * local_beams * tail_seg, -1)
    all_keys, all_values = split_pairs(jnp.concatenate([shared, tails], 1))
    step_id = jnp.arange(steps)
    same_step = step_id[:, None, None, None, None, None] == step_id[None, None, None, :, None, None]
    same_beam = (
        all_beams[None, :, None, None, None, None]
        == (first_beam + jnp.arange(local_beams))[None, None, None, None, :, None]
    )
    live = offset[:, None, None, None, None, None, :] <= step_id[None, None, None, None, :, None, None]
    tail_mask = jnp.broadcast_to(
        (same_step & same_beam)[None] & live,
        (groups, steps, beams, repeat, steps, local_beams, tail_seg),
    ).reshape(groups, many, -1)
    mask = jnp.concatenate(
        [jnp.broadcast_to(shared_ok[:, None, :], (groups, many, span)), tail_mask], -1
    )[:, None]
    scores = jnp.einsum("gkmd,gtkd->gkmt", grouped, all_keys, preferred_element_type=f32)
    scores = jnp.where(mask, scores, NEG)
    top = jnp.max(scores, -1).reshape(groups, KVH, steps, beams, repeat)
    top = exchange_max(top, ALL, n_dev)
    weights = jnp.where(mask, jnp.exp(scores - top.reshape(groups, KVH, many)[..., None]), 0.0)
    total = jnp.sum(weights, -1).reshape(groups, KVH, steps, beams, repeat)
    weighted = jnp.einsum(
        "gkmt,gtkd->gkmd", weights.astype(bf16), all_values, preferred_element_type=f32
    ).reshape(groups, KVH, steps, beams, repeat, HD)
    rows = steps * groups * beams
    piece = QD // n_dev
    per_head = HD // piece
    weighted = jnp.transpose(
        weighted.reshape(groups, KVH, steps, beams, repeat, per_head, piece), (1, 4, 5, 2, 0, 3, 6)
    ).reshape(n_dev, -1)
    total = jnp.repeat(jnp.transpose(total, (1, 4, 2, 0, 3)).reshape(QH, rows), per_head, 0)
    lanes = -(-rows // 128) * 128
    packed = jnp.concatenate([weighted, jnp.pad(total, ((0, 0), (0, lanes - rows)))], 1)
    pair = lax.axis_size("pair")
    packed = packed.reshape(n_seq // pair, pair, n_head, -1, 128)
    packed = exchange_sum(jnp.swapaxes(packed, 0, 1), "pair").reshape(n_dev // pair, -1, 128)
    packed = exchange_sum(packed, ("seq", "head")).reshape(-1)
    share = packed[: rows * piece].reshape(rows, piece)
    own_total = packed[rows * piece : rows * piece + rows]
    attn = (share / own_total[:, None]).astype(bf16)
    attn = exchange_gather(attn, "head", n_head, True)
    attn = jnp.transpose(attn, (1, 0, 2)).reshape(rows, -1)
    partial_out = jnp.dot(attn, w_out, preferred_element_type=f32)
    per_dev = rows // n_seq
    out_proj = seq_sum(partial_out.reshape(n_seq, per_dev, -1))
    out_sq = lax.psum(jnp.sum(out_proj * out_proj, -1), "head")
    x_all = step_tokens.reshape(rows, -1)
    x_f = lax.dynamic_slice_in_dim(x_all, seq_at * per_dev, per_dev, 0).astype(f32)
    state = (x_f + out_proj * lax.rsqrt(out_sq / D + EPS)[:, None] * post_gain).astype(bf16)
    state_all = seq_gather(state).reshape(rows, -1)
    state_f = state_all.astype(f32)
    scaled_two = (state_f * ffn_gain).astype(bf16)
    gate_part = jnp.dot(scaled_two, w_gate, preferred_element_type=f32)
    up_part = jnp.dot(scaled_two, w_up, preferred_element_type=f32)
    hidden = gate_part.shape[1]
    head_rows = rows // n_head
    packed = jnp.concatenate(
        [gate_part, up_part, jnp.pad(jnp.sum(state_f * state_f, -1)[:, None], ((0, 0), (0, 127)))],
        1,
    )
    packed = exchange_sum(packed.reshape(n_head, head_rows, -1), "head")
    norm_s = lax.rsqrt(packed[:, 2 * hidden] / D + EPS)[:, None]
    inner = (
        jax.nn.gelu(packed[:, :hidden] * norm_s, approximate=True)
        * (packed[:, hidden : 2 * hidden] * norm_s)
    ).astype(bf16)
    inner = exchange_gather(inner, "head", n_head).reshape(rows, hidden)
    ffn_out = seq_sum(jnp.dot(inner, w_down, preferred_element_type=f32).reshape(n_seq, per_dev, -1))
    ffn_sq = lax.psum(jnp.sum(ffn_out * ffn_out, -1), "head")
    result = (
        state.astype(f32) + ffn_out * lax.rsqrt(ffn_sq / D + EPS)[:, None] * final_gain
    ).astype(bf16)
    result = seq_gather(result)
    return result.reshape(steps, groups, beams, -1)


def solution(mesh):
    devices = mesh.devices
    fine = jax.sharding.Mesh(
        devices.reshape(devices.shape[0] // 2, 2, devices.shape[1]), ("seq", "pair", "head")
    )
    return jax.shard_map(
        shards,
        mesh=fine,
        in_specs=(
            P(None, None, None, "head"),
            P(),
            P(None, "head", SEQ, None),
            P(),
            P(None, ALL, None),
            P(),
            P(None, SEQ, "head"),
            P(),
            P("head"),
            P("head", SEQ),
            P("head", SEQ),
            P(),
            P(),
            P(SEQ, "head"),
            P("head"),
            P("head"),
            P("head", SEQ),
            P("head", SEQ),
            P(SEQ, "head"),
            P("head"),
        ),
        out_specs=P(None, None, None, "head"),
        check_vma=False,
    )
```

```python
import jax
import jax.numpy as jnp
from jax import lax
from jax.sharding import PartitionSpec as P

D = 2560
QH = 8
KVH = 4
HD = 256
QD = 2048


SEQ = ("seq", "pair")
ALL = ("seq", "pair", "head")

EPS = 1e-06
NEG = -1e30
QSCALE = 0.0625


def norm_heads(values, gain, scale):
    shaped = values.reshape(values.shape[:-1] + (-1, gain.shape[0]))
    shaped = shaped * lax.rsqrt(jnp.mean(shaped * shaped, -1, keepdims=True) + EPS) * gain * scale
    return shaped.reshape(values.shape)


def finish_keys(pairs, k_gain):
    half = pairs.shape[-1] // 2
    keys = norm_heads(pairs[..., :half], k_gain, 1.0)
    return jnp.concatenate([keys, pairs[..., half:]], -1).astype(jnp.bfloat16)


def split_pairs(pairs):
    half = pairs.shape[-1] // 2
    keys = pairs[..., :half].reshape(pairs.shape[:-1] + (KVH, HD))
    values = pairs[..., half:].reshape(pairs.shape[:-1] + (KVH, HD))
    return (keys, values)


def lane_shape(shape):
    size = 1
    for n in shape:
        size = size * n
    return shape if size % 128 else (size // 128, 128)


def exchange_sum(parts, axes, align=False):
    shape = lane_shape(parts.shape[1:]) if align else parts.shape[1:]
    moved = lax.all_to_all(parts.reshape((parts.shape[0],) + shape), axes, 0, 0, tiled=True)
    return jnp.sum(moved, 0).reshape(parts.shape[1:])


def exchange_max(value, axes, count):
    flat = value.reshape(-1, 128)
    spread = jnp.broadcast_to(flat[None], (count,) + flat.shape)
    return jnp.max(lax.all_to_all(spread, axes, 0, 0, tiled=True), 0).reshape(value.shape)


def exchange_gather(piece, axes, count, align=False):
    flat = piece.reshape(lane_shape(piece.shape)) if align else piece
    spread = jnp.broadcast_to(flat[None], (count,) + flat.shape)
    return lax.all_to_all(spread, axes, 0, 0, tiled=True).reshape((count,) + piece.shape)


def seq_sum(parts):
    pair = lax.axis_size("pair")
    parts = parts.reshape((parts.shape[0] // pair, pair) + parts.shape[1:])
    parts = exchange_sum(jnp.swapaxes(parts, 0, 1), "pair")
    return exchange_sum(parts, "seq", True)


def seq_gather(piece):
    pair = lax.axis_size("pair")
    outer = lax.axis_size("seq")
    got = exchange_gather(exchange_gather(piece, "seq", outer, True), "pair", pair)
    return jnp.swapaxes(got, 0, 1).reshape((outer * pair,) + piece.shape)


def project_tokens(tokens, in_gain, w_query, w_keyval, q_gain, k_gain):
    flat = tokens.reshape(-1, tokens.shape[-1]).astype(jnp.float32)
    scaled = (flat * in_gain).astype(jnp.bfloat16)
    q_part = jnp.dot(scaled, w_query, preferred_element_type=jnp.float32)
    kv_part = jnp.dot(scaled, w_keyval, preferred_element_type=jnp.float32)
    squares = jnp.sum(flat * flat, -1)
    n_head = lax.axis_size("head")
    n_seq = lax.axis_size("seq") * lax.axis_size("pair")
    rows = flat.shape[0]
    half = rows // n_head
    block = q_part.shape[1]
    packed = jnp.concatenate([q_part, kv_part, jnp.pad(squares[:, None], ((0, 0), (0, 127)))], 1)
    packed = exchange_sum(packed.reshape(n_head, half, -1), "head")
    factor = lax.rsqrt(packed[:, 2 * block] / D + EPS)[:, None]
    q_raw = (packed[:, :block] * factor).astype(jnp.bfloat16)
    kv_raw = (packed[:, block : 2 * block] * factor).astype(jnp.bfloat16)
    both = exchange_gather(
        jnp.concatenate([q_raw, kv_raw], 1), ALL, n_seq * n_head
    ).reshape(n_seq, n_head, half, 2 * block)
    both = jnp.transpose(both, (1, 2, 0, 3)).reshape(rows, n_seq, 2 * block)
    q_raw = both[:, :, :block].reshape(rows, -1)
    kv_raw = both[:, :, block:].reshape(rows, -1)
    queries = norm_heads(q_raw.astype(jnp.float32), q_gain, QSCALE).astype(jnp.bfloat16)
    fresh = finish_keys(kv_raw.astype(jnp.float32), k_gain)
    return (queries, fresh)


def shards(
    step_tokens,
    parents,
    tail_cache,
    tail_len,
    cache,
    cache_len,
    prompt_states,
    prompt_len,
    in_gain,
    w_query,
    w_keyval,
    q_gain,
    k_gain,
    w_out,
    post_gain,
    ffn_gain,
    w_gate,
    w_up,
    w_down,
    final_gain,
):
    f32 = jnp.float32
    bf16 = jnp.bfloat16
    n_head = lax.axis_size("head")
    n_seq = lax.axis_size("seq") * lax.axis_size("pair")
    seq_at = lax.axis_index("seq") * lax.axis_size("pair") + lax.axis_index("pair")
    head_at = lax.axis_index("head")
    flat_at = seq_at * n_head + head_at
    steps, groups, beams, width = step_tokens.shape
    pre = prompt_states.shape[0]
    repeat = QH // KVH
    rows = jnp.transpose(prompt_states, (1, 0, 2)).astype(f32)
    prompt_scaled = (rows * in_gain).astype(bf16).reshape(-1, width)
    prompt_squares = jnp.sum(rows * rows, -1).reshape(-1)
    prompt_terms = jnp.dot(
        prompt_scaled,
        lax.all_gather(w_keyval, SEQ, axis=1, tiled=True),
        preferred_element_type=f32,
    )
    prompt_sum, prompt_sq = (
        lax.psum_scatter(prompt_terms, "head", scatter_dimension=0, tiled=True),
        lax.psum_scatter(prompt_squares, "head", scatter_dimension=0, tiled=True),
    )
    prompt_pairs = finish_keys(prompt_sum * lax.rsqrt(prompt_sq / D + EPS)[:, None], k_gain)
    prompt_seg = prompt_pairs.shape[0] // pre
    prompt_pairs = jnp.transpose(prompt_pairs.reshape(prompt_seg, pre, -1), (1, 0, 2))
    prompt_ok = (flat_at * prompt_seg + jnp.arange(prompt_seg))[None, :] < prompt_len[:, None]
    cache_seg = cache.shape[1]
    cache_ok = (flat_at * cache_seg + jnp.arange(cache_seg))[None, :] < cache_len[:, None]
    span = max(prompt_seg, cache_seg)
    shared = jnp.concatenate(
        [
            jnp.pad(prompt_pairs, ((0, 0), (0, span - prompt_seg), (0, 0))),
            jnp.pad(cache, ((0, 0), (0, span - cache_seg), (0, 0))),
        ],
        0,
    )
    shared_ok = jnp.concatenate(
        [
            jnp.pad(prompt_ok, ((0, 0), (0, span - prompt_seg))),
            jnp.pad(cache_ok, ((0, 0), (0, span - cache_seg))),
        ],
        0,
    )
    shared_keys, shared_values = split_pairs(shared)
    tail_seg = tail_cache.shape[2]
    local_beams = tail_cache.shape[1]
    offset = (seq_at * tail_seg + jnp.arange(tail_seg))[None, :] - tail_len[:, None]
    all_beams = jnp.arange(beams)
    every_query, every_fresh = project_tokens(
        step_tokens, in_gain, w_query, w_keyval, q_gain, k_gain
    )
    every_query = every_query.reshape(steps, groups, beams, -1)
    every_fresh = every_fresh.reshape(steps, groups, beams, -1)
    everyone = exchange_gather(tail_cache, "head", n_head, True)
    everyone = jnp.moveaxis(everyone, 0, 1).reshape(
        (groups, beams) + tail_cache.shape[2:]
    )
    n_dev = n_seq * n_head
    first_beam = head_at * local_beams
    many = steps * beams * repeat
    grouped = jnp.transpose(
        every_query.reshape(steps, groups, beams, KVH, repeat, HD), (1, 3, 0, 2, 4, 5)
    ).reshape(groups, KVH, many, HD)
    source = jnp.broadcast_to(all_beams[None, :], (groups, beams))
    ancestors = []
    tail_states = []
    for step in range(steps):
        link = parents[step]
        source = jnp.take_along_axis(source, link, axis=1)
        ancestors = [jnp.take_along_axis(a, link, axis=1) for a in ancestors]
        ancestors.append(jnp.broadcast_to(all_beams[None, :], (groups, beams)))
        picks = lax.dynamic_slice_in_dim(source, first_beam, local_beams, 1)
        tail_state = jnp.take_along_axis(everyone, picks[:, :, None, None], axis=1)
        for back, anc in enumerate(ancestors):
            mine = lax.dynamic_slice_in_dim(anc, first_beam, local_beams, 1)
            written = jnp.take_along_axis(every_fresh[back], mine[:, :, None], axis=1)
            tail_state = jnp.where(
                (offset == back)[:, None, :, None], written[:, :, None, :], tail_state
            )
        tail_states.append(tail_state)
    tails = jnp.stack(tail_states, 1).reshape(groups, steps * local_beams * tail_seg, -1)
    all_keys, all_values = split_pairs(jnp.concatenate([shared, tails], 1))
    step_id = jnp.arange(steps)
    same_step = step_id[:, None, None, None, None, None] == step_id[None, None, None, :, None, None]
    same_beam = (
        all_beams[None, :, None, None, None, None]
        == (first_beam + jnp.arange(local_beams))[None, None, None, None, :, None]
    )
    live = offset[:, None, None, None, None, None, :] <= step_id[None, None, None, None, :, None, None]
    tail_mask = jnp.broadcast_to(
        (same_step & same_beam)[None] & live,
        (groups, steps, beams, repeat, steps, local_beams, tail_seg),
    ).reshape(groups, many, -1)
    mask = jnp.concatenate(
        [jnp.broadcast_to(shared_ok[:, None, :], (groups, many, span)), tail_mask], -1
    )[:, None]
    scores = jnp.einsum("gkmd,gtkd->gkmt", grouped, all_keys, preferred_element_type=f32)
    scores = jnp.where(mask, scores, NEG)
    top = jnp.max(scores, -1).reshape(groups, KVH, steps, beams, repeat)
    top = exchange_max(top, ALL, n_dev)
    weights = jnp.where(mask, jnp.exp(scores - top.reshape(groups, KVH, many)[..., None]), 0.0)
    total = jnp.sum(weights, -1).reshape(groups, KVH, steps, beams, repeat)
    weighted = jnp.einsum(
        "gkmt,gtkd->gkmd", weights.astype(bf16), all_values, preferred_element_type=f32
    ).reshape(groups, KVH, steps, beams, repeat, HD)
    rows = steps * groups * beams
    piece = QD // n_dev
    per_head = HD // piece
    weighted = jnp.transpose(
        weighted.reshape(groups, KVH, steps, beams, repeat, per_head, piece), (1, 4, 5, 2, 0, 3, 6)
    ).reshape(n_dev, -1)
    total = jnp.repeat(jnp.transpose(total, (1, 4, 2, 0, 3)).reshape(QH, rows), per_head, 0)
    lanes = -(-rows // 128) * 128
    packed = jnp.concatenate([weighted, jnp.pad(total, ((0, 0), (0, lanes - rows)))], 1)
    pair = lax.axis_size("pair")
    packed = packed.reshape(n_seq // pair, pair, n_head, -1, 128)
    packed = exchange_sum(jnp.swapaxes(packed, 0, 1), "pair").reshape(n_dev // pair, -1, 128)
    packed = exchange_sum(packed, ("seq", "head")).reshape(-1)
    share = packed[: rows * piece].reshape(rows, piece)
    own_total = packed[rows * piece : rows * piece + rows]
    attn = (share / own_total[:, None]).astype(bf16)
    attn = exchange_gather(attn, "head", n_head)
    attn = jnp.transpose(attn, (1, 0, 2)).reshape(rows, -1)
    partial_out = jnp.dot(attn, w_out, preferred_element_type=f32)
    per_dev = rows // n_seq
    out_proj = seq_sum(partial_out.reshape(n_seq, per_dev, -1))
    out_sq = lax.psum(jnp.sum(out_proj * out_proj, -1), "head")
    x_all = step_tokens.reshape(rows, -1)
    x_f = lax.dynamic_slice_in_dim(x_all, seq_at * per_dev, per_dev, 0).astype(f32)
    state = (x_f + out_proj * lax.rsqrt(out_sq / D + EPS)[:, None] * post_gain).astype(bf16)
    state_all = seq_gather(state).reshape(rows, -1)
    state_f = state_all.astype(f32)
    scaled_two = (state_f * ffn_gain).astype(bf16)
    gate_part = jnp.dot(scaled_two, w_gate, preferred_element_type=f32)
    up_part = jnp.dot(scaled_two, w_up, preferred_element_type=f32)
    hidden = gate_part.shape[1]
    head_rows = rows // n_head
    packed = jnp.concatenate(
        [gate_part, up_part, jnp.pad(jnp.sum(state_f * state_f, -1)[:, None], ((0, 0), (0, 127)))],
        1,
    )
    packed = exchange_sum(packed.reshape(n_head, head_rows, -1), "head")
    norm_s = lax.rsqrt(packed[:, 2 * hidden] / D + EPS)[:, None]
    inner = (
        jax.nn.gelu(packed[:, :hidden] * norm_s, approximate=True)
        * (packed[:, hidden : 2 * hidden] * norm_s)
    ).astype(bf16)
    inner = exchange_gather(inner, "head", n_head).reshape(rows, hidden)
    ffn_out = seq_sum(jnp.dot(inner, w_down, preferred_element_type=f32).reshape(n_seq, per_dev, -1))
    ffn_sq = lax.psum(jnp.sum(ffn_out * ffn_out, -1), "head")
    result = (
        state.astype(f32) + ffn_out * lax.rsqrt(ffn_sq / D + EPS)[:, None] * final_gain
    ).astype(bf16)
    result = seq_gather(result)
    return result.reshape(steps, groups, beams, -1)


def solution(mesh):
    devices = mesh.devices
    fine = jax.sharding.Mesh(
        devices.reshape(devices.shape[0] // 2, 2, devices.shape[1]), ("seq", "pair", "head")
    )
    return jax.shard_map(
        shards,
        mesh=fine,
        in_specs=(
            P(None, None, None, "head"),
            P(),
            P(None, "head", SEQ, None),
            P(),
            P(None, ALL, None),
            P(),
            P(None, SEQ, "head"),
            P(),
            P("head"),
            P("head", SEQ),
            P("head", SEQ),
            P(),
            P(),
            P(SEQ, "head"),
            P("head"),
            P("head"),
            P("head", SEQ),
            P("head", SEQ),
            P(SEQ, "head"),
            P("head"),
        ),
        out_specs=P(None, None, None, "head"),
        check_vma=False,
    )
```

```python
import jax
import jax.numpy as jnp
from jax import lax
from jax.sharding import PartitionSpec as P

D = 2560
QH = 8
KVH = 4
HD = 256
QD = 2048


SEQ = ("seq", "pair")
ALL = ("seq", "pair", "head")

EPS = 1e-06
NEG = -1e30
QSCALE = 0.0625


def norm_heads(values, gain, scale):
    shaped = values.reshape(values.shape[:-1] + (-1, gain.shape[0]))
    shaped = shaped * lax.rsqrt(jnp.mean(shaped * shaped, -1, keepdims=True) + EPS) * gain * scale
    return shaped.reshape(values.shape)


def finish_keys(pairs, k_gain):
    half = pairs.shape[-1] // 2
    keys = norm_heads(pairs[..., :half], k_gain, 1.0)
    return jnp.concatenate([keys, pairs[..., half:]], -1).astype(jnp.bfloat16)


def split_pairs(pairs):
    half = pairs.shape[-1] // 2
    keys = pairs[..., :half].reshape(pairs.shape[:-1] + (KVH, HD))
    values = pairs[..., half:].reshape(pairs.shape[:-1] + (KVH, HD))
    return (keys, values)


def lane_shape(shape):
    size = 1
    for n in shape:
        size = size * n
    return shape if size % 128 else (size // 128, 128)


def exchange_sum(parts, axes, align=False):
    shape = lane_shape(parts.shape[1:]) if align else parts.shape[1:]
    moved = lax.all_to_all(parts.reshape((parts.shape[0],) + shape), axes, 0, 0, tiled=True)
    return jnp.sum(moved, 0).reshape(parts.shape[1:])


def exchange_max(value, axes, count):
    flat = value.reshape(-1, 128)
    spread = jnp.broadcast_to(flat[None], (count,) + flat.shape)
    return jnp.max(lax.all_to_all(spread, axes, 0, 0, tiled=True), 0).reshape(value.shape)


def exchange_gather(piece, axes, count, align=False):
    flat = piece.reshape(lane_shape(piece.shape)) if align else piece
    spread = jnp.broadcast_to(flat[None], (count,) + flat.shape)
    return lax.all_to_all(spread, axes, 0, 0, tiled=True).reshape((count,) + piece.shape)


def seq_sum(parts):
    pair = lax.axis_size("pair")
    parts = parts.reshape((parts.shape[0] // pair, pair) + parts.shape[1:])
    parts = exchange_sum(jnp.swapaxes(parts, 0, 1), "pair")
    return exchange_sum(parts, "seq", True)


def seq_gather(piece):
    pair = lax.axis_size("pair")
    outer = lax.axis_size("seq")
    got = exchange_gather(exchange_gather(piece, "seq", outer, True), "pair", pair)
    return jnp.swapaxes(got, 0, 1).reshape((outer * pair,) + piece.shape)


def gather_columns(weight):
    pair = lax.axis_size("pair")
    outer = lax.axis_size("seq")
    part = lax.all_gather(weight, "seq", axis=1, tiled=True)
    both = exchange_gather(part, "pair", pair).reshape(pair, weight.shape[0], outer, -1)
    return jnp.transpose(both, (1, 2, 0, 3)).reshape(weight.shape[0], -1)


def project_tokens(tokens, in_gain, w_query, w_keyval, q_gain, k_gain):
    flat = tokens.reshape(-1, tokens.shape[-1]).astype(jnp.float32)
    scaled = (flat * in_gain).astype(jnp.bfloat16)
    q_part = jnp.dot(scaled, w_query, preferred_element_type=jnp.float32)
    kv_part = jnp.dot(scaled, w_keyval, preferred_element_type=jnp.float32)
    squares = jnp.sum(flat * flat, -1)
    n_head = lax.axis_size("head")
    n_seq = lax.axis_size("seq") * lax.axis_size("pair")
    rows = flat.shape[0]
    half = rows // n_head
    block = q_part.shape[1]
    packed = jnp.concatenate([q_part, kv_part, jnp.pad(squares[:, None], ((0, 0), (0, 127)))], 1)
    packed = exchange_sum(packed.reshape(n_head, half, -1), "head")
    factor = lax.rsqrt(packed[:, 2 * block] / D + EPS)[:, None]
    q_raw = (packed[:, :block] * factor).astype(jnp.bfloat16)
    kv_raw = (packed[:, block : 2 * block] * factor).astype(jnp.bfloat16)
    both = exchange_gather(
        jnp.concatenate([q_raw, kv_raw], 1), ALL, n_seq * n_head
    ).reshape(n_seq, n_head, half, 2 * block)
    both = jnp.transpose(both, (1, 2, 0, 3)).reshape(rows, n_seq, 2 * block)
    q_raw = both[:, :, :block].reshape(rows, -1)
    kv_raw = both[:, :, block:].reshape(rows, -1)
    queries = norm_heads(q_raw.astype(jnp.float32), q_gain, QSCALE).astype(jnp.bfloat16)
    fresh = finish_keys(kv_raw.astype(jnp.float32), k_gain)
    return (queries, fresh)


def shards(
    step_tokens,
    parents,
    tail_cache,
    tail_len,
    cache,
    cache_len,
    prompt_states,
    prompt_len,
    in_gain,
    w_query,
    w_keyval,
    q_gain,
    k_gain,
    w_out,
    post_gain,
    ffn_gain,
    w_gate,
    w_up,
    w_down,
    final_gain,
):
    f32 = jnp.float32
    bf16 = jnp.bfloat16
    n_head = lax.axis_size("head")
    n_seq = lax.axis_size("seq") * lax.axis_size("pair")
    seq_at = lax.axis_index("seq") * lax.axis_size("pair") + lax.axis_index("pair")
    head_at = lax.axis_index("head")
    flat_at = seq_at * n_head + head_at
    steps, groups, beams, width = step_tokens.shape
    pre = prompt_states.shape[0]
    repeat = QH // KVH
    rows = jnp.transpose(prompt_states, (1, 0, 2)).astype(f32)
    prompt_scaled = (rows * in_gain).astype(bf16).reshape(-1, width)
    prompt_squares = jnp.sum(rows * rows, -1).reshape(-1)
    prompt_terms = jnp.dot(
        prompt_scaled,
        gather_columns(w_keyval),
        preferred_element_type=f32,
    )
    prompt_sum, prompt_sq = (
        lax.psum_scatter(prompt_terms, "head", scatter_dimension=0, tiled=True),
        lax.psum_scatter(prompt_squares, "head", scatter_dimension=0, tiled=True),
    )
    prompt_pairs = finish_keys(prompt_sum * lax.rsqrt(prompt_sq / D + EPS)[:, None], k_gain)
    prompt_seg = prompt_pairs.shape[0] // pre
    prompt_pairs = jnp.transpose(prompt_pairs.reshape(prompt_seg, pre, -1), (1, 0, 2))
    prompt_ok = (flat_at * prompt_seg + jnp.arange(prompt_seg))[None, :] < prompt_len[:, None]
    cache_seg = cache.shape[1]
    cache_ok = (flat_at * cache_seg + jnp.arange(cache_seg))[None, :] < cache_len[:, None]
    span = max(prompt_seg, cache_seg)
    shared = jnp.concatenate(
        [
            jnp.pad(prompt_pairs, ((0, 0), (0, span - prompt_seg), (0, 0))),
            jnp.pad(cache, ((0, 0), (0, span - cache_seg), (0, 0))),
        ],
        0,
    )
    shared_ok = jnp.concatenate(
        [
            jnp.pad(prompt_ok, ((0, 0), (0, span - prompt_seg))),
            jnp.pad(cache_ok, ((0, 0), (0, span - cache_seg))),
        ],
        0,
    )
    shared_keys, shared_values = split_pairs(shared)
    tail_seg = tail_cache.shape[2]
    local_beams = tail_cache.shape[1]
    offset = (seq_at * tail_seg + jnp.arange(tail_seg))[None, :] - tail_len[:, None]
    all_beams = jnp.arange(beams)
    every_query, every_fresh = project_tokens(
        step_tokens, in_gain, w_query, w_keyval, q_gain, k_gain
    )
    every_query = every_query.reshape(steps, groups, beams, -1)
    every_fresh = every_fresh.reshape(steps, groups, beams, -1)
    everyone = lax.all_gather(tail_cache, "head", axis=1, tiled=True)
    n_dev = n_seq * n_head
    first_beam = head_at * local_beams
    many = steps * beams * repeat
    grouped = jnp.transpose(
        every_query.reshape(steps, groups, beams, KVH, repeat, HD), (1, 3, 0, 2, 4, 5)
    ).reshape(groups, KVH, many, HD)
    source = jnp.broadcast_to(all_beams[None, :], (groups, beams))
    ancestors = []
    tail_states = []
    for step in range(steps):
        link = parents[step]
        source = jnp.take_along_axis(source, link, axis=1)
        ancestors = [jnp.take_along_axis(a, link, axis=1) for a in ancestors]
        ancestors.append(jnp.broadcast_to(all_beams[None, :], (groups, beams)))
        picks = lax.dynamic_slice_in_dim(source, first_beam, local_beams, 1)
        tail_state = jnp.take_along_axis(everyone, picks[:, :, None, None], axis=1)
        for back, anc in enumerate(ancestors):
            mine = lax.dynamic_slice_in_dim(anc, first_beam, local_beams, 1)
            written = jnp.take_along_axis(every_fresh[back], mine[:, :, None], axis=1)
            tail_state = jnp.where(
                (offset == back)[:, None, :, None], written[:, :, None, :], tail_state
            )
        tail_states.append(tail_state)
    tails = jnp.stack(tail_states, 1).reshape(groups, steps * local_beams * tail_seg, -1)
    all_keys, all_values = split_pairs(jnp.concatenate([shared, tails], 1))
    step_id = jnp.arange(steps)
    same_step = step_id[:, None, None, None, None, None] == step_id[None, None, None, :, None, None]
    same_beam = (
        all_beams[None, :, None, None, None, None]
        == (first_beam + jnp.arange(local_beams))[None, None, None, None, :, None]
    )
    live = offset[:, None, None, None, None, None, :] <= step_id[None, None, None, None, :, None, None]
    tail_mask = jnp.broadcast_to(
        (same_step & same_beam)[None] & live,
        (groups, steps, beams, repeat, steps, local_beams, tail_seg),
    ).reshape(groups, many, -1)
    mask = jnp.concatenate(
        [jnp.broadcast_to(shared_ok[:, None, :], (groups, many, span)), tail_mask], -1
    )[:, None]
    scores = jnp.einsum("gkmd,gtkd->gkmt", grouped, all_keys, preferred_element_type=f32)
    scores = jnp.where(mask, scores, NEG)
    top = jnp.max(scores, -1).reshape(groups, KVH, steps, beams, repeat)
    top = exchange_max(top, ALL, n_dev)
    weights = jnp.where(mask, jnp.exp(scores - top.reshape(groups, KVH, many)[..., None]), 0.0)
    total = jnp.sum(weights, -1).reshape(groups, KVH, steps, beams, repeat)
    weighted = jnp.einsum(
        "gkmt,gtkd->gkmd", weights.astype(bf16), all_values, preferred_element_type=f32
    ).reshape(groups, KVH, steps, beams, repeat, HD)
    rows = steps * groups * beams
    piece = QD // n_dev
    per_head = HD // piece
    weighted = jnp.transpose(
        weighted.reshape(groups, KVH, steps, beams, repeat, per_head, piece), (1, 4, 5, 2, 0, 3, 6)
    ).reshape(n_dev, -1)
    total = jnp.repeat(jnp.transpose(total, (1, 4, 2, 0, 3)).reshape(QH, rows), per_head, 0)
    lanes = -(-rows // 128) * 128
    packed = jnp.concatenate([weighted, jnp.pad(total, ((0, 0), (0, lanes - rows)))], 1)
    pair = lax.axis_size("pair")
    packed = packed.reshape(n_seq // pair, pair, n_head, -1, 128)
    packed = exchange_sum(jnp.swapaxes(packed, 0, 1), "pair").reshape(n_dev // pair, -1, 128)
    packed = exchange_sum(packed, ("seq", "head")).reshape(-1)
    share = packed[: rows * piece].reshape(rows, piece)
    own_total = packed[rows * piece : rows * piece + rows]
    attn = (share / own_total[:, None]).astype(bf16)
    attn = exchange_gather(attn, "head", n_head)
    attn = jnp.transpose(attn, (1, 0, 2)).reshape(rows, -1)
    partial_out = jnp.dot(attn, w_out, preferred_element_type=f32)
    per_dev = rows // n_seq
    out_proj = seq_sum(partial_out.reshape(n_seq, per_dev, -1))
    out_sq = lax.psum(jnp.sum(out_proj * out_proj, -1), "head")
    x_all = step_tokens.reshape(rows, -1)
    x_f = lax.dynamic_slice_in_dim(x_all, seq_at * per_dev, per_dev, 0).astype(f32)
    state = (x_f + out_proj * lax.rsqrt(out_sq / D + EPS)[:, None] * post_gain).astype(bf16)
    state_all = seq_gather(state).reshape(rows, -1)
    state_f = state_all.astype(f32)
    scaled_two = (state_f * ffn_gain).astype(bf16)
    gate_part = jnp.dot(scaled_two, w_gate, preferred_element_type=f32)
    up_part = jnp.dot(scaled_two, w_up, preferred_element_type=f32)
    hidden = gate_part.shape[1]
    head_rows = rows // n_head
    packed = jnp.concatenate(
        [gate_part, up_part, jnp.pad(jnp.sum(state_f * state_f, -1)[:, None], ((0, 0), (0, 127)))],
        1,
    )
    packed = exchange_sum(packed.reshape(n_head, head_rows, -1), "head")
    norm_s = lax.rsqrt(packed[:, 2 * hidden] / D + EPS)[:, None]
    inner = (
        jax.nn.gelu(packed[:, :hidden] * norm_s, approximate=True)
        * (packed[:, hidden : 2 * hidden] * norm_s)
    ).astype(bf16)
    inner = exchange_gather(inner, "head", n_head).reshape(rows, hidden)
    ffn_out = seq_sum(jnp.dot(inner, w_down, preferred_element_type=f32).reshape(n_seq, per_dev, -1))
    ffn_sq = lax.psum(jnp.sum(ffn_out * ffn_out, -1), "head")
    result = (
        state.astype(f32) + ffn_out * lax.rsqrt(ffn_sq / D + EPS)[:, None] * final_gain
    ).astype(bf16)
    result = seq_gather(result)
    return result.reshape(steps, groups, beams, -1)


def solution(mesh):
    devices = mesh.devices
    fine = jax.sharding.Mesh(
        devices.reshape(devices.shape[0] // 2, 2, devices.shape[1]), ("seq", "pair", "head")
    )
    return jax.shard_map(
        shards,
        mesh=fine,
        in_specs=(
            P(None, None, None, "head"),
            P(),
            P(None, "head", SEQ, None),
            P(),
            P(None, ALL, None),
            P(),
            P(None, SEQ, "head"),
            P(),
            P("head"),
            P("head", SEQ),
            P("head", SEQ),
            P(),
            P(),
            P(SEQ, "head"),
            P("head"),
            P("head"),
            P("head", SEQ),
            P("head", SEQ),
            P(SEQ, "head"),
            P("head"),
        ),
        out_specs=P(None, None, None, "head"),
        check_vma=False,
    )
```

```python
import jax
import jax.numpy as jnp
from jax import lax
from jax.sharding import PartitionSpec as P

D = 2560
QH = 8
KVH = 4
HD = 256
QD = 2048


SEQ = ("seq", "pair")
ALL = ("seq", "pair", "head")

EPS = 1e-06
NEG = -1e30
QSCALE = 0.0625


def norm_heads(values, gain, scale):
    shaped = values.reshape(values.shape[:-1] + (-1, gain.shape[0]))
    shaped = shaped * lax.rsqrt(jnp.mean(shaped * shaped, -1, keepdims=True) + EPS) * gain * scale
    return shaped.reshape(values.shape)


def finish_keys(pairs, k_gain):
    half = pairs.shape[-1] // 2
    keys = norm_heads(pairs[..., :half], k_gain, 1.0)
    return jnp.concatenate([keys, pairs[..., half:]], -1).astype(jnp.bfloat16)


def split_pairs(pairs):
    half = pairs.shape[-1] // 2
    keys = pairs[..., :half].reshape(pairs.shape[:-1] + (KVH, HD))
    values = pairs[..., half:].reshape(pairs.shape[:-1] + (KVH, HD))
    return (keys, values)


def lane_shape(shape):
    size = 1
    for n in shape:
        size = size * n
    return shape if size % 128 else (size // 128, 128)


def exchange_sum(parts, axes, align=False):
    shape = lane_shape(parts.shape[1:]) if align else parts.shape[1:]
    moved = lax.all_to_all(parts.reshape((parts.shape[0],) + shape), axes, 0, 0, tiled=True)
    return jnp.sum(moved, 0).reshape(parts.shape[1:])


def exchange_max(value, axes, count):
    flat = value.reshape(-1, 128)
    spread = jnp.broadcast_to(flat[None], (count,) + flat.shape)
    return jnp.max(lax.all_to_all(spread, axes, 0, 0, tiled=True), 0).reshape(value.shape)


def exchange_gather(piece, axes, count, align=False):
    flat = piece.reshape(lane_shape(piece.shape)) if align else piece
    spread = jnp.broadcast_to(flat[None], (count,) + flat.shape)
    return lax.all_to_all(spread, axes, 0, 0, tiled=True).reshape((count,) + piece.shape)


def seq_sum(parts):
    pair = lax.axis_size("pair")
    parts = parts.reshape((parts.shape[0] // pair, pair) + parts.shape[1:])
    parts = exchange_sum(jnp.swapaxes(parts, 0, 1), "pair")
    return exchange_sum(parts, "seq", True)


def seq_gather(piece):
    pair = lax.axis_size("pair")
    outer = lax.axis_size("seq")
    got = exchange_gather(exchange_gather(piece, "seq", outer, True), "pair", pair)
    return jnp.swapaxes(got, 0, 1).reshape((outer * pair,) + piece.shape)


def project_tokens(tokens, in_gain, w_query, w_keyval, q_gain, k_gain):
    flat = tokens.reshape(-1, tokens.shape[-1]).astype(jnp.float32)
    scaled = (flat * in_gain).astype(jnp.bfloat16)
    q_part = jnp.dot(scaled, w_query, preferred_element_type=jnp.float32)
    kv_part = jnp.dot(scaled, w_keyval, preferred_element_type=jnp.float32)
    squares = jnp.sum(flat * flat, -1)
    n_head = lax.axis_size("head")
    n_seq = lax.axis_size("seq") * lax.axis_size("pair")
    rows = flat.shape[0]
    half = rows // n_head
    block = q_part.shape[1]
    packed = jnp.concatenate([q_part, kv_part, jnp.pad(squares[:, None], ((0, 0), (0, 127)))], 1)
    packed = exchange_sum(packed.reshape(n_head, half, -1), "head")
    factor = lax.rsqrt(packed[:, 2 * block] / D + EPS)[:, None]
    q_raw = (packed[:, :block] * factor).astype(jnp.bfloat16)
    kv_raw = (packed[:, block : 2 * block] * factor).astype(jnp.bfloat16)
    both = exchange_gather(
        jnp.concatenate([q_raw, kv_raw], 1), ALL, n_seq * n_head
    ).reshape(n_seq, n_head, half, 2 * block)
    both = jnp.transpose(both, (1, 2, 0, 3)).reshape(rows, n_seq, 2 * block)
    q_raw = both[:, :, :block].reshape(rows, -1)
    kv_raw = both[:, :, block:].reshape(rows, -1)
    queries = norm_heads(q_raw.astype(jnp.float32), q_gain, QSCALE).astype(jnp.bfloat16)
    fresh = finish_keys(kv_raw.astype(jnp.float32), k_gain)
    return (queries, fresh)


def shards(
    step_tokens,
    parents,
    tail_cache,
    tail_len,
    cache,
    cache_len,
    prompt_states,
    prompt_len,
    in_gain,
    w_query,
    w_keyval,
    q_gain,
    k_gain,
    w_out,
    post_gain,
    ffn_gain,
    w_gate,
    w_up,
    w_down,
    final_gain,
):
    f32 = jnp.float32
    bf16 = jnp.bfloat16
    n_head = lax.axis_size("head")
    n_seq = lax.axis_size("seq") * lax.axis_size("pair")
    seq_at = lax.axis_index("seq") * lax.axis_size("pair") + lax.axis_index("pair")
    head_at = lax.axis_index("head")
    flat_at = seq_at * n_head + head_at
    steps, groups, beams, width = step_tokens.shape
    pre = prompt_states.shape[0]
    repeat = QH // KVH
    rows = jnp.transpose(prompt_states, (1, 0, 2)).astype(f32)
    prompt_scaled = (rows * in_gain).astype(bf16).reshape(-1, width)
    prompt_squares = jnp.sum(rows * rows, -1).reshape(-1)
    prompt_terms = jnp.dot(
        prompt_scaled,
        lax.all_gather(w_keyval, SEQ, axis=1, tiled=True),
        preferred_element_type=f32,
    )
    prompt_sum, prompt_sq = (
        lax.psum_scatter(prompt_terms, "head", scatter_dimension=0, tiled=True),
        lax.psum_scatter(prompt_squares, "head", scatter_dimension=0, tiled=True),
    )
    prompt_pairs = finish_keys(prompt_sum * lax.rsqrt(prompt_sq / D + EPS)[:, None], k_gain)
    prompt_seg = prompt_pairs.shape[0] // pre
    prompt_pairs = jnp.transpose(prompt_pairs.reshape(prompt_seg, pre, -1), (1, 0, 2))
    prompt_ok = (flat_at * prompt_seg + jnp.arange(prompt_seg))[None, :] < prompt_len[:, None]
    cache_seg = cache.shape[1]
    cache_ok = (flat_at * cache_seg + jnp.arange(cache_seg))[None, :] < cache_len[:, None]
    span = max(prompt_seg, cache_seg)
    shared = jnp.concatenate(
        [
            jnp.pad(prompt_pairs, ((0, 0), (0, span - prompt_seg), (0, 0))),
            jnp.pad(cache, ((0, 0), (0, span - cache_seg), (0, 0))),
        ],
        0,
    )
    shared_ok = jnp.concatenate(
        [
            jnp.pad(prompt_ok, ((0, 0), (0, span - prompt_seg))),
            jnp.pad(cache_ok, ((0, 0), (0, span - cache_seg))),
        ],
        0,
    )
    shared_keys, shared_values = split_pairs(shared)
    tail_seg = tail_cache.shape[2]
    local_beams = tail_cache.shape[1]
    offset = (seq_at * tail_seg + jnp.arange(tail_seg))[None, :] - tail_len[:, None]
    all_beams = jnp.arange(beams)
    every_query, every_fresh = project_tokens(
        step_tokens, in_gain, w_query, w_keyval, q_gain, k_gain
    )
    every_query = every_query.reshape(steps, groups, beams, -1)
    every_fresh = every_fresh.reshape(steps, groups, beams, -1)
    everyone = lax.all_gather(tail_cache, "head", axis=1, tiled=True)
    n_dev = n_seq * n_head
    first_beam = head_at * local_beams
    many = steps * beams * repeat
    grouped = jnp.transpose(
        every_query.reshape(steps, groups, beams, KVH, repeat, HD), (1, 3, 0, 2, 4, 5)
    ).reshape(groups, KVH, many, HD)
    source = jnp.broadcast_to(all_beams[None, :], (groups, beams))
    ancestors = []
    tail_states = []
    for step in range(steps):
        link = parents[step]
        source = jnp.take_along_axis(source, link, axis=1)
        ancestors = [jnp.take_along_axis(a, link, axis=1) for a in ancestors]
        ancestors.append(jnp.broadcast_to(all_beams[None, :], (groups, beams)))
        picks = lax.dynamic_slice_in_dim(source, first_beam, local_beams, 1)
        tail_state = jnp.take_along_axis(everyone, picks[:, :, None, None], axis=1)
        for back, anc in enumerate(ancestors):
            mine = lax.dynamic_slice_in_dim(anc, first_beam, local_beams, 1)
            written = jnp.take_along_axis(every_fresh[back], mine[:, :, None], axis=1)
            tail_state = jnp.where(
                (offset == back)[:, None, :, None], written[:, :, None, :], tail_state
            )
        tail_states.append(tail_state)
    tails = jnp.stack(tail_states, 1).reshape(groups, steps * local_beams * tail_seg, -1)
    all_keys, all_values = split_pairs(jnp.concatenate([shared, tails], 1))
    step_id = jnp.arange(steps)
    same_step = step_id[:, None, None, None, None, None] == step_id[None, None, None, :, None, None]
    same_beam = (
        all_beams[None, :, None, None, None, None]
        == (first_beam + jnp.arange(local_beams))[None, None, None, None, :, None]
    )
    live = offset[:, None, None, None, None, None, :] <= step_id[None, None, None, None, :, None, None]
    tail_mask = jnp.broadcast_to(
        (same_step & same_beam)[None] & live,
        (groups, steps, beams, repeat, steps, local_beams, tail_seg),
    ).reshape(groups, many, -1)
    mask = jnp.concatenate(
        [jnp.broadcast_to(shared_ok[:, None, :], (groups, many, span)), tail_mask], -1
    )[:, None]
    scores = jnp.einsum("gkmd,gtkd->gkmt", grouped, all_keys, preferred_element_type=f32)
    scores = jnp.where(mask, scores, NEG)
    top = jnp.max(scores, -1).reshape(groups, KVH, steps, beams, repeat)
    top = exchange_max(top, ALL, n_dev)
    weights = jnp.where(mask, jnp.exp(scores - top.reshape(groups, KVH, many)[..., None]), 0.0)
    total = jnp.sum(weights, -1).reshape(groups, KVH, steps, beams, repeat)
    weighted = jnp.einsum(
        "gkmt,gtkd->gkmd", weights.astype(bf16), all_values, preferred_element_type=f32
    ).reshape(groups, KVH, steps, beams, repeat, HD)
    rows = steps * groups * beams
    piece = QD // n_dev
    per_head = HD // piece
    weighted = jnp.transpose(
        weighted.reshape(groups, KVH, steps, beams, repeat, per_head, piece), (1, 4, 5, 2, 0, 3, 6)
    ).reshape(n_dev, -1)
    total = jnp.repeat(jnp.transpose(total, (1, 4, 2, 0, 3)).reshape(QH, rows), per_head, 0)
    lanes = -(-rows // 128) * 128
    packed = jnp.concatenate([weighted, jnp.pad(total, ((0, 0), (0, lanes - rows)))], 1)
    pair = lax.axis_size("pair")
    packed = packed.reshape(n_seq // pair, pair, n_head, -1, 128)
    packed = exchange_sum(jnp.swapaxes(packed, 0, 1), "pair").reshape(n_dev // pair, -1, 128)
    packed = exchange_sum(packed, ("seq", "head")).reshape(-1)
    share = packed[: rows * piece].reshape(rows, piece)
    own_total = packed[rows * piece : rows * piece + rows]
    attn = (share / own_total[:, None]).astype(bf16)
    attn = exchange_gather(attn, "head", n_head)
    attn = jnp.transpose(attn, (1, 0, 2)).reshape(rows, -1)
    partial_out = jnp.dot(attn, w_out, preferred_element_type=f32)
    per_dev = rows // n_seq
    out_proj = seq_sum(partial_out.reshape(n_seq, per_dev, -1))
    out_sq = jnp.sum(exchange_gather(jnp.sum(out_proj * out_proj, -1), "head", n_head), 0)
    x_all = step_tokens.reshape(rows, -1)
    x_f = lax.dynamic_slice_in_dim(x_all, seq_at * per_dev, per_dev, 0).astype(f32)
    state = (x_f + out_proj * lax.rsqrt(out_sq / D + EPS)[:, None] * post_gain).astype(bf16)
    state_all = seq_gather(state).reshape(rows, -1)
    state_f = state_all.astype(f32)
    scaled_two = (state_f * ffn_gain).astype(bf16)
    gate_part = jnp.dot(scaled_two, w_gate, preferred_element_type=f32)
    up_part = jnp.dot(scaled_two, w_up, preferred_element_type=f32)
    hidden = gate_part.shape[1]
    head_rows = rows // n_head
    packed = jnp.concatenate(
        [gate_part, up_part, jnp.pad(jnp.sum(state_f * state_f, -1)[:, None], ((0, 0), (0, 127)))],
        1,
    )
    packed = exchange_sum(packed.reshape(n_head, head_rows, -1), "head")
    norm_s = lax.rsqrt(packed[:, 2 * hidden] / D + EPS)[:, None]
    inner = (
        jax.nn.gelu(packed[:, :hidden] * norm_s, approximate=True)
        * (packed[:, hidden : 2 * hidden] * norm_s)
    ).astype(bf16)
    inner = exchange_gather(inner, "head", n_head).reshape(rows, hidden)
    ffn_out = seq_sum(jnp.dot(inner, w_down, preferred_element_type=f32).reshape(n_seq, per_dev, -1))
    ffn_sq = jnp.sum(exchange_gather(jnp.sum(ffn_out * ffn_out, -1), "head", n_head), 0)
    result = (
        state.astype(f32) + ffn_out * lax.rsqrt(ffn_sq / D + EPS)[:, None] * final_gain
    ).astype(bf16)
    result = seq_gather(result)
    return result.reshape(steps, groups, beams, -1)


def solution(mesh):
    devices = mesh.devices
    fine = jax.sharding.Mesh(
        devices.reshape(devices.shape[0] // 2, 2, devices.shape[1]), ("seq", "pair", "head")
    )
    return jax.shard_map(
        shards,
        mesh=fine,
        in_specs=(
            P(None, None, None, "head"),
            P(),
            P(None, "head", SEQ, None),
            P(),
            P(None, ALL, None),
            P(),
            P(None, SEQ, "head"),
            P(),
            P("head"),
            P("head", SEQ),
            P("head", SEQ),
            P(),
            P(),
            P(SEQ, "head"),
            P("head"),
            P("head"),
            P("head", SEQ),
            P("head", SEQ),
            P(SEQ, "head"),
            P("head"),
        ),
        out_specs=P(None, None, None, "head"),
        check_vma=False,
    )
```

```python
import jax
import jax.numpy as jnp
from jax import lax
from jax.sharding import PartitionSpec as P

D = 2560
QH = 8
KVH = 4
HD = 256
QD = 2048


SEQ = ("seq", "pair")
ALL = ("seq", "pair", "head")

EPS = 1e-06
NEG = -1e30
QSCALE = 0.0625


def norm_heads(values, gain, scale):
    shaped = values.reshape(values.shape[:-1] + (-1, gain.shape[0]))
    shaped = shaped * lax.rsqrt(jnp.mean(shaped * shaped, -1, keepdims=True) + EPS) * gain * scale
    return shaped.reshape(values.shape)


def finish_keys(pairs, k_gain):
    half = pairs.shape[-1] // 2
    keys = norm_heads(pairs[..., :half], k_gain, 1.0)
    return jnp.concatenate([keys, pairs[..., half:]], -1).astype(jnp.bfloat16)


def split_pairs(pairs):
    half = pairs.shape[-1] // 2
    keys = pairs[..., :half].reshape(pairs.shape[:-1] + (KVH, HD))
    values = pairs[..., half:].reshape(pairs.shape[:-1] + (KVH, HD))
    return (keys, values)


def lane_shape(shape):
    size = 1
    for n in shape:
        size = size * n
    return shape if size % 128 else (size // 128, 128)


def exchange_sum(parts, axes, align=False):
    shape = lane_shape(parts.shape[1:]) if align else parts.shape[1:]
    moved = lax.all_to_all(parts.reshape((parts.shape[0],) + shape), axes, 0, 0, tiled=True)
    return jnp.sum(moved, 0).reshape(parts.shape[1:])


def exchange_max(value, axes, count):
    flat = value.reshape(-1, 128)
    spread = jnp.broadcast_to(flat[None], (count,) + flat.shape)
    return jnp.max(lax.all_to_all(spread, axes, 0, 0, tiled=True), 0).reshape(value.shape)


def exchange_gather(piece, axes, count, align=False):
    flat = piece.reshape(lane_shape(piece.shape)) if align else piece
    spread = jnp.broadcast_to(flat[None], (count,) + flat.shape)
    return lax.all_to_all(spread, axes, 0, 0, tiled=True).reshape((count,) + piece.shape)


def seq_sum(parts):
    pair = lax.axis_size("pair")
    parts = parts.reshape((parts.shape[0] // pair, pair) + parts.shape[1:])
    parts = exchange_sum(jnp.swapaxes(parts, 0, 1), "pair")
    return exchange_sum(parts, "seq", True)


def seq_gather(piece):
    pair = lax.axis_size("pair")
    outer = lax.axis_size("seq")
    got = exchange_gather(exchange_gather(piece, "seq", outer, True), "pair", pair)
    return jnp.swapaxes(got, 0, 1).reshape((outer * pair,) + piece.shape)


def project_tokens(tokens, in_gain, w_query, w_keyval, q_gain, k_gain):
    flat = tokens.reshape(-1, tokens.shape[-1]).astype(jnp.float32)
    scaled = (flat * in_gain).astype(jnp.bfloat16)
    q_part = jnp.dot(scaled, w_query, preferred_element_type=jnp.float32)
    kv_part = jnp.dot(scaled, w_keyval, preferred_element_type=jnp.float32)
    squares = jnp.sum(flat * flat, -1)
    n_head = lax.axis_size("head")
    n_seq = lax.axis_size("seq") * lax.axis_size("pair")
    rows = flat.shape[0]
    half = rows // n_head
    block = q_part.shape[1]
    packed = jnp.concatenate([q_part, kv_part, jnp.pad(squares[:, None], ((0, 0), (0, 127)))], 1)
    packed = exchange_sum(packed.reshape(n_head, half, -1), "head")
    factor = lax.rsqrt(packed[:, 2 * block] / D + EPS)[:, None]
    q_raw = (packed[:, :block] * factor).astype(jnp.bfloat16)
    kv_raw = (packed[:, block : 2 * block] * factor).astype(jnp.bfloat16)
    both = exchange_gather(
        jnp.concatenate([q_raw, kv_raw], 1), ALL, n_seq * n_head
    ).reshape(n_seq, n_head, half, 2 * block)
    both = jnp.transpose(both, (1, 2, 0, 3)).reshape(rows, n_seq, 2 * block)
    q_raw = both[:, :, :block].reshape(rows, -1)
    kv_raw = both[:, :, block:].reshape(rows, -1)
    queries = norm_heads(q_raw.astype(jnp.float32), q_gain, QSCALE).astype(jnp.bfloat16)
    fresh = finish_keys(kv_raw.astype(jnp.float32), k_gain)
    return (queries, fresh)


def shards(
    step_tokens,
    parents,
    tail_cache,
    tail_len,
    cache,
    cache_len,
    prompt_states,
    prompt_len,
    in_gain,
    w_query,
    w_keyval,
    q_gain,
    k_gain,
    w_out,
    post_gain,
    ffn_gain,
    w_gate,
    w_up,
    w_down,
    final_gain,
):
    f32 = jnp.float32
    bf16 = jnp.bfloat16
    n_head = lax.axis_size("head")
    n_seq = lax.axis_size("seq") * lax.axis_size("pair")
    seq_at = lax.axis_index("seq") * lax.axis_size("pair") + lax.axis_index("pair")
    head_at = lax.axis_index("head")
    flat_at = seq_at * n_head + head_at
    steps, groups, beams, width = step_tokens.shape
    pre = prompt_states.shape[0]
    repeat = QH // KVH
    rows = jnp.transpose(prompt_states, (1, 0, 2)).astype(f32)
    prompt_scaled = (rows * in_gain).astype(bf16).reshape(-1, width)
    prompt_squares = jnp.sum(rows * rows, -1).reshape(-1)
    prompt_terms = jnp.dot(
        prompt_scaled,
        lax.all_gather(w_keyval, SEQ, axis=1, tiled=True),
        preferred_element_type=f32,
    )
    prompt_sum, prompt_sq = (
        lax.psum_scatter(prompt_terms, "head", scatter_dimension=0, tiled=True),
        lax.psum_scatter(prompt_squares, "head", scatter_dimension=0, tiled=True),
    )
    prompt_pairs = finish_keys(prompt_sum * lax.rsqrt(prompt_sq / D + EPS)[:, None], k_gain)
    prompt_seg = prompt_pairs.shape[0] // pre
    prompt_pairs = jnp.transpose(prompt_pairs.reshape(prompt_seg, pre, -1), (1, 0, 2))
    prompt_ok = (flat_at * prompt_seg + jnp.arange(prompt_seg))[None, :] < prompt_len[:, None]
    cache_seg = cache.shape[1]
    cache_ok = (flat_at * cache_seg + jnp.arange(cache_seg))[None, :] < cache_len[:, None]
    span = max(prompt_seg, cache_seg)
    shared = jnp.concatenate(
        [
            jnp.pad(prompt_pairs, ((0, 0), (0, span - prompt_seg), (0, 0))),
            jnp.pad(cache, ((0, 0), (0, span - cache_seg), (0, 0))),
        ],
        0,
    )
    shared_ok = jnp.concatenate(
        [
            jnp.pad(prompt_ok, ((0, 0), (0, span - prompt_seg))),
            jnp.pad(cache_ok, ((0, 0), (0, span - cache_seg))),
        ],
        0,
    )
    shared_keys, shared_values = split_pairs(shared)
    tail_seg = tail_cache.shape[2]
    local_beams = tail_cache.shape[1]
    offset = (seq_at * tail_seg + jnp.arange(tail_seg))[None, :] - tail_len[:, None]
    all_beams = jnp.arange(beams)
    every_query, every_fresh = project_tokens(
        step_tokens, in_gain, w_query, w_keyval, q_gain, k_gain
    )
    every_query = every_query.reshape(steps, groups, beams, -1)
    every_fresh = every_fresh.reshape(steps, groups, beams, -1)
    everyone = lax.all_gather(tail_cache, "head", axis=1, tiled=True)
    n_dev = n_seq * n_head
    first_beam = head_at * local_beams
    many = steps * beams * repeat
    grouped = jnp.transpose(
        every_query.reshape(steps, groups, beams, KVH, repeat, HD), (1, 3, 0, 2, 4, 5)
    ).reshape(groups, KVH, many, HD)
    source = jnp.broadcast_to(all_beams[None, :], (groups, beams))
    ancestors = []
    tail_states = []
    for step in range(steps):
        link = parents[step]
        source = jnp.take_along_axis(source, link, axis=1)
        ancestors = [jnp.take_along_axis(a, link, axis=1) for a in ancestors]
        ancestors.append(jnp.broadcast_to(all_beams[None, :], (groups, beams)))
        picks = lax.dynamic_slice_in_dim(source, first_beam, local_beams, 1)
        tail_state = jnp.take_along_axis(everyone, picks[:, :, None, None], axis=1)
        for back, anc in enumerate(ancestors):
            mine = lax.dynamic_slice_in_dim(anc, first_beam, local_beams, 1)
            written = jnp.take_along_axis(every_fresh[back], mine[:, :, None], axis=1)
            tail_state = jnp.where(
                (offset == back)[:, None, :, None], written[:, :, None, :], tail_state
            )
        tail_states.append(tail_state)
    tails = jnp.stack(tail_states, 1).reshape(groups, steps * local_beams * tail_seg, -1)
    all_keys, all_values = split_pairs(jnp.concatenate([shared, tails], 1))
    step_id = jnp.arange(steps)
    same_step = step_id[:, None, None, None, None, None] == step_id[None, None, None, :, None, None]
    same_beam = (
        all_beams[None, :, None, None, None, None]
        == (first_beam + jnp.arange(local_beams))[None, None, None, None, :, None]
    )
    live = offset[:, None, None, None, None, None, :] <= step_id[None, None, None, None, :, None, None]
    tail_mask = jnp.broadcast_to(
        (same_step & same_beam)[None] & live,
        (groups, steps, beams, repeat, steps, local_beams, tail_seg),
    ).reshape(groups, many, -1)
    mask = jnp.concatenate(
        [jnp.broadcast_to(shared_ok[:, None, :], (groups, many, span)), tail_mask], -1
    )[:, None]
    scores = jnp.einsum("gkmd,gtkd->gkmt", grouped, all_keys, preferred_element_type=f32)
    scores = jnp.where(mask, scores, NEG)
    top = jnp.max(scores, -1).reshape(groups, KVH, steps, beams, repeat)
    top = exchange_max(exchange_max(top, "pair", lax.axis_size("pair")), ("seq", "head"), n_dev // 2)
    weights = jnp.where(mask, jnp.exp(scores - top.reshape(groups, KVH, many)[..., None]), 0.0)
    total = jnp.sum(weights, -1).reshape(groups, KVH, steps, beams, repeat)
    weighted = jnp.einsum(
        "gkmt,gtkd->gkmd", weights.astype(bf16), all_values, preferred_element_type=f32
    ).reshape(groups, KVH, steps, beams, repeat, HD)
    rows = steps * groups * beams
    piece = QD // n_dev
    per_head = HD // piece
    weighted = jnp.transpose(
        weighted.reshape(groups, KVH, steps, beams, repeat, per_head, piece), (1, 4, 5, 2, 0, 3, 6)
    ).reshape(n_dev, -1)
    total = jnp.repeat(jnp.transpose(total, (1, 4, 2, 0, 3)).reshape(QH, rows), per_head, 0)
    lanes = -(-rows // 128) * 128
    packed = jnp.concatenate([weighted, jnp.pad(total, ((0, 0), (0, lanes - rows)))], 1)
    pair = lax.axis_size("pair")
    packed = packed.reshape(n_seq // pair, pair, n_head, -1, 128)
    packed = exchange_sum(jnp.swapaxes(packed, 0, 1), "pair").reshape(n_dev // pair, -1, 128)
    packed = exchange_sum(packed, ("seq", "head")).reshape(-1)
    share = packed[: rows * piece].reshape(rows, piece)
    own_total = packed[rows * piece : rows * piece + rows]
    attn = (share / own_total[:, None]).astype(bf16)
    attn = exchange_gather(attn, "head", n_head)
    attn = jnp.transpose(attn, (1, 0, 2)).reshape(rows, -1)
    partial_out = jnp.dot(attn, w_out, preferred_element_type=f32)
    per_dev = rows // n_seq
    out_proj = seq_sum(partial_out.reshape(n_seq, per_dev, -1))
    out_sq = lax.psum(jnp.sum(out_proj * out_proj, -1), "head")
    x_all = step_tokens.reshape(rows, -1)
    x_f = lax.dynamic_slice_in_dim(x_all, seq_at * per_dev, per_dev, 0).astype(f32)
    state = (x_f + out_proj * lax.rsqrt(out_sq / D + EPS)[:, None] * post_gain).astype(bf16)
    state_all = seq_gather(state).reshape(rows, -1)
    state_f = state_all.astype(f32)
    scaled_two = (state_f * ffn_gain).astype(bf16)
    gate_part = jnp.dot(scaled_two, w_gate, preferred_element_type=f32)
    up_part = jnp.dot(scaled_two, w_up, preferred_element_type=f32)
    hidden = gate_part.shape[1]
    head_rows = rows // n_head
    packed = jnp.concatenate(
        [gate_part, up_part, jnp.pad(jnp.sum(state_f * state_f, -1)[:, None], ((0, 0), (0, 127)))],
        1,
    )
    packed = exchange_sum(packed.reshape(n_head, head_rows, -1), "head")
    norm_s = lax.rsqrt(packed[:, 2 * hidden] / D + EPS)[:, None]
    inner = (
        jax.nn.gelu(packed[:, :hidden] * norm_s, approximate=True)
        * (packed[:, hidden : 2 * hidden] * norm_s)
    ).astype(bf16)
    inner = exchange_gather(inner, "head", n_head).reshape(rows, hidden)
    ffn_out = seq_sum(jnp.dot(inner, w_down, preferred_element_type=f32).reshape(n_seq, per_dev, -1))
    ffn_sq = lax.psum(jnp.sum(ffn_out * ffn_out, -1), "head")
    result = (
        state.astype(f32) + ffn_out * lax.rsqrt(ffn_sq / D + EPS)[:, None] * final_gain
    ).astype(bf16)
    result = seq_gather(result)
    return result.reshape(steps, groups, beams, -1)


def solution(mesh):
    devices = mesh.devices
    fine = jax.sharding.Mesh(
        devices.reshape(devices.shape[0] // 2, 2, devices.shape[1]), ("seq", "pair", "head")
    )
    return jax.shard_map(
        shards,
        mesh=fine,
        in_specs=(
            P(None, None, None, "head"),
            P(),
            P(None, "head", SEQ, None),
            P(),
            P(None, ALL, None),
            P(),
            P(None, SEQ, "head"),
            P(),
            P("head"),
            P("head", SEQ),
            P("head", SEQ),
            P(),
            P(),
            P(SEQ, "head"),
            P("head"),
            P("head"),
            P("head", SEQ),
            P("head", SEQ),
            P(SEQ, "head"),
            P("head"),
        ),
        out_specs=P(None, None, None, "head"),
        check_vma=False,
    )
```

```python
import jax
import jax.numpy as jnp
from jax import lax
from jax.sharding import PartitionSpec as P

D = 2560
QH = 8
KVH = 4
HD = 256
QD = 2048


SEQ = ("seq", "pair")
ALL = ("seq", "pair", "head")

EPS = 1e-06
NEG = -1e30
QSCALE = 0.0625


def norm_heads(values, gain, scale):
    shaped = values.reshape(values.shape[:-1] + (-1, gain.shape[0]))
    shaped = shaped * lax.rsqrt(jnp.mean(shaped * shaped, -1, keepdims=True) + EPS) * gain * scale
    return shaped.reshape(values.shape)


def finish_keys(pairs, k_gain):
    half = pairs.shape[-1] // 2
    keys = norm_heads(pairs[..., :half], k_gain, 1.0)
    return jnp.concatenate([keys, pairs[..., half:]], -1).astype(jnp.bfloat16)


def split_pairs(pairs):
    half = pairs.shape[-1] // 2
    keys = pairs[..., :half].reshape(pairs.shape[:-1] + (KVH, HD))
    values = pairs[..., half:].reshape(pairs.shape[:-1] + (KVH, HD))
    return (keys, values)


def lane_shape(shape):
    size = 1
    for n in shape:
        size = size * n
    return shape if size % 128 else (size // 128, 128)


def exchange_sum(parts, axes, align=False):
    shape = lane_shape(parts.shape[1:]) if align else parts.shape[1:]
    moved = lax.all_to_all(parts.reshape((parts.shape[0],) + shape), axes, 0, 0, tiled=True)
    return jnp.sum(moved, 0).reshape(parts.shape[1:])


def exchange_max(value, axes, count):
    flat = value.reshape(-1, 128)
    spread = jnp.broadcast_to(flat[None], (count,) + flat.shape)
    return jnp.max(lax.all_to_all(spread, axes, 0, 0, tiled=True), 0).reshape(value.shape)


def exchange_gather(piece, axes, count, align=False):
    flat = piece.reshape(lane_shape(piece.shape)) if align else piece
    spread = jnp.broadcast_to(flat[None], (count,) + flat.shape)
    return lax.all_to_all(spread, axes, 0, 0, tiled=True).reshape((count,) + piece.shape)


def seq_sum(parts):
    pair = lax.axis_size("pair")
    parts = parts.reshape((parts.shape[0] // pair, pair) + parts.shape[1:])
    parts = exchange_sum(jnp.swapaxes(parts, 0, 1), "pair")
    return exchange_sum(parts, "seq", True)


def seq_gather(piece):
    pair = lax.axis_size("pair")
    outer = lax.axis_size("seq")
    got = exchange_gather(exchange_gather(piece, "seq", outer, True), "pair", pair, True)
    return jnp.swapaxes(got, 0, 1).reshape((outer * pair,) + piece.shape)


def project_tokens(tokens, in_gain, w_query, w_keyval, q_gain, k_gain):
    flat = tokens.reshape(-1, tokens.shape[-1]).astype(jnp.float32)
    scaled = (flat * in_gain).astype(jnp.bfloat16)
    q_part = jnp.dot(scaled, w_query, preferred_element_type=jnp.float32)
    kv_part = jnp.dot(scaled, w_keyval, preferred_element_type=jnp.float32)
    squares = jnp.sum(flat * flat, -1)
    n_head = lax.axis_size("head")
    n_seq = lax.axis_size("seq") * lax.axis_size("pair")
    rows = flat.shape[0]
    half = rows // n_head
    block = q_part.shape[1]
    packed = jnp.concatenate([q_part, kv_part, jnp.pad(squares[:, None], ((0, 0), (0, 127)))], 1)
    packed = exchange_sum(packed.reshape(n_head, half, -1), "head")
    factor = lax.rsqrt(packed[:, 2 * block] / D + EPS)[:, None]
    q_raw = (packed[:, :block] * factor).astype(jnp.bfloat16)
    kv_raw = (packed[:, block : 2 * block] * factor).astype(jnp.bfloat16)
    both = exchange_gather(
        jnp.concatenate([q_raw, kv_raw], 1), ALL, n_seq * n_head
    ).reshape(n_seq, n_head, half, 2 * block)
    both = jnp.transpose(both, (1, 2, 0, 3)).reshape(rows, n_seq, 2 * block)
    q_raw = both[:, :, :block].reshape(rows, -1)
    kv_raw = both[:, :, block:].reshape(rows, -1)
    queries = norm_heads(q_raw.astype(jnp.float32), q_gain, QSCALE).astype(jnp.bfloat16)
    fresh = finish_keys(kv_raw.astype(jnp.float32), k_gain)
    return (queries, fresh)


def shards(
    step_tokens,
    parents,
    tail_cache,
    tail_len,
    cache,
    cache_len,
    prompt_states,
    prompt_len,
    in_gain,
    w_query,
    w_keyval,
    q_gain,
    k_gain,
    w_out,
    post_gain,
    ffn_gain,
    w_gate,
    w_up,
    w_down,
    final_gain,
):
    f32 = jnp.float32
    bf16 = jnp.bfloat16
    n_head = lax.axis_size("head")
    n_seq = lax.axis_size("seq") * lax.axis_size("pair")
    seq_at = lax.axis_index("seq") * lax.axis_size("pair") + lax.axis_index("pair")
    head_at = lax.axis_index("head")
    flat_at = seq_at * n_head + head_at
    steps, groups, beams, width = step_tokens.shape
    pre = prompt_states.shape[0]
    repeat = QH // KVH
    rows = jnp.transpose(prompt_states, (1, 0, 2)).astype(f32)
    prompt_scaled = (rows * in_gain).astype(bf16).reshape(-1, width)
    prompt_squares = jnp.sum(rows * rows, -1).reshape(-1)
    prompt_terms = jnp.dot(
        prompt_scaled,
        lax.all_gather(w_keyval, SEQ, axis=1, tiled=True),
        preferred_element_type=f32,
    )
    prompt_sum, prompt_sq = (
        lax.psum_scatter(prompt_terms, "head", scatter_dimension=0, tiled=True),
        lax.psum_scatter(prompt_squares, "head", scatter_dimension=0, tiled=True),
    )
    prompt_pairs = finish_keys(prompt_sum * lax.rsqrt(prompt_sq / D + EPS)[:, None], k_gain)
    prompt_seg = prompt_pairs.shape[0] // pre
    prompt_pairs = jnp.transpose(prompt_pairs.reshape(prompt_seg, pre, -1), (1, 0, 2))
    prompt_ok = (flat_at * prompt_seg + jnp.arange(prompt_seg))[None, :] < prompt_len[:, None]
    cache_seg = cache.shape[1]
    cache_ok = (flat_at * cache_seg + jnp.arange(cache_seg))[None, :] < cache_len[:, None]
    span = max(prompt_seg, cache_seg)
    shared = jnp.concatenate(
        [
            jnp.pad(prompt_pairs, ((0, 0), (0, span - prompt_seg), (0, 0))),
            jnp.pad(cache, ((0, 0), (0, span - cache_seg), (0, 0))),
        ],
        0,
    )
    shared_ok = jnp.concatenate(
        [
            jnp.pad(prompt_ok, ((0, 0), (0, span - prompt_seg))),
            jnp.pad(cache_ok, ((0, 0), (0, span - cache_seg))),
        ],
        0,
    )
    shared_keys, shared_values = split_pairs(shared)
    tail_seg = tail_cache.shape[2]
    local_beams = tail_cache.shape[1]
    offset = (seq_at * tail_seg + jnp.arange(tail_seg))[None, :] - tail_len[:, None]
    all_beams = jnp.arange(beams)
    every_query, every_fresh = project_tokens(
        step_tokens, in_gain, w_query, w_keyval, q_gain, k_gain
    )
    every_query = every_query.reshape(steps, groups, beams, -1)
    every_fresh = every_fresh.reshape(steps, groups, beams, -1)
    everyone = lax.all_gather(tail_cache, "head", axis=1, tiled=True)
    n_dev = n_seq * n_head
    first_beam = head_at * local_beams
    many = steps * beams * repeat
    grouped = jnp.transpose(
        every_query.reshape(steps, groups, beams, KVH, repeat, HD), (1, 3, 0, 2, 4, 5)
    ).reshape(groups, KVH, many, HD)
    source = jnp.broadcast_to(all_beams[None, :], (groups, beams))
    ancestors = []
    tail_states = []
    for step in range(steps):
        link = parents[step]
        source = jnp.take_along_axis(source, link, axis=1)
        ancestors = [jnp.take_along_axis(a, link, axis=1) for a in ancestors]
        ancestors.append(jnp.broadcast_to(all_beams[None, :], (groups, beams)))
        picks = lax.dynamic_slice_in_dim(source, first_beam, local_beams, 1)
        tail_state = jnp.take_along_axis(everyone, picks[:, :, None, None], axis=1)
        for back, anc in enumerate(ancestors):
            mine = lax.dynamic_slice_in_dim(anc, first_beam, local_beams, 1)
            written = jnp.take_along_axis(every_fresh[back], mine[:, :, None], axis=1)
            tail_state = jnp.where(
                (offset == back)[:, None, :, None], written[:, :, None, :], tail_state
            )
        tail_states.append(tail_state)
    tails = jnp.stack(tail_states, 1).reshape(groups, steps * local_beams * tail_seg, -1)
    all_keys, all_values = split_pairs(jnp.concatenate([shared, tails], 1))
    step_id = jnp.arange(steps)
    same_step = step_id[:, None, None, None, None, None] == step_id[None, None, None, :, None, None]
    same_beam = (
        all_beams[None, :, None, None, None, None]
        == (first_beam + jnp.arange(local_beams))[None, None, None, None, :, None]
    )
    live = offset[:, None, None, None, None, None, :] <= step_id[None, None, None, None, :, None, None]
    tail_mask = jnp.broadcast_to(
        (same_step & same_beam)[None] & live,
        (groups, steps, beams, repeat, steps, local_beams, tail_seg),
    ).reshape(groups, many, -1)
    mask = jnp.concatenate(
        [jnp.broadcast_to(shared_ok[:, None, :], (groups, many, span)), tail_mask], -1
    )[:, None]
    scores = jnp.einsum("gkmd,gtkd->gkmt", grouped, all_keys, preferred_element_type=f32)
    scores = jnp.where(mask, scores, NEG)
    top = jnp.max(scores, -1).reshape(groups, KVH, steps, beams, repeat)
    top = exchange_max(top, ALL, n_dev)
    weights = jnp.where(mask, jnp.exp(scores - top.reshape(groups, KVH, many)[..., None]), 0.0)
    total = jnp.sum(weights, -1).reshape(groups, KVH, steps, beams, repeat)
    weighted = jnp.einsum(
        "gkmt,gtkd->gkmd", weights.astype(bf16), all_values, preferred_element_type=f32
    ).reshape(groups, KVH, steps, beams, repeat, HD)
    rows = steps * groups * beams
    piece = QD // n_dev
    per_head = HD // piece
    weighted = jnp.transpose(
        weighted.reshape(groups, KVH, steps, beams, repeat, per_head, piece), (1, 4, 5, 2, 0, 3, 6)
    ).reshape(n_dev, -1)
    total = jnp.repeat(jnp.transpose(total, (1, 4, 2, 0, 3)).reshape(QH, rows), per_head, 0)
    lanes = -(-rows // 128) * 128
    packed = jnp.concatenate([weighted, jnp.pad(total, ((0, 0), (0, lanes - rows)))], 1)
    pair = lax.axis_size("pair")
    packed = packed.reshape(n_seq // pair, pair, n_head, -1, 128)
    packed = exchange_sum(jnp.swapaxes(packed, 0, 1), "pair").reshape(n_dev // pair, -1, 128)
    packed = exchange_sum(packed, ("seq", "head")).reshape(-1)
    share = packed[: rows * piece].reshape(rows, piece)
    own_total = packed[rows * piece : rows * piece + rows]
    attn = (share / own_total[:, None]).astype(bf16)
    attn = exchange_gather(attn, "head", n_head)
    attn = jnp.transpose(attn, (1, 0, 2)).reshape(rows, -1)
    partial_out = jnp.dot(attn, w_out, preferred_element_type=f32)
    per_dev = rows // n_seq
    out_proj = seq_sum(partial_out.reshape(n_seq, per_dev, -1))
    out_sq = lax.psum(jnp.sum(out_proj * out_proj, -1), "head")
    x_all = step_tokens.reshape(rows, -1)
    x_f = lax.dynamic_slice_in_dim(x_all, seq_at * per_dev, per_dev, 0).astype(f32)
    state = (x_f + out_proj * lax.rsqrt(out_sq / D + EPS)[:, None] * post_gain).astype(bf16)
    state_all = seq_gather(state).reshape(rows, -1)
    state_f = state_all.astype(f32)
    scaled_two = (state_f * ffn_gain).astype(bf16)
    gate_part = jnp.dot(scaled_two, w_gate, preferred_element_type=f32)
    up_part = jnp.dot(scaled_two, w_up, preferred_element_type=f32)
    hidden = gate_part.shape[1]
    head_rows = rows // n_head
    packed = jnp.concatenate(
        [gate_part, up_part, jnp.pad(jnp.sum(state_f * state_f, -1)[:, None], ((0, 0), (0, 127)))],
        1,
    )
    packed = exchange_sum(packed.reshape(n_head, head_rows, -1), "head")
    norm_s = lax.rsqrt(packed[:, 2 * hidden] / D + EPS)[:, None]
    inner = (
        jax.nn.gelu(packed[:, :hidden] * norm_s, approximate=True)
        * (packed[:, hidden : 2 * hidden] * norm_s)
    ).astype(bf16)
    inner = exchange_gather(inner, "head", n_head).reshape(rows, hidden)
    ffn_out = seq_sum(jnp.dot(inner, w_down, preferred_element_type=f32).reshape(n_seq, per_dev, -1))
    ffn_sq = lax.psum(jnp.sum(ffn_out * ffn_out, -1), "head")
    result = (
        state.astype(f32) + ffn_out * lax.rsqrt(ffn_sq / D + EPS)[:, None] * final_gain
    ).astype(bf16)
    result = seq_gather(result)
    return result.reshape(steps, groups, beams, -1)


def solution(mesh):
    devices = mesh.devices
    fine = jax.sharding.Mesh(
        devices.reshape(devices.shape[0] // 2, 2, devices.shape[1]), ("seq", "pair", "head")
    )
    return jax.shard_map(
        shards,
        mesh=fine,
        in_specs=(
            P(None, None, None, "head"),
            P(),
            P(None, "head", SEQ, None),
            P(),
            P(None, ALL, None),
            P(),
            P(None, SEQ, "head"),
            P(),
            P("head"),
            P("head", SEQ),
            P("head", SEQ),
            P(),
            P(),
            P(SEQ, "head"),
            P("head"),
            P("head"),
            P("head", SEQ),
            P("head", SEQ),
            P(SEQ, "head"),
            P("head"),
        ),
        out_specs=P(None, None, None, "head"),
        check_vma=False,
    )
```
